32 devices in a mesh: grp: 2 (over x), seq: 16 (over z, y, core).
Axes of the slice: x: 2, y: 2, z: 4, core: 2. Of those that a mesh axis runs over, the one named last changes fastest.
Arguments:
- scalars: bfloat16 [256, 4096], P(None, ('grp', 'seq')), parts along dimension 1, may hold values from -6 to 6
- vectors: bfloat16 [3, 256, 4096], P(None, None, ('grp', 'seq')), parts along dimension 2, may hold values from -6 to 6
- w_qkw_s: bfloat16 [2, 768, 256], replicated, may hold values from -0.375 to 0.375
- w_qkw_v: bfloat16 [2, 768, 256], replicated, may hold values from -0.375 to 0.375
- w_out_s: bfloat16 [2, 256, 256], replicated, may hold values from -0.375 to 0.375
- w_out_v: bfloat16 [2, 256, 256], replicated, may hold values from -0.375 to 0.375
- w_up: bfloat16 [2, 1024, 256], replicated, may hold values from -0.375 to 0.375
- w_down: bfloat16 [2, 256, 1024], replicated, may hold values from -0.1875 to 0.1875
- w_mix: bfloat16 [2, 256, 256], replicated, may hold values from -0.375 to 0.375
- w_gate: bfloat16 [2, 256, 256], replicated, may hold values from -0.375 to 0.375
- gains: float32 [2, 4, 256], replicated, may hold values from 0.5 to 1.5
- pe_w1: float32 [2, 64, 16], replicated, may hold values from -24 to 24
- pe_w2: float32 [2, 64, 64], replicated, may hold values from -0.75 to 0.75
- pe_w3: float32 [2, 256, 64], replicated, may hold values from -1.5 to 1.5
- rates: float32 [2, 256], replicated, may hold values from 0.05 to 40
Outputs:
- scalars_out: bfloat16 [256, 4096], P(None, ('grp', 'seq')), parts along dimension 1
- vectors_out: bfloat16 [3, 256, 4096], P(None, None, ('grp', 'seq')), parts along dimension 2
The draws below stay inside these ranges and needn't reach their ends.
There are 2 independent parts, one for each index of `grp`. The reference program is written for one: setup_inputs(seed, part) draws one part's arguments, and reference() takes and returns one part's arrays. A program takes and returns all parts, laid end to end along the dimension named above; an argument that names none is the same for every part. Nothing has to cross between parts.
All inputs are finite; a program needn't handle non-finite values.
Results may differ from the reference program's by a relative error of at most 0.02.
Values may be sent and summed in bfloat16 or wider, within the bound.
No kernel may reach another device: no remote copies, remote signals or barrier semaphores. Data moves between devices by JAX's collectives and lax.ppermute only.
A program may use at most 64 MiB of HBM per device.

```python
import math
import jax
import jax.numpy as jnp
from jax import lax

CH = 256
FF = 1024
PEH = 64
PEF = 16
LAYERS = 2
TOKENS = 2048


def level_of(key, extent, pieces, low, high):
    factor_of, own = 1.0, jax.random.fold_in(key, 6)
    for position, blocks in pieces:
        draws = jnp.exp(jax.random.uniform(jax.random.fold_in(own, position), (blocks,), jnp.float32, low / len(pieces), high / len(pieces)))
        factor_of = factor_of * jnp.repeat(draws, extent[position] // blocks).reshape([-1 if axis == position else 1 for axis in range(len(extent))])
    return factor_of


def noise(key, extent, width, most, pieces=(), kind=jnp.bfloat16):
    result = width * jax.random.normal(key, extent, jnp.float32)
    if pieces:
        result = result * level_of(key, extent, pieces, -0.22, 0.18)
    return jnp.clip(result, -most, most).astype(kind)


def setup_inputs(seed: int = 0, part: int = 0) -> dict:
    splits = jax.random.split(jax.random.key(seed), 16)
    part_splits = jax.random.split(jax.random.fold_in(splits[15], part), 16)
    scalars = noise(part_splits[0], (CH, TOKENS), 1.0, 6.0, ((1, 16),))
    vectors = noise(part_splits[1], (3, CH, TOKENS), 1.0, 6.0, ((2, 16),))
    w_qkw_s = noise(splits[2], (LAYERS, 3 * CH, CH), CH ** -0.5, 0.375)
    w_qkw_v = noise(splits[3], (LAYERS, 3 * CH, CH), CH ** -0.5, 0.375)
    w_out_s = noise(splits[4], (LAYERS, CH, CH), CH ** -0.5, 0.375)
    w_out_v = noise(splits[5], (LAYERS, CH, CH), CH ** -0.5, 0.375)
    w_up = noise(splits[6], (LAYERS, FF, CH), CH ** -0.5, 0.375)
    w_down = noise(splits[7], (LAYERS, CH, FF), FF ** -0.5, 0.1875)
    w_mix = noise(splits[8], (LAYERS, CH, CH), CH ** -0.5, 0.375)
    w_gate = noise(splits[9], (LAYERS, CH, CH), CH ** -0.5, 0.375)
    gains = jnp.clip(1.0 + 0.1 * jax.random.normal(splits[10], (LAYERS, 4, CH), jnp.float32), 0.5, 1.5)
    pe_w1 = noise(splits[11], (LAYERS, PEH, PEF), 6.0, 24.0, (), jnp.float32)
    pe_w2 = noise(splits[12], (LAYERS, PEH, PEH), PEH ** -0.5, 0.75, (), jnp.float32)
    pe_w3 = noise(splits[13], (LAYERS, CH, PEH), (PEH // 4) ** -0.5, 1.5, (), jnp.float32)
    rates = jnp.clip(jnp.exp(jax.random.uniform(splits[14], (LAYERS, CH), jnp.float32, math.log(0.05), math.log(40.0))), 0.05, 40.0)
    return {"scalars": scalars, "vectors": vectors, "w_qkw_s": w_qkw_s, "w_qkw_v": w_qkw_v, "w_out_s": w_out_s, "w_out_v": w_out_v, "w_up": w_up, "w_down": w_down, "w_mix": w_mix, "w_gate": w_gate, "gains": gains, "pe_w1": pe_w1, "pe_w2": pe_w2, "pe_w3": pe_w3, "rates": rates}


def filter_values(positions, length, first, second, third, decay):
    count = first.shape[1] // 2
    freqs = jnp.arange(1, count + 1, dtype=jnp.int32)
    turns = freqs[:, None] * positions[None, :] % length
    angle = turns.astype(jnp.float32) * (2.0 * math.pi / length)
    feats = jnp.concatenate([jnp.cos(angle), jnp.sin(angle)], axis=0)
    hid_one = jnp.sin(jnp.dot(first, feats, precision=lax.Precision.HIGHEST))
    hid_two = jnp.sin(jnp.dot(second, hid_one, precision=lax.Precision.HIGHEST))
    raw = jnp.dot(third, hid_two, precision=lax.Precision.HIGHEST)
    envelope = jnp.exp(-decay[:, None] * positions[None, :].astype(jnp.float32) / length)
    return (raw * envelope / math.sqrt(length)).astype(jnp.bfloat16)

def scalar_norm(field, gain):
    return field * lax.rsqrt(lax.optimization_barrier(jnp.mean(field * field, axis=0, keepdims=True)) + 1e-05) * gain[:, None]

def vector_norm(field, gain):
    return field * lax.rsqrt(lax.optimization_barrier(jnp.mean(field * field, axis=(0, 1), keepdims=True)) + 1e-05) * gain[None, :, None]

def mix_vec(weight, field):
    return jnp.einsum('oc,jct->jot', weight.astype(jnp.float32), field.astype(jnp.float32))

def reference(scalars, vectors, w_qkw_s, w_qkw_v, w_out_s, w_out_v, w_up, w_down, w_mix, w_gate, gains, pe_w1, pe_w2, pe_w3, rates):
    length = scalars.shape[1]
    chans = scalars.shape[0]
    positions = jnp.arange(length, dtype=jnp.int32)
    state_s = scalars.astype(jnp.float32)
    state_v = vectors.astype(jnp.float32)
    for layer in range(w_qkw_s.shape[0]):
        filt = filter_values(positions, length, pe_w1[layer], pe_w2[layer], pe_w3[layer], rates[layer])
        normed_s = scalar_norm(state_s, gains[layer, 0]).astype(jnp.bfloat16)
        normed_v = vector_norm(state_v, gains[layer, 1]).astype(jnp.bfloat16)
        proj_s = jnp.dot(w_qkw_s[layer], normed_s, preferred_element_type=jnp.float32)
        query_s = proj_s[:chans].astype(jnp.bfloat16)
        signal_s = (proj_s[chans:2 * chans] * proj_s[2 * chans:]).astype(jnp.bfloat16)
        proj_v = mix_vec(w_qkw_v[layer], normed_v)
        query_v = proj_v[:, :chans].astype(jnp.bfloat16)
        key_v = proj_v[:, chans:2 * chans].astype(jnp.bfloat16)
        value_v = proj_v[:, 2 * chans:].astype(jnp.bfloat16)
        spec_h = jnp.fft.fft(filt.astype(jnp.float32), axis=-1)
        spec_x = jnp.fft.fft(signal_s.astype(jnp.float32), axis=-1)
        conv_s = jnp.real(jnp.fft.ifft(spec_h * spec_x, axis=-1)).astype(jnp.float32).astype(jnp.bfloat16)
        spec_k = jnp.fft.fft(key_v.astype(jnp.float32), axis=-1)
        spec_w = jnp.fft.fft(value_v.astype(jnp.float32), axis=-1)
        k_one = jnp.roll(spec_k, -1, axis=0)
        k_two = jnp.roll(spec_k, -2, axis=0)
        w_one = jnp.roll(spec_w, -1, axis=0)
        w_two = jnp.roll(spec_w, -2, axis=0)
        cross = k_one * w_two - k_two * w_one
        conv_v = (jnp.real(jnp.fft.ifft(cross, axis=-1)).astype(jnp.float32) / math.sqrt(length)).astype(jnp.bfloat16)
        qs_f = query_s.astype(jnp.float32)
        out_s = (qs_f * conv_s.astype(jnp.float32) + lax.optimization_barrier(jnp.sum(query_v.astype(jnp.float32) * conv_v.astype(jnp.float32), axis=0))).astype(jnp.bfloat16)
        out_v = (qs_f[None] * conv_v.astype(jnp.float32)).astype(jnp.bfloat16)
        state_s = state_s + jnp.dot(w_out_s[layer], out_s, preferred_element_type=jnp.float32)
        state_v = state_v + mix_vec(w_out_v[layer], out_v)
        mlp_s = scalar_norm(state_s, gains[layer, 2]).astype(jnp.bfloat16)
        mlp_v = vector_norm(state_v, gains[layer, 3]).astype(jnp.bfloat16)
        hidden = jax.nn.gelu(jnp.dot(w_up[layer], mlp_s, preferred_element_type=jnp.float32)).astype(jnp.bfloat16)
        gate = jax.nn.sigmoid(jnp.dot(w_gate[layer], mlp_s, preferred_element_type=jnp.float32))
        state_s = state_s + jnp.dot(w_down[layer], hidden, preferred_element_type=jnp.float32)
        state_v = state_v + mix_vec(w_mix[layer], mlp_v) * gate[None]
    return (state_s.astype(jnp.bfloat16), state_v.astype(jnp.bfloat16))
```

```python
import math

import jax
import jax.numpy as jnp
import numpy as np
from jax import lax
from jax.sharding import PartitionSpec as P

HIGH = lax.Precision.HIGHEST


def filter_values(positions, length, first, second, third, decay):
    count = first.shape[1] // 2
    freqs = jnp.arange(1, count + 1, dtype=jnp.int32)
    turns = freqs[:, None] * positions[None, :] % length
    angle = turns.astype(jnp.float32) * (2.0 * math.pi / length)
    feats = jnp.concatenate([jnp.cos(angle), jnp.sin(angle)], axis=0)
    hid_one = jnp.sin(jnp.dot(first, feats, precision=HIGH))
    hid_two = jnp.sin(jnp.dot(second, hid_one, precision=HIGH))
    raw = jnp.dot(third, hid_two, precision=HIGH)
    envelope = jnp.exp(-decay[:, None] * positions[None, :].astype(jnp.float32) / length)
    return (raw * envelope / math.sqrt(length)).astype(jnp.bfloat16)


def scalar_norm(field, gain):
    return field * lax.rsqrt(jnp.mean(field * field, axis=0, keepdims=True) + 1e-05) * gain[:, None]


def vector_norm(field, gain):
    return (
        field
        * lax.rsqrt(jnp.mean(field * field, axis=(0, 1), keepdims=True) + 1e-05)
        * gain[None, :, None]
    )


def make_tables(shards, local):
    length = shards * local
    a = np.arange(shards)
    ang_s = 2.0 * np.pi * np.outer(a, a) / shards
    lead_fwd = np.concatenate([np.cos(ang_s), -np.sin(ang_s)], axis=0)
    lead_inv = np.concatenate([np.cos(ang_s), -np.sin(ang_s)], axis=1)
    b = np.arange(local)
    ang_t = 2.0 * np.pi * np.outer(a, b) / length
    tw_c = np.cos(ang_t)[:, None, None, :]
    tw_s = np.sin(ang_t)[:, None, None, :]
    ang_l = 2.0 * np.pi * np.outer(b, b) / local
    cos_l, sin_l = np.cos(ang_l), np.sin(ang_l)
    lane_fwd = np.block([[cos_l, -sin_l], [sin_l, cos_l]])
    lane_inv = np.block([[cos_l, sin_l], [-sin_l, cos_l]])
    f32 = lambda v: jnp.asarray(v, dtype=jnp.float32)
    return tuple(f32(v) for v in (lead_fwd, lead_inv, tw_c, tw_s, lane_fwd, lane_inv))


def forward_dft(field, tables):
    lead_fwd, _, tw_c, tw_s, lane_fwd, _ = tables
    shards = field.shape[0]
    stage = jnp.einsum("ka,apcb->kpcb", lead_fwd, field, precision=HIGH)
    st_r, st_i = stage[:shards], stage[shards:]
    tw_r = st_r * tw_c + st_i * tw_s
    tw_i = st_i * tw_c - st_r * tw_s
    joined = jnp.concatenate([tw_r, tw_i], axis=-1)
    return jnp.einsum("kpcb,bm->kpcm", joined, lane_fwd, precision=HIGH)


def inverse_dft(spec, tables):
    _, lead_inv, tw_c, tw_s, _, lane_inv = tables
    local = spec.shape[-1] // 2
    back = jnp.einsum("kpcm,mb->kpcb", spec, lane_inv, precision=HIGH)
    bk_r, bk_i = back[..., :local], back[..., local:]
    un_r = bk_r * tw_c - bk_i * tw_s
    un_i = bk_r * tw_s + bk_i * tw_c
    stacked = jnp.concatenate([un_r, un_i], axis=0)
    return jnp.einsum("ak,kpcb->apcb", lead_inv, stacked, precision=HIGH)


def cmul(a_r, a_i, b_r, b_i):
    return a_r * b_r - a_i * b_i, a_r * b_i + a_i * b_r


def convolve(received, filt_spec, tables):
    shards, _, chans, local = received.shape
    length = shards * local
    spec = forward_dft(received.astype(jnp.float32), tables)
    re, im = spec[..., :local], spec[..., local:]
    h_r, h_i = filt_spec[..., :local], filt_spec[..., local:]
    p_r, p_i = cmul(re[:, 0], im[:, 0], h_r, h_i)
    outs_r, outs_i = [p_r], [p_i]
    for j in range(3):
        one, two = (j + 1) % 3, (j + 2) % 3
        a_r, a_i = cmul(re[:, 1 + one], im[:, 1 + one], re[:, 4 + two], im[:, 4 + two])
        b_r, b_i = cmul(re[:, 1 + two], im[:, 1 + two], re[:, 4 + one], im[:, 4 + one])
        outs_r.append(a_r - b_r)
        outs_i.append(a_i - b_i)
    prod = jnp.concatenate([jnp.stack(outs_r, axis=1), jnp.stack(outs_i, axis=1)], axis=-1)
    result = inverse_dft(prod, tables)
    inv_root = 1.0 / math.sqrt(length)
    scale = jnp.array([1.0, inv_root, inv_root, inv_root], dtype=jnp.float32) / length
    return (result * scale[None, :, None, None]).astype(jnp.bfloat16)


def per_device(
    scalars,
    vectors,
    w_qkw_s,
    w_qkw_v,
    w_out_s,
    w_out_v,
    w_up,
    w_down,
    w_mix,
    w_gate,
    gains,
    pe_w1,
    pe_w2,
    pe_w3,
    rates,
):
    chans = scalars.shape[0]
    tok_local = scalars.shape[1]
    shards = lax.axis_size("seq")
    rank = lax.axis_index("seq")
    length = tok_local * shards
    own = chans // shards
    depth = w_qkw_s.shape[0]
    tables = make_tables(shards, tok_local)
    positions = jnp.arange(length, dtype=jnp.int32)
    filt = []
    for layer in range(depth):
        third = lax.dynamic_slice_in_dim(pe_w3[layer], rank * own, own, axis=0)
        decay = lax.dynamic_slice_in_dim(rates[layer], rank * own, own, axis=0)
        made = filter_values(positions, length, pe_w1[layer], pe_w2[layer], third, decay)
        filt.append(made.reshape(own, shards, tok_local).transpose(1, 0, 2))
    filt = jnp.stack(filt, axis=1).astype(jnp.float32)
    filt_spec = forward_dft(filt, tables)
    state_s = scalars.astype(jnp.float32)
    state_v = vectors.astype(jnp.float32)
    for layer in range(depth):
        normed_s = scalar_norm(state_s, gains[layer, 0]).astype(jnp.bfloat16)
        normed_v = vector_norm(state_v, gains[layer, 1]).astype(jnp.bfloat16)
        proj_s = jnp.dot(w_qkw_s[layer], normed_s, preferred_element_type=jnp.float32)
        query_s = proj_s[:chans].astype(jnp.bfloat16)
        signal_s = (proj_s[chans : 2 * chans] * proj_s[2 * chans :]).astype(jnp.bfloat16)
        proj_v = jnp.einsum(
            "oc,jct->jot", w_qkw_v[layer], normed_v, preferred_element_type=jnp.float32
        ).astype(jnp.bfloat16)
        query_v = proj_v[:, :chans]
        key_v = proj_v[:, chans : 2 * chans].reshape(3, shards, own, tok_local)
        val_v = proj_v[:, 2 * chans :].reshape(3, shards, own, tok_local)
        outgoing = jnp.concatenate(
            [
                signal_s.reshape(shards, 1, own, tok_local),
                key_v.transpose(1, 0, 2, 3),
                val_v.transpose(1, 0, 2, 3),
            ],
            axis=1,
        )
        regrouped = lax.all_to_all(outgoing, "seq", 0, 0, tiled=True)
        convolved = convolve(regrouped, filt_spec[:, layer], tables)
        returned = lax.all_to_all(convolved, "seq", 0, 0, tiled=True)
        conv_s = returned[:, 0].reshape(chans, tok_local).astype(jnp.float32)
        conv_v = returned[:, 1:].transpose(1, 0, 2, 3).reshape(3, chans, tok_local)
        conv_v = conv_v.astype(jnp.float32)
        qs_f = query_s.astype(jnp.float32)
        out_s = (qs_f * conv_s + jnp.sum(query_v.astype(jnp.float32) * conv_v, axis=0)).astype(
            jnp.bfloat16
        )
        out_v = (qs_f[None] * conv_v).astype(jnp.bfloat16)
        state_s = state_s + jnp.dot(w_out_s[layer], out_s, preferred_element_type=jnp.float32)
        state_v = state_v + jnp.einsum(
            "oc,jct->jot", w_out_v[layer], out_v, preferred_element_type=jnp.float32
        )
        mlp_s = scalar_norm(state_s, gains[layer, 2]).astype(jnp.bfloat16)
        mlp_v = vector_norm(state_v, gains[layer, 3]).astype(jnp.bfloat16)
        hidden = jax.nn.gelu(
            jnp.dot(w_up[layer], mlp_s, preferred_element_type=jnp.float32)
        ).astype(jnp.bfloat16)
        gate = jax.nn.sigmoid(jnp.dot(w_gate[layer], mlp_s, preferred_element_type=jnp.float32))
        state_s = state_s + jnp.dot(w_down[layer], hidden, preferred_element_type=jnp.float32)
        state_v = (
            state_v
            + jnp.einsum("oc,jct->jot", w_mix[layer], mlp_v, preferred_element_type=jnp.float32)
            * gate[None]
        )
    return (state_s.astype(jnp.bfloat16), state_v.astype(jnp.bfloat16))


def solution(mesh):
    in_specs = (
        P(None, ("grp", "seq")),
        P(None, None, ("grp", "seq")),
        P(),
        P(),
        P(),
        P(),
        P(),
        P(),
        P(),
        P(),
        P(),
        P(),
        P(),
        P(),
        P(),
    )
    out_specs = (P(None, ("grp", "seq")), P(None, None, ("grp", "seq")))
    return jax.shard_map(
        per_device, mesh=mesh, in_specs=in_specs, out_specs=out_specs, check_vma=False
    )
```

```python
import math

import jax
import jax.numpy as jnp
import numpy as np
from jax import lax
from jax.sharding import PartitionSpec as P

HIGH = lax.Precision.HIGHEST
FAST = lax.Precision.DEFAULT


def filter_values(positions, length, first, second, third, decay):
    count = first.shape[1] // 2
    freqs = jnp.arange(1, count + 1, dtype=jnp.int32)
    turns = freqs[:, None] * positions[None, :] % length
    angle = turns.astype(jnp.float32) * (2.0 * math.pi / length)
    feats = jnp.concatenate([jnp.cos(angle), jnp.sin(angle)], axis=0)
    hid_one = jnp.sin(jnp.dot(first, feats, precision=HIGH))
    hid_two = jnp.sin(jnp.dot(second, hid_one, precision=HIGH))
    raw = jnp.dot(third, hid_two, precision=HIGH)
    envelope = jnp.exp(-decay[:, None] * positions[None, :].astype(jnp.float32) / length)
    return (raw * envelope / math.sqrt(length)).astype(jnp.bfloat16)


def scalar_norm(field, gain):
    return field * lax.rsqrt(jnp.mean(field * field, axis=0, keepdims=True) + 1e-05) * gain[:, None]


def vector_norm(field, gain):
    return (
        field
        * lax.rsqrt(jnp.mean(field * field, axis=(0, 1), keepdims=True) + 1e-05)
        * gain[None, :, None]
    )


def make_tables(shards, local):
    length = shards * local
    a = np.arange(shards)
    ang_s = 2.0 * np.pi * np.outer(a, a) / shards
    lead_fwd = np.concatenate([np.cos(ang_s), -np.sin(ang_s)], axis=0)
    lead_inv = np.concatenate([np.cos(ang_s), -np.sin(ang_s)], axis=1)
    b = np.arange(local)
    ang_t = 2.0 * np.pi * np.outer(a, b) / length
    tw_c = np.cos(ang_t)[:, None, None, :]
    tw_s = np.sin(ang_t)[:, None, None, :]
    ang_l = 2.0 * np.pi * np.outer(b, b) / local
    cos_l, sin_l = np.cos(ang_l), np.sin(ang_l)
    lane_fwd = np.block([[cos_l, -sin_l], [sin_l, cos_l]])
    lane_inv = np.block([[cos_l, sin_l], [-sin_l, cos_l]])
    f32 = lambda v: jnp.asarray(v, dtype=jnp.float32)
    return tuple(f32(v) for v in (lead_fwd, lead_inv, tw_c, tw_s, lane_fwd, lane_inv))


def forward_dft(field, tables, prec):
    lead_fwd, _, tw_c, tw_s, lane_fwd, _ = tables
    shards, planes, chans, local = field.shape
    stage = jnp.dot(lead_fwd, field.reshape(shards, -1), precision=prec)
    stage = stage.reshape(2 * shards, planes, chans, local)
    st_r, st_i = stage[:shards], stage[shards:]
    tw_r = st_r * tw_c + st_i * tw_s
    tw_i = st_i * tw_c - st_r * tw_s
    joined = jnp.concatenate([tw_r, tw_i], axis=-1).reshape(-1, 2 * local)
    spec = jnp.dot(joined, lane_fwd, precision=prec)
    return spec.reshape(shards, planes, chans, 2 * local)


def inverse_dft(spec, tables, prec):
    _, lead_inv, tw_c, tw_s, _, lane_inv = tables
    shards, planes, chans, width = spec.shape
    local = width // 2
    back = jnp.dot(spec.reshape(-1, width), lane_inv, precision=prec)
    back = back.reshape(shards, planes, chans, width)
    bk_r, bk_i = back[..., :local], back[..., local:]
    un_r = bk_r * tw_c - bk_i * tw_s
    un_i = bk_r * tw_s + bk_i * tw_c
    stacked = jnp.concatenate([un_r, un_i], axis=0).reshape(2 * shards, -1)
    whole = jnp.dot(lead_inv, stacked, precision=prec)
    return whole.reshape(shards, planes, chans, local)


def cmul(a_r, a_i, b_r, b_i):
    return a_r * b_r - a_i * b_i, a_r * b_i + a_i * b_r


def convolve(received, filt_spec, tables):
    shards, _, chans, local = received.shape
    length = shards * local
    spec = forward_dft(received.astype(jnp.float32), tables, FAST)
    re, im = spec[..., :local], spec[..., local:]
    h_r, h_i = filt_spec[..., :local], filt_spec[..., local:]
    p_r, p_i = cmul(re[:, 0], im[:, 0], h_r, h_i)
    outs_r, outs_i = [p_r], [p_i]
    for j in range(3):
        one, two = (j + 1) % 3, (j + 2) % 3
        a_r, a_i = cmul(re[:, 1 + one], im[:, 1 + one], re[:, 4 + two], im[:, 4 + two])
        b_r, b_i = cmul(re[:, 1 + two], im[:, 1 + two], re[:, 4 + one], im[:, 4 + one])
        outs_r.append(a_r - b_r)
        outs_i.append(a_i - b_i)
    prod = jnp.concatenate([jnp.stack(outs_r, axis=1), jnp.stack(outs_i, axis=1)], axis=-1)
    result = inverse_dft(prod, tables, FAST)
    inv_root = 1.0 / math.sqrt(length)
    scale = jnp.array([1.0, inv_root, inv_root, inv_root], dtype=jnp.float32) / length
    return (result * scale[None, :, None, None]).astype(jnp.bfloat16)


def per_device(
    scalars,
    vectors,
    w_qkw_s,
    w_qkw_v,
    w_out_s,
    w_out_v,
    w_up,
    w_down,
    w_mix,
    w_gate,
    gains,
    pe_w1,
    pe_w2,
    pe_w3,
    rates,
):
    chans = scalars.shape[0]
    tok_local = scalars.shape[1]
    shards = lax.axis_size("seq")
    rank = lax.axis_index("seq")
    length = tok_local * shards
    own = chans // shards
    depth = w_qkw_s.shape[0]
    tables = make_tables(shards, tok_local)
    positions = jnp.arange(length, dtype=jnp.int32)
    filt = []
    for layer in range(depth):
        third = lax.dynamic_slice_in_dim(pe_w3[layer], rank * own, own, axis=0)
        decay = lax.dynamic_slice_in_dim(rates[layer], rank * own, own, axis=0)
        made = filter_values(positions, length, pe_w1[layer], pe_w2[layer], third, decay)
        filt.append(made.reshape(own, shards, tok_local).transpose(1, 0, 2))
    filt = jnp.stack(filt, axis=1).astype(jnp.float32)
    filt_spec = forward_dft(filt, tables, FAST)
    state_s = scalars.astype(jnp.float32)
    state_v = vectors.astype(jnp.float32)
    for layer in range(depth):
        normed_s = scalar_norm(state_s, gains[layer, 0]).astype(jnp.bfloat16)
        normed_v = vector_norm(state_v, gains[layer, 1]).astype(jnp.bfloat16)
        proj_s = jnp.dot(w_qkw_s[layer], normed_s, preferred_element_type=jnp.float32)
        query_s = proj_s[:chans].astype(jnp.bfloat16)
        signal_s = (proj_s[chans : 2 * chans] * proj_s[2 * chans :]).astype(jnp.bfloat16)
        proj_v = jnp.stack(
            [
                jnp.dot(w_qkw_v[layer], normed_v[j], preferred_element_type=jnp.float32)
                for j in range(3)
            ]
        ).astype(jnp.bfloat16)
        query_v = proj_v[:, :chans]
        key_v = proj_v[:, chans : 2 * chans].reshape(3, shards, own, tok_local)
        val_v = proj_v[:, 2 * chans :].reshape(3, shards, own, tok_local)
        outgoing = jnp.concatenate(
            [
                signal_s.reshape(shards, 1, own, tok_local),
                key_v.transpose(1, 0, 2, 3),
                val_v.transpose(1, 0, 2, 3),
            ],
            axis=1,
        )
        regrouped = lax.all_to_all(outgoing, "seq", 0, 0, tiled=True)
        convolved = convolve(regrouped, filt_spec[:, layer], tables)
        returned = lax.all_to_all(convolved, "seq", 0, 0, tiled=True)
        conv_s = returned[:, 0].reshape(chans, tok_local).astype(jnp.float32)
        conv_v = returned[:, 1:].transpose(1, 0, 2, 3).reshape(3, chans, tok_local)
        conv_v = conv_v.astype(jnp.float32)
        qs_f = query_s.astype(jnp.float32)
        out_s = (qs_f * conv_s + jnp.sum(query_v.astype(jnp.float32) * conv_v, axis=0)).astype(
            jnp.bfloat16
        )
        out_v = (qs_f[None] * conv_v).astype(jnp.bfloat16)
        state_s = state_s + jnp.dot(w_out_s[layer], out_s, preferred_element_type=jnp.float32)
        state_v = state_v + jnp.einsum(
            "oc,jct->jot", w_out_v[layer], out_v, preferred_element_type=jnp.float32
        )
        mlp_s = scalar_norm(state_s, gains[layer, 2]).astype(jnp.bfloat16)
        mlp_v = vector_norm(state_v, gains[layer, 3]).astype(jnp.bfloat16)
        hidden = jax.nn.gelu(
            jnp.dot(w_up[layer], mlp_s, preferred_element_type=jnp.float32)
        ).astype(jnp.bfloat16)
        gate = jax.nn.sigmoid(jnp.dot(w_gate[layer], mlp_s, preferred_element_type=jnp.float32))
        state_s = state_s + jnp.dot(w_down[layer], hidden, preferred_element_type=jnp.float32)
        state_v = (
            state_v
            + jnp.einsum("oc,jct->jot", w_mix[layer], mlp_v, preferred_element_type=jnp.float32)
            * gate[None]
        )
    return (state_s.astype(jnp.bfloat16), state_v.astype(jnp.bfloat16))


def solution(mesh):
    in_specs = (
        P(None, ("grp", "seq")),
        P(None, None, ("grp", "seq")),
        P(),
        P(),
        P(),
        P(),
        P(),
        P(),
        P(),
        P(),
        P(),
        P(),
        P(),
        P(),
        P(),
    )
    out_specs = (P(None, ("grp", "seq")), P(None, None, ("grp", "seq")))
    return jax.shard_map(
        per_device, mesh=mesh, in_specs=in_specs, out_specs=out_specs, check_vma=False
    )
```

```python
import math

import jax
import jax.numpy as jnp
import numpy as np
from jax import lax
from jax.sharding import PartitionSpec as P

HIGH = lax.Precision.HIGHEST
FAST = lax.Precision.DEFAULT


def filter_values(positions, length, first, second, third, decay):
    count = first.shape[1] // 2
    freqs = jnp.arange(1, count + 1, dtype=jnp.int32)
    turns = freqs[:, None] * positions[None, :] % length
    angle = turns.astype(jnp.float32) * (2.0 * math.pi / length)
    feats = jnp.concatenate([jnp.cos(angle), jnp.sin(angle)], axis=0)
    hid_one = jnp.sin(jnp.dot(first, feats, precision=HIGH))
    hid_two = jnp.sin(jnp.dot(second, hid_one, precision=HIGH))
    raw = jnp.dot(third, hid_two, precision=HIGH)
    envelope = jnp.exp(-decay[:, None] * positions[None, :].astype(jnp.float32) / length)
    return (raw * envelope / math.sqrt(length)).astype(jnp.bfloat16)


def scalar_norm(field, gain):
    return field * lax.rsqrt(jnp.mean(field * field, axis=0, keepdims=True) + 1e-05) * gain[:, None]


def vector_norm(field, gain):
    return (
        field
        * lax.rsqrt(jnp.mean(field * field, axis=(0, 1), keepdims=True) + 1e-05)
        * gain[None, :, None]
    )


def make_tables(shards, local):
    length = shards * local
    a = np.arange(shards)
    ang_s = 2.0 * np.pi * np.outer(a, a) / shards
    lead_fwd = np.concatenate([np.cos(ang_s), -np.sin(ang_s)], axis=0)
    lead_inv = np.concatenate([np.cos(ang_s), -np.sin(ang_s)], axis=1)
    b = np.arange(local)
    ang_t = 2.0 * np.pi * np.outer(a, b) / length
    tw_c = np.cos(ang_t)[:, None, None, :]
    tw_s = np.sin(ang_t)[:, None, None, :]
    ang_l = 2.0 * np.pi * np.outer(b, b) / local
    cos_l, sin_l = np.cos(ang_l), np.sin(ang_l)
    lane_fwd = np.block([[cos_l, -sin_l], [sin_l, cos_l]])
    lane_inv = np.block([[cos_l, sin_l], [-sin_l, cos_l]])
    f32 = lambda v: jnp.asarray(v, dtype=jnp.float32)
    return tuple(f32(v) for v in (lead_fwd, lead_inv, tw_c, tw_s, lane_fwd, lane_inv))


def forward_dft(field, tables, prec):
    lead_fwd, _, tw_c, tw_s, lane_fwd, _ = tables
    shards, planes, chans, local = field.shape
    stage = jnp.dot(lead_fwd, field.reshape(shards, -1), precision=prec)
    stage = stage.reshape(2 * shards, planes, chans, local)
    st_r, st_i = stage[:shards], stage[shards:]
    tw_r = st_r * tw_c + st_i * tw_s
    tw_i = st_i * tw_c - st_r * tw_s
    joined = jnp.concatenate([tw_r, tw_i], axis=-1).reshape(-1, 2 * local)
    spec = jnp.dot(joined, lane_fwd, precision=prec)
    return spec.reshape(shards, planes, chans, 2 * local)


def inverse_dft(spec, tables, prec):
    _, lead_inv, tw_c, tw_s, _, lane_inv = tables
    shards, planes, chans, width = spec.shape
    local = width // 2
    back = jnp.dot(spec.reshape(-1, width), lane_inv, precision=prec)
    back = back.reshape(shards, planes, chans, width)
    bk_r, bk_i = back[..., :local], back[..., local:]
    un_r = bk_r * tw_c - bk_i * tw_s
    un_i = bk_r * tw_s + bk_i * tw_c
    stacked = jnp.concatenate([un_r, un_i], axis=0).reshape(2 * shards, -1)
    whole = jnp.dot(lead_inv, stacked, precision=prec)
    return whole.reshape(shards, planes, chans, local)


def cmul(a_r, a_i, b_r, b_i):
    return a_r * b_r - a_i * b_i, a_r * b_i + a_i * b_r


def convolve(received, filt_spec, tables):
    shards, _, chans, local = received.shape
    length = shards * local
    spec = forward_dft(received.astype(jnp.float32), tables, FAST)
    re, im = spec[..., :local], spec[..., local:]
    h_r, h_i = filt_spec[..., :local], filt_spec[..., local:]
    p_r, p_i = cmul(re[:, 0], im[:, 0], h_r, h_i)
    outs_r, outs_i = [p_r], [p_i]
    for j in range(3):
        one, two = (j + 1) % 3, (j + 2) % 3
        a_r, a_i = cmul(re[:, 1 + one], im[:, 1 + one], re[:, 4 + two], im[:, 4 + two])
        b_r, b_i = cmul(re[:, 1 + two], im[:, 1 + two], re[:, 4 + one], im[:, 4 + one])
        outs_r.append(a_r - b_r)
        outs_i.append(a_i - b_i)
    prod = jnp.concatenate([jnp.stack(outs_r, axis=1), jnp.stack(outs_i, axis=1)], axis=-1)
    result = inverse_dft(prod, tables, FAST)
    inv_root = 1.0 / math.sqrt(length)
    scale = jnp.array([1.0, inv_root, inv_root, inv_root], dtype=jnp.float32) / length
    return (result * scale[None, :, None, None]).astype(jnp.bfloat16)


def per_device(
    scalars,
    vectors,
    w_qkw_s,
    w_qkw_v,
    w_out_s,
    w_out_v,
    w_up,
    w_down,
    w_mix,
    w_gate,
    gains,
    pe_w1,
    pe_w2,
    pe_w3,
    rates,
):
    chans = scalars.shape[0]
    tok_local = scalars.shape[1]
    shards = lax.axis_size("seq")
    rank = lax.axis_index("seq")
    length = tok_local * shards
    own = chans // shards
    depth = w_qkw_s.shape[0]
    tables = make_tables(shards, tok_local)
    positions = jnp.arange(length, dtype=jnp.int32)

    def filter_spec(first, second, third, decay):
        third = lax.dynamic_slice_in_dim(third, rank * own, own, axis=0)
        decay = lax.dynamic_slice_in_dim(decay, rank * own, own, axis=0)
        made = filter_values(positions, length, first, second, third, decay)
        made = made.reshape(own, shards, tok_local).transpose(1, 0, 2)
        return forward_dft(made[:, None].astype(jnp.float32), tables, FAST)[:, 0]

    spec_next = filter_spec(pe_w1[0], pe_w2[0], pe_w3[0], rates[0])
    state_s = scalars.astype(jnp.float32)
    state_v = vectors.astype(jnp.float32)
    for layer in range(depth):
        normed_s = scalar_norm(state_s, gains[layer, 0]).astype(jnp.bfloat16)
        normed_v = vector_norm(state_v, gains[layer, 1]).astype(jnp.bfloat16)
        proj_s = jnp.dot(w_qkw_s[layer], normed_s, preferred_element_type=jnp.float32)
        query_s = proj_s[:chans].astype(jnp.bfloat16)
        signal_s = (proj_s[chans : 2 * chans] * proj_s[2 * chans :]).astype(jnp.bfloat16)
        proj_v = jnp.stack(
            [
                jnp.dot(w_qkw_v[layer], normed_v[j], preferred_element_type=jnp.float32)
                for j in range(3)
            ]
        ).astype(jnp.bfloat16)
        query_v = proj_v[:, :chans]
        key_v = proj_v[:, chans : 2 * chans].reshape(3, shards, own, tok_local)
        val_v = proj_v[:, 2 * chans :].reshape(3, shards, own, tok_local)
        outgoing = jnp.concatenate(
            [
                signal_s.reshape(shards, 1, own, tok_local),
                key_v.transpose(1, 0, 2, 3),
                val_v.transpose(1, 0, 2, 3),
            ],
            axis=1,
        )
        regrouped = lax.all_to_all(outgoing, "seq", 0, 0, tiled=True)
        convolved = convolve(regrouped, spec_next, tables)
        if layer + 1 < depth:
            tied = lax.optimization_barrier(
                (pe_w1[layer + 1], pe_w2[layer + 1], pe_w3[layer + 1], rates[layer + 1], convolved)
            )
            spec_next = filter_spec(*tied[:4])
        returned = lax.all_to_all(convolved, "seq", 0, 0, tiled=True)
        conv_s = returned[:, 0].reshape(chans, tok_local).astype(jnp.float32)
        conv_v = returned[:, 1:].transpose(1, 0, 2, 3).reshape(3, chans, tok_local)
        conv_v = conv_v.astype(jnp.float32)
        qs_f = query_s.astype(jnp.float32)
        out_s = (qs_f * conv_s + jnp.sum(query_v.astype(jnp.float32) * conv_v, axis=0)).astype(
            jnp.bfloat16
        )
        out_v = (qs_f[None] * conv_v).astype(jnp.bfloat16)
        state_s = state_s + jnp.dot(w_out_s[layer], out_s, preferred_element_type=jnp.float32)
        state_v = state_v + jnp.einsum(
            "oc,jct->jot", w_out_v[layer], out_v, preferred_element_type=jnp.float32
        )
        mlp_s = scalar_norm(state_s, gains[layer, 2]).astype(jnp.bfloat16)
        mlp_v = vector_norm(state_v, gains[layer, 3]).astype(jnp.bfloat16)
        hidden = jax.nn.gelu(
            jnp.dot(w_up[layer], mlp_s, preferred_element_type=jnp.float32)
        ).astype(jnp.bfloat16)
        gate = jax.nn.sigmoid(jnp.dot(w_gate[layer], mlp_s, preferred_element_type=jnp.float32))
        state_s = state_s + jnp.dot(w_down[layer], hidden, preferred_element_type=jnp.float32)
        state_v = (
            state_v
            + jnp.einsum("oc,jct->jot", w_mix[layer], mlp_v, preferred_element_type=jnp.float32)
            * gate[None]
        )
    return (state_s.astype(jnp.bfloat16), state_v.astype(jnp.bfloat16))


def solution(mesh):
    in_specs = (
        P(None, ("grp", "seq")),
        P(None, None, ("grp", "seq")),
        P(),
        P(),
        P(),
        P(),
        P(),
        P(),
        P(),
        P(),
        P(),
        P(),
        P(),
        P(),
        P(),
    )
    out_specs = (P(None, ("grp", "seq")), P(None, None, ("grp", "seq")))
    return jax.shard_map(
        per_device, mesh=mesh, in_specs=in_specs, out_specs=out_specs, check_vma=False
    )
```

```python
import math

import jax
import jax.numpy as jnp
import numpy as np
from jax import lax
from jax.experimental import pallas as pl
from jax.sharding import PartitionSpec as P

HIGH = lax.Precision.HIGHEST
FAST = lax.Precision.DEFAULT


def filter_values(positions, length, first, second, third, decay):
    count = first.shape[1] // 2
    freqs = jnp.arange(1, count + 1, dtype=jnp.int32)
    turns = freqs[:, None] * positions[None, :] % length
    angle = turns.astype(jnp.float32) * (2.0 * math.pi / length)
    feats = jnp.concatenate([jnp.cos(angle), jnp.sin(angle)], axis=0)
    hid_one = jnp.sin(jnp.dot(first, feats, precision=HIGH))
    hid_two = jnp.sin(jnp.dot(second, hid_one, precision=HIGH))
    raw = jnp.dot(third, hid_two, precision=HIGH)
    envelope = jnp.exp(-decay[:, None] * positions[None, :].astype(jnp.float32) / length)
    return (raw * envelope / math.sqrt(length)).astype(jnp.bfloat16)


def scalar_norm(field, gain):
    return field * lax.rsqrt(jnp.mean(field * field, axis=0, keepdims=True) + 1e-05) * gain[:, None]


def vector_norm(field, gain):
    return (
        field
        * lax.rsqrt(jnp.mean(field * field, axis=(0, 1), keepdims=True) + 1e-05)
        * gain[None, :, None]
    )


def make_tables(shards, local):
    length = shards * local
    a = np.arange(shards)
    ang_s = 2.0 * np.pi * np.outer(a, a) / shards
    lead_fwd = np.concatenate([np.cos(ang_s), -np.sin(ang_s)], axis=0)
    lead_inv = np.concatenate([np.cos(ang_s), -np.sin(ang_s)], axis=1)
    b = np.arange(local)
    ang_t = 2.0 * np.pi * np.outer(a, b) / length
    tw_c = np.cos(ang_t)[:, None, None, :]
    tw_s = np.sin(ang_t)[:, None, None, :]
    ang_l = 2.0 * np.pi * np.outer(b, b) / local
    cos_l, sin_l = np.cos(ang_l), np.sin(ang_l)
    lane_fwd = np.block([[cos_l, -sin_l], [sin_l, cos_l]])
    lane_inv = np.block([[cos_l, sin_l], [-sin_l, cos_l]])
    f32 = lambda v: jnp.asarray(v, dtype=jnp.float32)
    return tuple(f32(v) for v in (lead_fwd, lead_inv, tw_c, tw_s, lane_fwd, lane_inv))


def forward_dft(field, tables, prec):
    lead_fwd, _, tw_c, tw_s, lane_fwd, _ = tables
    shards, planes, chans, local = field.shape
    stage = jnp.dot(lead_fwd, field.reshape(shards, -1), precision=prec)
    stage = stage.reshape(2 * shards, planes, chans, local)
    st_r, st_i = stage[:shards], stage[shards:]
    tw_r = st_r * tw_c + st_i * tw_s
    tw_i = st_i * tw_c - st_r * tw_s
    joined = jnp.concatenate([tw_r, tw_i], axis=-1).reshape(-1, 2 * local)
    spec = jnp.dot(joined, lane_fwd, precision=prec)
    return spec.reshape(shards, planes, chans, 2 * local)


def inverse_dft(spec, tables, prec):
    _, lead_inv, tw_c, tw_s, _, lane_inv = tables
    shards, planes, chans, width = spec.shape
    local = width // 2
    back = jnp.dot(spec.reshape(-1, width), lane_inv, precision=prec)
    back = back.reshape(shards, planes, chans, width)
    bk_r, bk_i = back[..., :local], back[..., local:]
    un_r = bk_r * tw_c - bk_i * tw_s
    un_i = bk_r * tw_s + bk_i * tw_c
    stacked = jnp.concatenate([un_r, un_i], axis=0).reshape(2 * shards, -1)
    whole = jnp.dot(lead_inv, stacked, precision=prec)
    return whole.reshape(shards, planes, chans, local)


def cmul(a_r, a_i, b_r, b_i):
    return a_r * b_r - a_i * b_i, a_r * b_i + a_i * b_r


def convolve(received, filt_spec, tables):
    shards, _, chans, local = received.shape
    length = shards * local
    spec = forward_dft(received.astype(jnp.float32), tables, FAST)
    re, im = spec[..., :local], spec[..., local:]
    h_r, h_i = filt_spec[..., :local], filt_spec[..., local:]
    p_r, p_i = cmul(re[:, 0], im[:, 0], h_r, h_i)
    outs_r, outs_i = [p_r], [p_i]
    for j in range(3):
        one, two = (j + 1) % 3, (j + 2) % 3
        a_r, a_i = cmul(re[:, 1 + one], im[:, 1 + one], re[:, 4 + two], im[:, 4 + two])
        b_r, b_i = cmul(re[:, 1 + two], im[:, 1 + two], re[:, 4 + one], im[:, 4 + one])
        outs_r.append(a_r - b_r)
        outs_i.append(a_i - b_i)
    prod = jnp.concatenate([jnp.stack(outs_r, axis=1), jnp.stack(outs_i, axis=1)], axis=-1)
    result = inverse_dft(prod, tables, FAST)
    inv_root = 1.0 / math.sqrt(length)
    scale = jnp.array([1.0, inv_root, inv_root, inv_root], dtype=jnp.float32) / length
    return (result * scale[None, :, None, None]).astype(jnp.bfloat16)


def gelu_tanh(x):
    return 0.5 * x * (1.0 + jnp.tanh(math.sqrt(2.0 / math.pi) * (x + 0.044715 * (x * x * x))))


def token_step(post, pre, arrays, weights):
    f32, bf16 = jnp.float32, jnp.bfloat16
    state_s, state_v = arrays["state_s"], arrays["state_v"]
    chans, tok = state_s.shape
    full = lambda shape: pl.BlockSpec(shape, lambda i, n=len(shape): (0,) * n)

    def layer_spec(w, layer):
        return pl.BlockSpec((pl.Squeezed(),) + w.shape[1:], lambda i: (layer,) + (0,) * (w.ndim - 1))

    ins, specs = [state_s, state_v], [full(state_s.shape), full(state_v.shape)]
    post_names = ("w_out_s", "w_out_v", "w_up", "w_down", "w_mix", "w_gate")
    if post is not None:
        ins += [arrays["conv"], arrays["query"]]
        specs += [full(arrays["conv"].shape), full(arrays["query"].shape)]
        for name in post_names + ("gains_t",):
            ins.append(weights[name])
            specs.append(layer_spec(weights[name], post))
    if pre is not None:
        for name in ("w_qkw_s", "w_qkw_v", "gains_t"):
            ins.append(weights[name])
            specs.append(layer_spec(weights[name], pre))
    outs = []
    if pre is not None:
        outs += [((7, chans, tok), bf16), ((4, chans, tok), bf16)]
        if post is not None:
            outs += [((chans, tok), f32), ((3, chans, tok), f32)]
    else:
        outs += [((chans, tok), bf16), ((3, chans, tok), bf16)]

    def snorm(x, g):
        return x * lax.rsqrt(jnp.mean(x * x, axis=0, keepdims=True) + 1e-05) * g

    def vnorm(xs, g):
        total = sum(jnp.sum(x * x, axis=0, keepdims=True) for x in xs)
        scale = lax.rsqrt(total / (3 * chans) + 1e-05)
        return [x * scale * g for x in xs]

    def mm(w, x):
        return jnp.dot(w, x, preferred_element_type=f32)

    def kernel(*refs):
        refs = list(refs)
        ss_ref, sv_ref = refs.pop(0), refs.pop(0)
        ss = ss_ref[...].astype(f32)
        sv = [sv_ref[j].astype(f32) for j in range(3)]
        if post is not None:
            conv_ref, q_ref = refs.pop(0), refs.pop(0)
            wos, wov, wup, wdn, wmx, wgt, gp = [refs.pop(0) for _ in range(7)]
            g = gp[...]
            qs = q_ref[0].astype(f32)
            ys = conv_ref[0].astype(f32)
            yv = [conv_ref[1 + j].astype(f32) for j in range(3)]
            mix = q_ref[1].astype(f32) * yv[0]
            mix = mix + q_ref[2].astype(f32) * yv[1]
            mix = mix + q_ref[3].astype(f32) * yv[2]
            out_s = (qs * ys + mix).astype(bf16)
            ss = ss + mm(wos[...], out_s)
            sv = [sv[j] + mm(wov[...], (qs * yv[j]).astype(bf16)) for j in range(3)]
            mlp_s = snorm(ss, g[:, 2:3]).astype(bf16)
            mlp_v = [v.astype(bf16) for v in vnorm(sv, g[:, 3:4])]
            hidden = gelu_tanh(mm(wup[...], mlp_s)).astype(bf16)
            gate = 1.0 / (1.0 + jnp.exp(-mm(wgt[...], mlp_s)))
            ss = ss + mm(wdn[...], hidden)
            sv = [sv[j] + mm(wmx[...], mlp_v[j]) * gate for j in range(3)]
        if pre is not None:
            wqs, wqv, gq = [refs.pop(0) for _ in range(3)]
            g = gq[...]
            planes_ref, query_ref = refs.pop(0), refs.pop(0)
            normed_s = snorm(ss, g[:, 0:1]).astype(bf16)
            normed_v = [v.astype(bf16) for v in vnorm(sv, g[:, 1:2])]
            ps = mm(wqs[...], normed_s)
            query_ref[0] = ps[:chans].astype(bf16)
            planes_ref[0] = (ps[chans : 2 * chans] * ps[2 * chans :]).astype(bf16)
            for j in range(3):
                pv = mm(wqv[...], normed_v[j]).astype(bf16)
                query_ref[1 + j] = pv[:chans]
                planes_ref[1 + j] = pv[chans : 2 * chans]
                planes_ref[4 + j] = pv[2 * chans :]
            if post is not None:
                ns_ref, nv_ref = refs.pop(0), refs.pop(0)
                ns_ref[...] = ss
                for j in range(3):
                    nv_ref[j] = sv[j]
        else:
            os_ref, ov_ref = refs.pop(0), refs.pop(0)
            os_ref[...] = ss.astype(bf16)
            for j in range(3):
                ov_ref[j] = sv[j].astype(bf16)

    return pl.pallas_call(
        kernel,
        grid=(1,),
        in_specs=specs,
        out_specs=[full(shape) for shape, _ in outs],
        out_shape=[jax.ShapeDtypeStruct(shape, dtype) for shape, dtype in outs],
    )(*ins)


def per_device(
    scalars,
    vectors,
    w_qkw_s,
    w_qkw_v,
    w_out_s,
    w_out_v,
    w_up,
    w_down,
    w_mix,
    w_gate,
    gains,
    pe_w1,
    pe_w2,
    pe_w3,
    rates,
):
    chans = scalars.shape[0]
    tok_local = scalars.shape[1]
    shards = lax.axis_size("seq")
    rank = lax.axis_index("seq")
    length = tok_local * shards
    own = chans // shards
    depth = w_qkw_s.shape[0]
    tables = make_tables(shards, tok_local)
    positions = jnp.arange(length, dtype=jnp.int32)

    def filter_spec(first, second, third, decay):
        third = lax.dynamic_slice_in_dim(third, rank * own, own, axis=0)
        decay = lax.dynamic_slice_in_dim(decay, rank * own, own, axis=0)
        made = filter_values(positions, length, first, second, third, decay)
        made = made.reshape(own, shards, tok_local).transpose(1, 0, 2)
        return forward_dft(made[:, None].astype(jnp.float32), tables, FAST)[:, 0]

    spec_next = filter_spec(pe_w1[0], pe_w2[0], pe_w3[0], rates[0])
    weights = {
        "w_qkw_s": w_qkw_s,
        "w_qkw_v": w_qkw_v,
        "w_out_s": w_out_s,
        "w_out_v": w_out_v,
        "w_up": w_up,
        "w_down": w_down,
        "w_mix": w_mix,
        "w_gate": w_gate,
        "gains_t": gains.transpose(0, 2, 1),
    }
    arrays = {"state_s": scalars, "state_v": vectors}
    planes, query = token_step(None, 0, arrays, weights)
    for layer in range(depth):
        outgoing = planes.reshape(7, shards, own, tok_local).transpose(1, 0, 2, 3)
        regrouped = lax.all_to_all(outgoing, "seq", 0, 0, tiled=True)
        convolved = convolve(regrouped, spec_next, tables)
        if layer + 1 < depth:
            tied = lax.optimization_barrier(
                (pe_w1[layer + 1], pe_w2[layer + 1], pe_w3[layer + 1], rates[layer + 1], convolved)
            )
            spec_next = filter_spec(*tied[:4])
        returned = lax.all_to_all(convolved, "seq", 0, 0, tiled=True)
        arrays["conv"] = returned.transpose(1, 0, 2, 3).reshape(4, chans, tok_local)
        arrays["query"] = query
        if layer + 1 < depth:
            planes, query, new_s, new_v = token_step(layer, layer + 1, arrays, weights)
            arrays["state_s"], arrays["state_v"] = new_s, new_v
        else:
            return tuple(token_step(layer, None, arrays, weights))


def solution(mesh):
    in_specs = (
        P(None, ("grp", "seq")),
        P(None, None, ("grp", "seq")),
        P(),
        P(),
        P(),
        P(),
        P(),
        P(),
        P(),
        P(),
        P(),
        P(),
        P(),
        P(),
        P(),
    )
    out_specs = (P(None, ("grp", "seq")), P(None, None, ("grp", "seq")))
    return jax.shard_map(
        per_device, mesh=mesh, in_specs=in_specs, out_specs=out_specs, check_vma=False
    )
```

```python
import math

import jax
import jax.numpy as jnp
import numpy as np
from jax import lax
from jax.experimental import pallas as pl
from jax.sharding import PartitionSpec as P

HIGH = lax.Precision.HIGHEST
FAST = lax.Precision.DEFAULT


def filter_values(positions, length, first, second, third, decay):
    count = first.shape[1] // 2
    freqs = jnp.arange(1, count + 1, dtype=jnp.int32)
    turns = freqs[:, None] * positions[None, :] % length
    angle = turns.astype(jnp.float32) * (2.0 * math.pi / length)
    feats = jnp.concatenate([jnp.cos(angle), jnp.sin(angle)], axis=0)
    hid_one = jnp.sin(jnp.dot(first, feats, precision=HIGH))
    hid_two = jnp.sin(jnp.dot(second, hid_one, precision=HIGH))
    raw = jnp.dot(third, hid_two, precision=HIGH)
    envelope = jnp.exp(-decay[:, None] * positions[None, :].astype(jnp.float32) / length)
    return (raw * envelope / math.sqrt(length)).astype(jnp.bfloat16)


def scalar_norm(field, gain):
    return field * lax.rsqrt(jnp.mean(field * field, axis=0, keepdims=True) + 1e-05) * gain[:, None]


def vector_norm(field, gain):
    return (
        field
        * lax.rsqrt(jnp.mean(field * field, axis=(0, 1), keepdims=True) + 1e-05)
        * gain[None, :, None]
    )


def make_tables(shards, local):
    length = shards * local
    a = np.arange(shards)
    ang_s = 2.0 * np.pi * np.outer(a, a) / shards
    lead_fwd = np.concatenate([np.cos(ang_s), -np.sin(ang_s)], axis=0)
    lead_inv = np.concatenate([np.cos(ang_s), -np.sin(ang_s)], axis=1)
    b = np.arange(local)
    ang_t = 2.0 * np.pi * np.outer(a, b) / length
    tw_c = np.cos(ang_t)[:, None, None, :]
    tw_s = np.sin(ang_t)[:, None, None, :]
    ang_l = 2.0 * np.pi * np.outer(b, b) / local
    cos_l, sin_l = np.cos(ang_l), np.sin(ang_l)
    lane_fwd = np.block([[cos_l, -sin_l], [sin_l, cos_l]])
    lane_inv = np.block([[cos_l, sin_l], [-sin_l, cos_l]])
    f32 = lambda v: jnp.asarray(v, dtype=jnp.float32)
    return tuple(f32(v) for v in (lead_fwd, lead_inv, tw_c, tw_s, lane_fwd, lane_inv))


def forward_dft(field, tables, prec):
    lead_fwd, _, tw_c, tw_s, lane_fwd, _ = tables
    shards, planes, chans, local = field.shape
    stage = jnp.dot(lead_fwd, field.reshape(shards, -1), precision=prec)
    stage = stage.reshape(2 * shards, planes, chans, local)
    st_r, st_i = stage[:shards], stage[shards:]
    tw_r = st_r * tw_c + st_i * tw_s
    tw_i = st_i * tw_c - st_r * tw_s
    joined = jnp.concatenate([tw_r, tw_i], axis=-1).reshape(-1, 2 * local)
    spec = jnp.dot(joined, lane_fwd, precision=prec)
    return spec.reshape(shards, planes, chans, 2 * local)


def inverse_dft(spec, tables, prec):
    _, lead_inv, tw_c, tw_s, _, lane_inv = tables
    shards, planes, chans, width = spec.shape
    local = width // 2
    back = jnp.dot(spec.reshape(-1, width), lane_inv, precision=prec)
    back = back.reshape(shards, planes, chans, width)
    bk_r, bk_i = back[..., :local], back[..., local:]
    un_r = bk_r * tw_c - bk_i * tw_s
    un_i = bk_r * tw_s + bk_i * tw_c
    stacked = jnp.concatenate([un_r, un_i], axis=0).reshape(2 * shards, -1)
    whole = jnp.dot(lead_inv, stacked, precision=prec)
    return whole.reshape(shards, planes, chans, local)


def cmul(a_r, a_i, b_r, b_i):
    return a_r * b_r - a_i * b_i, a_r * b_i + a_i * b_r


def convolve(received, filt_spec, tables):
    shards, _, chans, local = received.shape
    length = shards * local
    spec = forward_dft(received.astype(jnp.float32), tables, FAST)
    re, im = spec[..., :local], spec[..., local:]
    h_r, h_i = filt_spec[..., :local], filt_spec[..., local:]
    p_r, p_i = cmul(re[:, 0], im[:, 0], h_r, h_i)
    outs_r, outs_i = [p_r], [p_i]
    for j in range(3):
        one, two = (j + 1) % 3, (j + 2) % 3
        a_r, a_i = cmul(re[:, 1 + one], im[:, 1 + one], re[:, 4 + two], im[:, 4 + two])
        b_r, b_i = cmul(re[:, 1 + two], im[:, 1 + two], re[:, 4 + one], im[:, 4 + one])
        outs_r.append(a_r - b_r)
        outs_i.append(a_i - b_i)
    prod = jnp.concatenate([jnp.stack(outs_r, axis=1), jnp.stack(outs_i, axis=1)], axis=-1)
    result = inverse_dft(prod, tables, FAST)
    inv_root = 1.0 / math.sqrt(length)
    scale = jnp.array([1.0, inv_root, inv_root, inv_root], dtype=jnp.float32) / length
    return (result * scale[None, :, None, None]).astype(jnp.bfloat16)


def gelu_tanh(x):
    return 0.5 * x * (1.0 + jnp.tanh(math.sqrt(2.0 / math.pi) * (x + 0.044715 * (x * x * x))))


def token_step(post, pre, arrays, weights, shards):
    f32, bf16 = jnp.float32, jnp.bfloat16
    state_s, state_v = arrays["state_s"], arrays["state_v"]
    chans, tok = state_s.shape
    own = chans // shards
    packed = own % 16 == 0
    full = lambda shape: pl.BlockSpec(shape, lambda i, n=len(shape): (0,) * n)

    def layer_spec(w, layer):
        return pl.BlockSpec((pl.Squeezed(),) + w.shape[1:], lambda i: (layer,) + (0,) * (w.ndim - 1))

    ins, specs = [state_s, state_v], [full(state_s.shape), full(state_v.shape)]
    post_names = ("w_out_s", "w_out_v", "w_up", "w_down", "w_mix", "w_gate")
    if post is not None:
        ins += [arrays["conv"], arrays["query"]]
        specs += [full(arrays["conv"].shape), full(arrays["query"].shape)]
        for name in post_names + ("gains_t",):
            ins.append(weights[name])
            specs.append(layer_spec(weights[name], post))
    if pre is not None:
        for name in ("w_qkw_s", "w_qkw_v", "gains_t"):
            ins.append(weights[name])
            specs.append(layer_spec(weights[name], pre))
    outs = []
    if pre is not None:
        plane_shape = (shards, 7, own, tok) if packed else (7, chans, tok)
        outs += [(plane_shape, bf16), ((4, chans, tok), bf16)]
        if post is not None:
            outs += [((chans, tok), f32), ((3, chans, tok), f32)]
    else:
        outs += [((chans, tok), bf16), ((3, chans, tok), bf16)]

    def snorm(x, g):
        return x * lax.rsqrt(jnp.mean(x * x, axis=0, keepdims=True) + 1e-05) * g

    def vnorm(xs, g):
        total = sum(jnp.sum(x * x, axis=0, keepdims=True) for x in xs)
        scale = lax.rsqrt(total / (3 * chans) + 1e-05)
        return [x * scale * g for x in xs]

    def mm(w, x):
        return jnp.dot(w, x, preferred_element_type=f32)

    def kernel(*refs):
        refs = list(refs)
        ss_ref, sv_ref = refs.pop(0), refs.pop(0)
        ss = ss_ref[...].astype(f32)
        sv = [sv_ref[j].astype(f32) for j in range(3)]
        if post is not None:
            conv_ref, q_ref = refs.pop(0), refs.pop(0)
            wos, wov, wup, wdn, wmx, wgt, gp = [refs.pop(0) for _ in range(7)]
            g = gp[...].T
            qs = q_ref[0].astype(f32)
            if packed:
                planes = [jnp.concatenate([conv_ref[d, p] for d in range(shards)], axis=0) for p in range(4)]
            else:
                planes = [conv_ref[p] for p in range(4)]
            ys = planes[0].astype(f32)
            yv = [planes[1 + j].astype(f32) for j in range(3)]
            mix = q_ref[1].astype(f32) * yv[0]
            mix = mix + q_ref[2].astype(f32) * yv[1]
            mix = mix + q_ref[3].astype(f32) * yv[2]
            out_s = (qs * ys + mix).astype(bf16)
            ss = ss + mm(wos[...], out_s)
            sv = [sv[j] + mm(wov[...], (qs * yv[j]).astype(bf16)) for j in range(3)]
            mlp_s = snorm(ss, g[:, 2:3]).astype(bf16)
            mlp_v = [v.astype(bf16) for v in vnorm(sv, g[:, 3:4])]
            hidden = gelu_tanh(mm(wup[...], mlp_s)).astype(bf16)
            gate = 1.0 / (1.0 + jnp.exp(-mm(wgt[...], mlp_s)))
            ss = ss + mm(wdn[...], hidden)
            sv = [sv[j] + mm(wmx[...], mlp_v[j]) * gate for j in range(3)]
        if pre is not None:
            wqs, wqv, gq = [refs.pop(0) for _ in range(3)]
            g = gq[...].T
            planes_ref, query_ref = refs.pop(0), refs.pop(0)

            def put(p, value):
                if packed:
                    for d in range(shards):
                        planes_ref[d, p] = value[d * own : (d + 1) * own]
                else:
                    planes_ref[p] = value

            normed_s = snorm(ss, g[:, 0:1]).astype(bf16)
            normed_v = [v.astype(bf16) for v in vnorm(sv, g[:, 1:2])]
            ps = mm(wqs[...], normed_s)
            query_ref[0] = ps[:chans].astype(bf16)
            put(0, (ps[chans : 2 * chans] * ps[2 * chans :]).astype(bf16))
            for j in range(3):
                pv = mm(wqv[...], normed_v[j]).astype(bf16)
                query_ref[1 + j] = pv[:chans]
                put(1 + j, pv[chans : 2 * chans])
                put(4 + j, pv[2 * chans :])
            if post is not None:
                ns_ref, nv_ref = refs.pop(0), refs.pop(0)
                ns_ref[...] = ss
                for j in range(3):
                    nv_ref[j] = sv[j]
        else:
            os_ref, ov_ref = refs.pop(0), refs.pop(0)
            os_ref[...] = ss.astype(bf16)
            for j in range(3):
                ov_ref[j] = sv[j].astype(bf16)

    return pl.pallas_call(
        kernel,
        grid=(1,),
        in_specs=specs,
        out_specs=[full(shape) for shape, _ in outs],
        out_shape=[jax.ShapeDtypeStruct(shape, dtype) for shape, dtype in outs],
    )(*ins)


def per_device(
    scalars,
    vectors,
    w_qkw_s,
    w_qkw_v,
    w_out_s,
    w_out_v,
    w_up,
    w_down,
    w_mix,
    w_gate,
    gains,
    pe_w1,
    pe_w2,
    pe_w3,
    rates,
):
    chans = scalars.shape[0]
    tok_local = scalars.shape[1]
    shards = lax.axis_size("seq")
    rank = lax.axis_index("seq")
    length = tok_local * shards
    own = chans // shards
    depth = w_qkw_s.shape[0]
    tables = make_tables(shards, tok_local)
    positions = jnp.arange(length, dtype=jnp.int32)

    def filter_spec(first, second, third, decay):
        third = lax.dynamic_slice_in_dim(third, rank * own, own, axis=0)
        decay = lax.dynamic_slice_in_dim(decay, rank * own, own, axis=0)
        made = filter_values(positions, length, first, second, third, decay)
        made = made.reshape(own, shards, tok_local).transpose(1, 0, 2)
        return forward_dft(made[:, None].astype(jnp.float32), tables, FAST)[:, 0]

    spec_next = filter_spec(pe_w1[0], pe_w2[0], pe_w3[0], rates[0])
    weights = {
        "w_qkw_s": w_qkw_s,
        "w_qkw_v": w_qkw_v,
        "w_out_s": w_out_s,
        "w_out_v": w_out_v,
        "w_up": w_up,
        "w_down": w_down,
        "w_mix": w_mix,
        "w_gate": w_gate,
        "gains_t": gains,
    }
    arrays = {"state_s": scalars, "state_v": vectors}
    packed = own % 16 == 0
    planes, query = token_step(None, 0, arrays, weights, shards)
    for layer in range(depth):
        outgoing = planes
        if not packed:
            outgoing = planes.reshape(7, shards, own, tok_local).transpose(1, 0, 2, 3)
        regrouped = lax.all_to_all(outgoing, "seq", 0, 0, tiled=True)
        convolved = convolve(regrouped, spec_next, tables)
        if layer + 1 < depth:
            tied = lax.optimization_barrier(
                (pe_w1[layer + 1], pe_w2[layer + 1], pe_w3[layer + 1], rates[layer + 1], convolved)
            )
            spec_next = filter_spec(*tied[:4])
        returned = lax.all_to_all(convolved, "seq", 0, 0, tiled=True)
        arrays["conv"] = returned
        if not packed:
            arrays["conv"] = returned.transpose(1, 0, 2, 3).reshape(4, chans, tok_local)
        arrays["query"] = query
        if layer + 1 < depth:
            planes, query, new_s, new_v = token_step(layer, layer + 1, arrays, weights, shards)
            arrays["state_s"], arrays["state_v"] = new_s, new_v
        else:
            return tuple(token_step(layer, None, arrays, weights, shards))


def solution(mesh):
    in_specs = (
        P(None, ("grp", "seq")),
        P(None, None, ("grp", "seq")),
        P(),
        P(),
        P(),
        P(),
        P(),
        P(),
        P(),
        P(),
        P(),
        P(),
        P(),
        P(),
        P(),
    )
    out_specs = (P(None, ("grp", "seq")), P(None, None, ("grp", "seq")))
    return jax.shard_map(
        per_device, mesh=mesh, in_specs=in_specs, out_specs=out_specs, check_vma=False
    )
```

```python
import math

import jax
import jax.numpy as jnp
import numpy as np
from jax import lax
from jax.experimental import pallas as pl
from jax.sharding import PartitionSpec as P

HIGH = lax.Precision.HIGHEST
FAST = lax.Precision.DEFAULT


def filter_values(positions, length, first, second, third, decay):
    count = first.shape[1] // 2
    freqs = jnp.arange(1, count + 1, dtype=jnp.int32)
    turns = freqs[:, None] * positions[None, :] % length
    angle = turns.astype(jnp.float32) * (2.0 * math.pi / length)
    feats = jnp.concatenate([jnp.cos(angle), jnp.sin(angle)], axis=0)
    hid_one = jnp.sin(jnp.dot(first, feats, precision=HIGH))
    hid_two = jnp.sin(jnp.dot(second, hid_one, precision=HIGH))
    raw = jnp.dot(third, hid_two, precision=HIGH)
    envelope = jnp.exp(-decay[:, None] * positions[None, :].astype(jnp.float32) / length)
    return (raw * envelope / math.sqrt(length)).astype(jnp.bfloat16)


def scalar_norm(field, gain):
    return field * lax.rsqrt(jnp.mean(field * field, axis=0, keepdims=True) + 1e-05) * gain[:, None]


def vector_norm(field, gain):
    return (
        field
        * lax.rsqrt(jnp.mean(field * field, axis=(0, 1), keepdims=True) + 1e-05)
        * gain[None, :, None]
    )


def make_tables(shards, local):
    length = shards * local
    a = np.arange(shards)
    ang_s = 2.0 * np.pi * np.outer(a, a) / shards
    lead_fwd = np.concatenate([np.cos(ang_s), -np.sin(ang_s)], axis=0)
    lead_inv = np.concatenate([np.cos(ang_s), -np.sin(ang_s)], axis=1)
    b = np.arange(local)
    ang_t = 2.0 * np.pi * np.outer(a, b) / length
    tw_c = np.cos(ang_t)[:, None, None, :]
    tw_s = np.sin(ang_t)[:, None, None, :]
    ang_l = 2.0 * np.pi * np.outer(b, b) / local
    cos_l, sin_l = np.cos(ang_l), np.sin(ang_l)
    lane_fwd = np.block([[cos_l, -sin_l], [sin_l, cos_l]])
    lane_inv = np.block([[cos_l, sin_l], [-sin_l, cos_l]])
    f32 = lambda v: jnp.asarray(v, dtype=jnp.float32)
    bf16 = lambda v: jnp.asarray(v, dtype=jnp.bfloat16)
    return (bf16(lead_fwd), bf16(lead_inv), f32(tw_c), f32(tw_s), bf16(lane_fwd), bf16(lane_inv))


def forward_dft(field, tables, prec):
    lead_fwd, _, tw_c, tw_s, lane_fwd, _ = tables
    shards, planes, chans, local = field.shape
    flat = field.reshape(shards, -1).astype(jnp.bfloat16)
    stage = jnp.dot(lead_fwd, flat, preferred_element_type=jnp.float32)
    stage = stage.reshape(2 * shards, planes, chans, local)
    st_r, st_i = stage[:shards], stage[shards:]
    tw_r = st_r * tw_c + st_i * tw_s
    tw_i = st_i * tw_c - st_r * tw_s
    joined = jnp.concatenate([tw_r, tw_i], axis=-1).reshape(-1, 2 * local).astype(jnp.bfloat16)
    spec = jnp.dot(joined, lane_fwd, preferred_element_type=jnp.float32)
    return spec.reshape(shards, planes, chans, 2 * local)


def inverse_dft(spec, tables, prec):
    _, lead_inv, tw_c, tw_s, _, lane_inv = tables
    shards, planes, chans, width = spec.shape
    local = width // 2
    flat = spec.reshape(-1, width).astype(jnp.bfloat16)
    back = jnp.dot(flat, lane_inv, preferred_element_type=jnp.float32)
    back = back.reshape(shards, planes, chans, width)
    bk_r, bk_i = back[..., :local], back[..., local:]
    un_r = bk_r * tw_c - bk_i * tw_s
    un_i = bk_r * tw_s + bk_i * tw_c
    stacked = jnp.concatenate([un_r, un_i], axis=0).reshape(2 * shards, -1).astype(jnp.bfloat16)
    whole = jnp.dot(lead_inv, stacked, preferred_element_type=jnp.float32)
    return whole.reshape(shards, planes, chans, local)


def cmul(a_r, a_i, b_r, b_i):
    return a_r * b_r - a_i * b_i, a_r * b_i + a_i * b_r


def convolve(received, filt_spec, tables):
    shards, _, chans, local = received.shape
    length = shards * local
    spec = forward_dft(received.astype(jnp.float32), tables, FAST)
    re, im = spec[..., :local], spec[..., local:]
    h_r, h_i = filt_spec[..., :local], filt_spec[..., local:]
    p_r, p_i = cmul(re[:, 0], im[:, 0], h_r, h_i)
    outs_r, outs_i = [p_r], [p_i]
    for j in range(3):
        one, two = (j + 1) % 3, (j + 2) % 3
        a_r, a_i = cmul(re[:, 1 + one], im[:, 1 + one], re[:, 4 + two], im[:, 4 + two])
        b_r, b_i = cmul(re[:, 1 + two], im[:, 1 + two], re[:, 4 + one], im[:, 4 + one])
        outs_r.append(a_r - b_r)
        outs_i.append(a_i - b_i)
    prod = jnp.concatenate([jnp.stack(outs_r, axis=1), jnp.stack(outs_i, axis=1)], axis=-1)
    result = inverse_dft(prod, tables, FAST)
    inv_root = 1.0 / math.sqrt(length)
    scale = jnp.array([1.0, inv_root, inv_root, inv_root], dtype=jnp.float32) / length
    return (result * scale[None, :, None, None]).astype(jnp.bfloat16)


def gelu_tanh(x):
    return 0.5 * x * (1.0 + jnp.tanh(math.sqrt(2.0 / math.pi) * (x + 0.044715 * (x * x * x))))


def token_step(post, pre, arrays, weights, shards):
    f32, bf16 = jnp.float32, jnp.bfloat16
    state_s, state_v = arrays["state_s"], arrays["state_v"]
    chans, tok = state_s.shape
    own = chans // shards
    packed = own % 16 == 0
    full = lambda shape: pl.BlockSpec(shape, lambda i, n=len(shape): (0,) * n)

    def layer_spec(w, layer):
        return pl.BlockSpec((pl.Squeezed(),) + w.shape[1:], lambda i: (layer,) + (0,) * (w.ndim - 1))

    ins, specs = [state_s, state_v], [full(state_s.shape), full(state_v.shape)]
    post_names = ("w_out_s", "w_out_v", "w_up", "w_down", "w_mix", "w_gate")
    if post is not None:
        ins += [arrays["conv"], arrays["query"]]
        specs += [full(arrays["conv"].shape), full(arrays["query"].shape)]
        for name in post_names + ("gains_t",):
            ins.append(weights[name])
            specs.append(layer_spec(weights[name], post))
    if pre is not None:
        for name in ("w_qkw_s", "w_qkw_v", "gains_t"):
            ins.append(weights[name])
            specs.append(layer_spec(weights[name], pre))
    outs = []
    if pre is not None:
        plane_shape = (shards, 7, own, tok) if packed else (7, chans, tok)
        outs += [(plane_shape, bf16), ((4, chans, tok), bf16)]
        if post is not None:
            outs += [((chans, tok), f32), ((3, chans, tok), f32)]
    else:
        outs += [((chans, tok), bf16), ((3, chans, tok), bf16)]

    def snorm(x, g):
        return x * lax.rsqrt(jnp.mean(x * x, axis=0, keepdims=True) + 1e-05) * g

    def vnorm(xs, g):
        total = sum(jnp.sum(x * x, axis=0, keepdims=True) for x in xs)
        scale = lax.rsqrt(total / (3 * chans) + 1e-05)
        return [x * scale * g for x in xs]

    def mm(w, x):
        return jnp.dot(w, x, preferred_element_type=f32)

    def kernel(*refs):
        refs = list(refs)
        ss_ref, sv_ref = refs.pop(0), refs.pop(0)
        ss = ss_ref[...].astype(f32)
        sv = [sv_ref[j].astype(f32) for j in range(3)]
        if post is not None:
            conv_ref, q_ref = refs.pop(0), refs.pop(0)
            wos, wov, wup, wdn, wmx, wgt, gp = [refs.pop(0) for _ in range(7)]
            g = gp[...].T
            qs = q_ref[0].astype(f32)
            if packed:
                planes = [jnp.concatenate([conv_ref[d, p] for d in range(shards)], axis=0) for p in range(4)]
            else:
                planes = [conv_ref[p] for p in range(4)]
            ys = planes[0].astype(f32)
            yv = [planes[1 + j].astype(f32) for j in range(3)]
            mix = q_ref[1].astype(f32) * yv[0]
            mix = mix + q_ref[2].astype(f32) * yv[1]
            mix = mix + q_ref[3].astype(f32) * yv[2]
            out_s = (qs * ys + mix).astype(bf16)
            ss = ss + mm(wos[...], out_s)
            sv = [sv[j] + mm(wov[...], (qs * yv[j]).astype(bf16)) for j in range(3)]
            mlp_s = snorm(ss, g[:, 2:3]).astype(bf16)
            mlp_v = [v.astype(bf16) for v in vnorm(sv, g[:, 3:4])]
            hidden = gelu_tanh(mm(wup[...], mlp_s)).astype(bf16)
            gate = 1.0 / (1.0 + jnp.exp(-mm(wgt[...], mlp_s)))
            ss = ss + mm(wdn[...], hidden)
            sv = [sv[j] + mm(wmx[...], mlp_v[j]) * gate for j in range(3)]
        if pre is not None:
            wqs, wqv, gq = [refs.pop(0) for _ in range(3)]
            g = gq[...].T
            planes_ref, query_ref = refs.pop(0), refs.pop(0)

            def put(p, value):
                if packed:
                    for d in range(shards):
                        planes_ref[d, p] = value[d * own : (d + 1) * own]
                else:
                    planes_ref[p] = value

            normed_s = snorm(ss, g[:, 0:1]).astype(bf16)
            normed_v = [v.astype(bf16) for v in vnorm(sv, g[:, 1:2])]
            ps = mm(wqs[...], normed_s)
            query_ref[0] = ps[:chans].astype(bf16)
            put(0, (ps[chans : 2 * chans] * ps[2 * chans :]).astype(bf16))
            for j in range(3):
                pv = mm(wqv[...], normed_v[j]).astype(bf16)
                query_ref[1 + j] = pv[:chans]
                put(1 + j, pv[chans : 2 * chans])
                put(4 + j, pv[2 * chans :])
            if post is not None:
                ns_ref, nv_ref = refs.pop(0), refs.pop(0)
                ns_ref[...] = ss
                for j in range(3):
                    nv_ref[j] = sv[j]
        else:
            os_ref, ov_ref = refs.pop(0), refs.pop(0)
            os_ref[...] = ss.astype(bf16)
            for j in range(3):
                ov_ref[j] = sv[j].astype(bf16)

    return pl.pallas_call(
        kernel,
        grid=(1,),
        in_specs=specs,
        out_specs=[full(shape) for shape, _ in outs],
        out_shape=[jax.ShapeDtypeStruct(shape, dtype) for shape, dtype in outs],
    )(*ins)


def per_device(
    scalars,
    vectors,
    w_qkw_s,
    w_qkw_v,
    w_out_s,
    w_out_v,
    w_up,
    w_down,
    w_mix,
    w_gate,
    gains,
    pe_w1,
    pe_w2,
    pe_w3,
    rates,
):
    chans = scalars.shape[0]
    tok_local = scalars.shape[1]
    shards = lax.axis_size("seq")
    rank = lax.axis_index("seq")
    length = tok_local * shards
    own = chans // shards
    depth = w_qkw_s.shape[0]
    tables = make_tables(shards, tok_local)
    positions = jnp.arange(length, dtype=jnp.int32)

    def filter_spec(first, second, third, decay):
        third = lax.dynamic_slice_in_dim(third, rank * own, own, axis=0)
        decay = lax.dynamic_slice_in_dim(decay, rank * own, own, axis=0)
        made = filter_values(positions, length, first, second, third, decay)
        made = made.reshape(own, shards, tok_local).transpose(1, 0, 2)
        return forward_dft(made[:, None].astype(jnp.float32), tables, FAST)[:, 0]

    spec_next = filter_spec(pe_w1[0], pe_w2[0], pe_w3[0], rates[0])
    weights = {
        "w_qkw_s": w_qkw_s,
        "w_qkw_v": w_qkw_v,
        "w_out_s": w_out_s,
        "w_out_v": w_out_v,
        "w_up": w_up,
        "w_down": w_down,
        "w_mix": w_mix,
        "w_gate": w_gate,
        "gains_t": gains,
    }
    arrays = {"state_s": scalars, "state_v": vectors}
    packed = own % 16 == 0
    planes, query = token_step(None, 0, arrays, weights, shards)
    for layer in range(depth):
        outgoing = planes
        if not packed:
            outgoing = planes.reshape(7, shards, own, tok_local).transpose(1, 0, 2, 3)
        regrouped = lax.all_to_all(outgoing, "seq", 0, 0, tiled=True)
        convolved = convolve(regrouped, spec_next, tables)
        if layer + 1 < depth:
            tied = lax.optimization_barrier(
                (pe_w1[layer + 1], pe_w2[layer + 1], pe_w3[layer + 1], rates[layer + 1], convolved)
            )
            spec_next = filter_spec(*tied[:4])
        returned = lax.all_to_all(convolved, "seq", 0, 0, tiled=True)
        arrays["conv"] = returned
        if not packed:
            arrays["conv"] = returned.transpose(1, 0, 2, 3).reshape(4, chans, tok_local)
        arrays["query"] = query
        if layer + 1 < depth:
            planes, query, new_s, new_v = token_step(layer, layer + 1, arrays, weights, shards)
            arrays["state_s"], arrays["state_v"] = new_s, new_v
        else:
            return tuple(token_step(layer, None, arrays, weights, shards))


def solution(mesh):
    in_specs = (
        P(None, ("grp", "seq")),
        P(None, None, ("grp", "seq")),
        P(),
        P(),
        P(),
        P(),
        P(),
        P(),
        P(),
        P(),
        P(),
        P(),
        P(),
        P(),
        P(),
    )
    out_specs = (P(None, ("grp", "seq")), P(None, None, ("grp", "seq")))
    return jax.shard_map(
        per_device, mesh=mesh, in_specs=in_specs, out_specs=out_specs, check_vma=False
    )
```

```python
import math

import jax
import jax.numpy as jnp
import numpy as np
from jax import lax
from jax.experimental import pallas as pl
from jax.sharding import PartitionSpec as P

HIGH = lax.Precision.HIGHEST
FAST = lax.Precision.DEFAULT


def filter_values(positions, length, first, second, third, decay):
    count = first.shape[1] // 2
    freqs = jnp.arange(1, count + 1, dtype=jnp.int32)
    turns = freqs[:, None] * positions[None, :] % length
    angle = turns.astype(jnp.float32) * (2.0 * math.pi / length)
    feats = jnp.concatenate([jnp.cos(angle), jnp.sin(angle)], axis=0)
    hid_one = jnp.sin(jnp.dot(first, feats, precision=HIGH))
    hid_two = jnp.sin(jnp.dot(second, hid_one, precision=HIGH))
    raw = jnp.dot(third, hid_two, precision=HIGH)
    envelope = jnp.exp(-decay[:, None] * positions[None, :].astype(jnp.float32) / length)
    return (raw * envelope / math.sqrt(length)).astype(jnp.bfloat16)


def scalar_norm(field, gain):
    return field * lax.rsqrt(jnp.mean(field * field, axis=0, keepdims=True) + 1e-05) * gain[:, None]


def vector_norm(field, gain):
    return (
        field
        * lax.rsqrt(jnp.mean(field * field, axis=(0, 1), keepdims=True) + 1e-05)
        * gain[None, :, None]
    )


def make_tables(shards, local):
    length = shards * local
    f32, bf16 = jnp.float32, jnp.bfloat16

    def turns(rows, cols, period):
        rows = jnp.arange(rows, dtype=jnp.int32)[:, None]
        cols = jnp.arange(cols, dtype=jnp.int32)[None, :]
        return ((rows * cols) % period).astype(f32) * (2.0 * math.pi / period)

    ang_s = turns(shards, shards, shards)
    cos_s, sin_s = jnp.cos(ang_s), jnp.sin(ang_s)
    lead_fwd = jnp.concatenate([cos_s, -sin_s], axis=0)
    lead_inv = jnp.concatenate([cos_s, -sin_s], axis=1)
    ang_t = turns(shards, local, length)
    tw_c = jnp.cos(ang_t)[:, None, None, :]
    tw_s = jnp.sin(ang_t)[:, None, None, :]
    ang_l = turns(local, local, local)
    cos_l, sin_l = jnp.cos(ang_l), jnp.sin(ang_l)
    lane_fwd = jnp.block([[cos_l, -sin_l], [sin_l, cos_l]])
    lane_inv = jnp.block([[cos_l, sin_l], [-sin_l, cos_l]])
    return (
        lead_fwd.astype(bf16),
        lead_inv.astype(bf16),
        tw_c,
        tw_s,
        lane_fwd.astype(bf16),
        lane_inv.astype(bf16),
    )


def forward_dft(field, tables, prec):
    lead_fwd, _, tw_c, tw_s, lane_fwd, _ = tables
    shards, planes, chans, local = field.shape
    flat = field.reshape(shards, -1).astype(jnp.bfloat16)
    stage = jnp.dot(lead_fwd, flat, preferred_element_type=jnp.float32)
    stage = stage.reshape(2 * shards, planes, chans, local)
    st_r, st_i = stage[:shards], stage[shards:]
    tw_r = st_r * tw_c + st_i * tw_s
    tw_i = st_i * tw_c - st_r * tw_s
    joined = jnp.concatenate([tw_r, tw_i], axis=-1).reshape(-1, 2 * local).astype(jnp.bfloat16)
    spec = jnp.dot(joined, lane_fwd, preferred_element_type=jnp.float32)
    return spec.reshape(shards, planes, chans, 2 * local)


def inverse_dft(spec, tables, prec):
    _, lead_inv, tw_c, tw_s, _, lane_inv = tables
    shards, planes, chans, width = spec.shape
    local = width // 2
    flat = spec.reshape(-1, width).astype(jnp.bfloat16)
    back = jnp.dot(flat, lane_inv, preferred_element_type=jnp.float32)
    back = back.reshape(shards, planes, chans, width)
    bk_r, bk_i = back[..., :local], back[..., local:]
    un_r = bk_r * tw_c - bk_i * tw_s
    un_i = bk_r * tw_s + bk_i * tw_c
    stacked = jnp.concatenate([un_r, un_i], axis=0).reshape(2 * shards, -1).astype(jnp.bfloat16)
    whole = jnp.dot(lead_inv, stacked, preferred_element_type=jnp.float32)
    return whole.reshape(shards, planes, chans, local)


def cmul(a_r, a_i, b_r, b_i):
    return a_r * b_r - a_i * b_i, a_r * b_i + a_i * b_r


def convolve(received, filt_spec, tables):
    shards, _, chans, local = received.shape
    length = shards * local
    spec = forward_dft(received.astype(jnp.float32), tables, FAST)
    re, im = spec[..., :local], spec[..., local:]
    h_r, h_i = filt_spec[..., :local], filt_spec[..., local:]
    p_r, p_i = cmul(re[:, 0], im[:, 0], h_r, h_i)
    outs_r, outs_i = [p_r], [p_i]
    for j in range(3):
        one, two = (j + 1) % 3, (j + 2) % 3
        a_r, a_i = cmul(re[:, 1 + one], im[:, 1 + one], re[:, 4 + two], im[:, 4 + two])
        b_r, b_i = cmul(re[:, 1 + two], im[:, 1 + two], re[:, 4 + one], im[:, 4 + one])
        outs_r.append(a_r - b_r)
        outs_i.append(a_i - b_i)
    prod = jnp.concatenate([jnp.stack(outs_r, axis=1), jnp.stack(outs_i, axis=1)], axis=-1)
    result = inverse_dft(prod, tables, FAST)
    inv_root = 1.0 / math.sqrt(length)
    scale = jnp.array([1.0, inv_root, inv_root, inv_root], dtype=jnp.float32) / length
    return (result * scale[None, :, None, None]).astype(jnp.bfloat16)


def gelu_tanh(x):
    return 0.5 * x * (1.0 + jnp.tanh(math.sqrt(2.0 / math.pi) * (x + 0.044715 * (x * x * x))))


def token_step(post, pre, arrays, weights, shards):
    f32, bf16 = jnp.float32, jnp.bfloat16
    state_s, state_v = arrays["state_s"], arrays["state_v"]
    chans, tok = state_s.shape
    own = chans // shards
    packed = own % 16 == 0
    full = lambda shape: pl.BlockSpec(shape, lambda i, n=len(shape): (0,) * n)

    def layer_spec(w, layer):
        return pl.BlockSpec((pl.Squeezed(),) + w.shape[1:], lambda i: (layer,) + (0,) * (w.ndim - 1))

    ins, specs = [state_s, state_v], [full(state_s.shape), full(state_v.shape)]
    post_names = ("w_out_s", "w_out_v", "w_up", "w_down", "w_mix", "w_gate")
    if post is not None:
        ins += [arrays["conv"], arrays["query"]]
        specs += [full(arrays["conv"].shape), full(arrays["query"].shape)]
        for name in post_names + ("gains_t",):
            ins.append(weights[name])
            specs.append(layer_spec(weights[name], post))
    if pre is not None:
        for name in ("w_qkw_s", "w_qkw_v", "gains_t"):
            ins.append(weights[name])
            specs.append(layer_spec(weights[name], pre))
    outs = []
    if pre is not None:
        plane_shape = (shards, 7, own, tok) if packed else (7, chans, tok)
        outs += [(plane_shape, bf16), ((4, chans, tok), bf16)]
        if post is not None:
            outs += [((chans, tok), f32), ((3, chans, tok), f32)]
    else:
        outs += [((chans, tok), bf16), ((3, chans, tok), bf16)]

    def snorm(x, g):
        return x * lax.rsqrt(jnp.mean(x * x, axis=0, keepdims=True) + 1e-05) * g

    def vnorm(xs, g):
        total = sum(jnp.sum(x * x, axis=0, keepdims=True) for x in xs)
        scale = lax.rsqrt(total / (3 * chans) + 1e-05)
        return [x * scale * g for x in xs]

    def mm(w, x):
        return jnp.dot(w, x, preferred_element_type=f32)

    def kernel(*refs):
        refs = list(refs)
        ss_ref, sv_ref = refs.pop(0), refs.pop(0)
        ss = ss_ref[...].astype(f32)
        sv = [sv_ref[j].astype(f32) for j in range(3)]
        if post is not None:
            conv_ref, q_ref = refs.pop(0), refs.pop(0)
            wos, wov, wup, wdn, wmx, wgt, gp = [refs.pop(0) for _ in range(7)]
            g = gp[...].T
            qs = q_ref[0].astype(f32)
            if packed:
                planes = [jnp.concatenate([conv_ref[d, p] for d in range(shards)], axis=0) for p in range(4)]
            else:
                planes = [conv_ref[p] for p in range(4)]
            ys = planes[0].astype(f32)
            yv = [planes[1 + j].astype(f32) for j in range(3)]
            mix = q_ref[1].astype(f32) * yv[0]
            mix = mix + q_ref[2].astype(f32) * yv[1]
            mix = mix + q_ref[3].astype(f32) * yv[2]
            out_s = (qs * ys + mix).astype(bf16)
            ss = ss + mm(wos[...], out_s)
            sv = [sv[j] + mm(wov[...], (qs * yv[j]).astype(bf16)) for j in range(3)]
            mlp_s = snorm(ss, g[:, 2:3]).astype(bf16)
            mlp_v = [v.astype(bf16) for v in vnorm(sv, g[:, 3:4])]
            hidden = gelu_tanh(mm(wup[...], mlp_s)).astype(bf16)
            gate = 1.0 / (1.0 + jnp.exp(-mm(wgt[...], mlp_s)))
            ss = ss + mm(wdn[...], hidden)
            sv = [sv[j] + mm(wmx[...], mlp_v[j]) * gate for j in range(3)]
        if pre is not None:
            wqs, wqv, gq = [refs.pop(0) for _ in range(3)]
            g = gq[...].T
            planes_ref, query_ref = refs.pop(0), refs.pop(0)

            def put(p, value):
                if packed:
                    for d in range(shards):
                        planes_ref[d, p] = value[d * own : (d + 1) * own]
                else:
                    planes_ref[p] = value

            normed_s = snorm(ss, g[:, 0:1]).astype(bf16)
            normed_v = [v.astype(bf16) for v in vnorm(sv, g[:, 1:2])]
            ps = mm(wqs[...], normed_s)
            query_ref[0] = ps[:chans].astype(bf16)
            put(0, (ps[chans : 2 * chans] * ps[2 * chans :]).astype(bf16))
            for j in range(3):
                pv = mm(wqv[...], normed_v[j]).astype(bf16)
                query_ref[1 + j] = pv[:chans]
                put(1 + j, pv[chans : 2 * chans])
                put(4 + j, pv[2 * chans :])
            if post is not None:
                ns_ref, nv_ref = refs.pop(0), refs.pop(0)
                ns_ref[...] = ss
                for j in range(3):
                    nv_ref[j] = sv[j]
        else:
            os_ref, ov_ref = refs.pop(0), refs.pop(0)
            os_ref[...] = ss.astype(bf16)
            for j in range(3):
                ov_ref[j] = sv[j].astype(bf16)

    return pl.pallas_call(
        kernel,
        grid=(1,),
        in_specs=specs,
        out_specs=[full(shape) for shape, _ in outs],
        out_shape=[jax.ShapeDtypeStruct(shape, dtype) for shape, dtype in outs],
    )(*ins)


def per_device(
    scalars,
    vectors,
    w_qkw_s,
    w_qkw_v,
    w_out_s,
    w_out_v,
    w_up,
    w_down,
    w_mix,
    w_gate,
    gains,
    pe_w1,
    pe_w2,
    pe_w3,
    rates,
):
    chans = scalars.shape[0]
    tok_local = scalars.shape[1]
    shards = lax.axis_size("seq")
    rank = lax.axis_index("seq")
    length = tok_local * shards
    own = chans // shards
    depth = w_qkw_s.shape[0]
    tables = make_tables(shards, tok_local)
    positions = jnp.arange(length, dtype=jnp.int32)

    def filter_spec(first, second, third, decay):
        third = lax.dynamic_slice_in_dim(third, rank * own, own, axis=0)
        decay = lax.dynamic_slice_in_dim(decay, rank * own, own, axis=0)
        made = filter_values(positions, length, first, second, third, decay)
        made = made.reshape(own, shards, tok_local).transpose(1, 0, 2)
        return forward_dft(made[:, None].astype(jnp.float32), tables, FAST)[:, 0]

    spec_next = filter_spec(pe_w1[0], pe_w2[0], pe_w3[0], rates[0])
    weights = {
        "w_qkw_s": w_qkw_s,
        "w_qkw_v": w_qkw_v,
        "w_out_s": w_out_s,
        "w_out_v": w_out_v,
        "w_up": w_up,
        "w_down": w_down,
        "w_mix": w_mix,
        "w_gate": w_gate,
        "gains_t": gains,
    }
    arrays = {"state_s": scalars, "state_v": vectors}
    packed = own % 16 == 0
    planes, query = token_step(None, 0, arrays, weights, shards)
    for layer in range(depth):
        outgoing = planes
        if not packed:
            outgoing = planes.reshape(7, shards, own, tok_local).transpose(1, 0, 2, 3)
        regrouped = lax.all_to_all(outgoing, "seq", 0, 0, tiled=True)
        convolved = convolve(regrouped, spec_next, tables)
        if layer + 1 < depth:
            tied = lax.optimization_barrier(
                (pe_w1[layer + 1], pe_w2[layer + 1], pe_w3[layer + 1], rates[layer + 1], convolved)
            )
            spec_next = filter_spec(*tied[:4])
        returned = lax.all_to_all(convolved, "seq", 0, 0, tiled=True)
        arrays["conv"] = returned
        if not packed:
            arrays["conv"] = returned.transpose(1, 0, 2, 3).reshape(4, chans, tok_local)
        arrays["query"] = query
        if layer + 1 < depth:
            planes, query, new_s, new_v = token_step(layer, layer + 1, arrays, weights, shards)
            arrays["state_s"], arrays["state_v"] = new_s, new_v
        else:
            return tuple(token_step(layer, None, arrays, weights, shards))


def solution(mesh):
    in_specs = (
        P(None, ("grp", "seq")),
        P(None, None, ("grp", "seq")),
        P(),
        P(),
        P(),
        P(),
        P(),
        P(),
        P(),
        P(),
        P(),
        P(),
        P(),
        P(),
        P(),
    )
    out_specs = (P(None, ("grp", "seq")), P(None, None, ("grp", "seq")))
    return jax.shard_map(
        per_device, mesh=mesh, in_specs=in_specs, out_specs=out_specs, check_vma=False
    )
```

```python
import math

import jax
import jax.numpy as jnp
import numpy as np
from jax import lax
from jax.experimental import pallas as pl
from jax.experimental.pallas import tpu as pltpu
from jax.sharding import PartitionSpec as P

HIGH = lax.Precision.HIGHEST
FAST = lax.Precision.DEFAULT


def filter_values(positions, length, first, second, third, decay):
    count = first.shape[1] // 2
    freqs = jnp.arange(1, count + 1, dtype=jnp.int32)
    turns = freqs[:, None] * positions[None, :] % length
    angle = turns.astype(jnp.float32) * (2.0 * math.pi / length)
    feats = jnp.concatenate([jnp.cos(angle), jnp.sin(angle)], axis=0)
    hid_one = jnp.sin(jnp.dot(first, feats, precision=HIGH))
    hid_two = jnp.sin(jnp.dot(second, hid_one, precision=HIGH))
    raw = jnp.dot(third, hid_two, precision=HIGH)
    envelope = jnp.exp(-decay[:, None] * positions[None, :].astype(jnp.float32) / length)
    return (raw * envelope / math.sqrt(length)).astype(jnp.bfloat16)


def scalar_norm(field, gain):
    return field * lax.rsqrt(jnp.mean(field * field, axis=0, keepdims=True) + 1e-05) * gain[:, None]


def vector_norm(field, gain):
    return (
        field
        * lax.rsqrt(jnp.mean(field * field, axis=(0, 1), keepdims=True) + 1e-05)
        * gain[None, :, None]
    )


def make_tables(shards, local):
    length = shards * local
    f32, bf16 = jnp.float32, jnp.bfloat16

    def turns(rows, cols, period):
        rows = jnp.arange(rows, dtype=jnp.int32)[:, None]
        cols = jnp.arange(cols, dtype=jnp.int32)[None, :]
        return ((rows * cols) % period).astype(f32) * (2.0 * math.pi / period)

    ang_s = turns(shards, shards, shards)
    cos_s, sin_s = jnp.cos(ang_s), jnp.sin(ang_s)
    lead_fwd = jnp.concatenate([cos_s, -sin_s], axis=0)
    lead_inv = jnp.concatenate([cos_s, -sin_s], axis=1)
    ang_t = turns(shards, local, length)
    tw_c = jnp.cos(ang_t)[:, None, None, :]
    tw_s = jnp.sin(ang_t)[:, None, None, :]
    ang_l = turns(local, local, local)
    cos_l, sin_l = jnp.cos(ang_l), jnp.sin(ang_l)
    lane_fwd = jnp.block([[cos_l, -sin_l], [sin_l, cos_l]])
    lane_inv = jnp.block([[cos_l, sin_l], [-sin_l, cos_l]])
    return (
        lead_fwd.astype(bf16),
        lead_inv.astype(bf16),
        tw_c,
        tw_s,
        lane_fwd.astype(bf16),
        lane_inv.astype(bf16),
    )


def forward_dft(field, tables, prec):
    lead_fwd, _, tw_c, tw_s, lane_fwd, _ = tables
    shards, planes, chans, local = field.shape
    flat = field.reshape(shards, -1).astype(jnp.bfloat16)
    stage = jnp.dot(lead_fwd, flat, preferred_element_type=jnp.float32)
    stage = stage.reshape(2 * shards, planes, chans, local)
    st_r, st_i = stage[:shards], stage[shards:]
    tw_r = st_r * tw_c + st_i * tw_s
    tw_i = st_i * tw_c - st_r * tw_s
    joined = jnp.concatenate([tw_r, tw_i], axis=-1).reshape(-1, 2 * local).astype(jnp.bfloat16)
    spec = jnp.dot(joined, lane_fwd, preferred_element_type=jnp.float32)
    return spec.reshape(shards, planes, chans, 2 * local)


def inverse_dft(spec, tables, prec):
    _, lead_inv, tw_c, tw_s, _, lane_inv = tables
    shards, planes, chans, width = spec.shape
    local = width // 2
    flat = spec.reshape(-1, width).astype(jnp.bfloat16)
    back = jnp.dot(flat, lane_inv, preferred_element_type=jnp.float32)
    back = back.reshape(shards, planes, chans, width)
    bk_r, bk_i = back[..., :local], back[..., local:]
    un_r = bk_r * tw_c - bk_i * tw_s
    un_i = bk_r * tw_s + bk_i * tw_c
    stacked = jnp.concatenate([un_r, un_i], axis=0).reshape(2 * shards, -1).astype(jnp.bfloat16)
    whole = jnp.dot(lead_inv, stacked, preferred_element_type=jnp.float32)
    return whole.reshape(shards, planes, chans, local)


def cmul(a_r, a_i, b_r, b_i):
    return a_r * b_r - a_i * b_i, a_r * b_i + a_i * b_r


def convolve(received, filt_spec, tables):
    shards, _, chans, local = received.shape
    length = shards * local
    spec = forward_dft(received.astype(jnp.float32), tables, FAST)
    re, im = spec[..., :local], spec[..., local:]
    h_r, h_i = filt_spec[..., :local], filt_spec[..., local:]
    p_r, p_i = cmul(re[:, 0], im[:, 0], h_r, h_i)
    outs_r, outs_i = [p_r], [p_i]
    for j in range(3):
        one, two = (j + 1) % 3, (j + 2) % 3
        a_r, a_i = cmul(re[:, 1 + one], im[:, 1 + one], re[:, 4 + two], im[:, 4 + two])
        b_r, b_i = cmul(re[:, 1 + two], im[:, 1 + two], re[:, 4 + one], im[:, 4 + one])
        outs_r.append(a_r - b_r)
        outs_i.append(a_i - b_i)
    prod = jnp.concatenate([jnp.stack(outs_r, axis=1), jnp.stack(outs_i, axis=1)], axis=-1)
    result = inverse_dft(prod, tables, FAST)
    inv_root = 1.0 / math.sqrt(length)
    scale = jnp.array([1.0, inv_root, inv_root, inv_root], dtype=jnp.float32) / length
    return (result * scale[None, :, None, None]).astype(jnp.bfloat16)


def gelu_tanh(x):
    return 0.5 * x * (1.0 + jnp.tanh(math.sqrt(2.0 / math.pi) * (x + 0.044715 * (x * x * x))))


def token_step(post, pre, arrays, weights, shards):
    f32, bf16 = jnp.float32, jnp.bfloat16
    state_s, state_v = arrays["state_s"], arrays["state_v"]
    chans, tok = state_s.shape
    own = chans // shards
    packed = own % 16 == 0
    full = lambda shape: pl.BlockSpec(shape, lambda i, n=len(shape): (0,) * n)

    def layer_spec(w, layer):
        return pl.BlockSpec((pl.Squeezed(),) + w.shape[1:], lambda i: (layer,) + (0,) * (w.ndim - 1))

    ins, specs = [state_s, state_v], [full(state_s.shape), full(state_v.shape)]
    late_names = ("w_up", "w_down", "w_mix", "w_gate")
    scratch = []
    if post is not None:
        ins += [arrays["conv"], arrays["query"]]
        specs += [full(arrays["conv"].shape), full(arrays["query"].shape)]
        for name in ("w_out_s", "w_out_v", "gains_t"):
            ins.append(weights[name])
            specs.append(layer_spec(weights[name], post))
        for name in late_names:
            ins.append(weights[name])
            specs.append(pl.BlockSpec(memory_space=pl.ANY))
            scratch.append(pltpu.VMEM(weights[name].shape[1:], weights[name].dtype))
        scratch.append(pltpu.SemaphoreType.DMA((len(late_names),)))
    if pre is not None:
        for name in ("w_qkw_s", "w_qkw_v", "gains_t"):
            ins.append(weights[name])
            specs.append(layer_spec(weights[name], pre))
    outs = []
    if pre is not None:
        plane_shape = (shards, 7, own, tok) if packed else (7, chans, tok)
        outs += [(plane_shape, bf16), ((4, chans, tok), bf16)]
        if post is not None:
            outs += [((chans, tok), f32), ((3, chans, tok), f32)]
    else:
        outs += [((chans, tok), bf16), ((3, chans, tok), bf16)]

    def snorm(x, g):
        return x * lax.rsqrt(jnp.mean(x * x, axis=0, keepdims=True) + 1e-05) * g

    def vnorm(xs, g):
        total = sum(jnp.sum(x * x, axis=0, keepdims=True) for x in xs)
        scale = lax.rsqrt(total / (3 * chans) + 1e-05)
        return [x * scale * g for x in xs]

    def mm(w, x):
        return jnp.dot(w, x, preferred_element_type=f32)

    def kernel(*refs):
        refs = list(refs)
        if post is not None:
            sems = refs.pop()
            bufs = [refs.pop() for _ in late_names][::-1]
        ss_ref, sv_ref = refs.pop(0), refs.pop(0)
        ss = ss_ref[...].astype(f32)
        sv = [sv_ref[j].astype(f32) for j in range(3)]
        if post is not None:
            conv_ref, q_ref = refs.pop(0), refs.pop(0)
            wos, wov, gp = [refs.pop(0) for _ in range(3)]
            copies = []
            for slot in range(len(late_names)):
                src_ref = refs.pop(0)
                copies.append(pltpu.make_async_copy(src_ref.at[post], bufs[slot], sems.at[slot]))
                copies[-1].start()
            g = gp[...].T
            qs = q_ref[0].astype(f32)
            if packed:
                planes = [jnp.concatenate([conv_ref[d, p] for d in range(shards)], axis=0) for p in range(4)]
            else:
                planes = [conv_ref[p] for p in range(4)]
            ys = planes[0].astype(f32)
            yv = [planes[1 + j].astype(f32) for j in range(3)]
            mix = q_ref[1].astype(f32) * yv[0]
            mix = mix + q_ref[2].astype(f32) * yv[1]
            mix = mix + q_ref[3].astype(f32) * yv[2]
            out_s = (qs * ys + mix).astype(bf16)
            ss = ss + mm(wos[...], out_s)
            sv = [sv[j] + mm(wov[...], (qs * yv[j]).astype(bf16)) for j in range(3)]
            mlp_s = snorm(ss, g[:, 2:3]).astype(bf16)
            mlp_v = [v.astype(bf16) for v in vnorm(sv, g[:, 3:4])]
            wup, wdn, wmx, wgt = bufs
            copies[0].wait()
            hidden = gelu_tanh(mm(wup[...], mlp_s)).astype(bf16)
            copies[3].wait()
            gate = 1.0 / (1.0 + jnp.exp(-mm(wgt[...], mlp_s)))
            copies[1].wait()
            ss = ss + mm(wdn[...], hidden)
            copies[2].wait()
            sv = [sv[j] + mm(wmx[...], mlp_v[j]) * gate for j in range(3)]
        if pre is not None:
            wqs, wqv, gq = [refs.pop(0) for _ in range(3)]
            g = gq[...].T
            planes_ref, query_ref = refs.pop(0), refs.pop(0)

            def put(p, value):
                if packed:
                    for d in range(shards):
                        planes_ref[d, p] = value[d * own : (d + 1) * own]
                else:
                    planes_ref[p] = value

            normed_s = snorm(ss, g[:, 0:1]).astype(bf16)
            normed_v = [v.astype(bf16) for v in vnorm(sv, g[:, 1:2])]
            ps = mm(wqs[...], normed_s)
            query_ref[0] = ps[:chans].astype(bf16)
            put(0, (ps[chans : 2 * chans] * ps[2 * chans :]).astype(bf16))
            for j in range(3):
                pv = mm(wqv[...], normed_v[j]).astype(bf16)
                query_ref[1 + j] = pv[:chans]
                put(1 + j, pv[chans : 2 * chans])
                put(4 + j, pv[2 * chans :])
            if post is not None:
                ns_ref, nv_ref = refs.pop(0), refs.pop(0)
                ns_ref[...] = ss
                for j in range(3):
                    nv_ref[j] = sv[j]
        else:
            os_ref, ov_ref = refs.pop(0), refs.pop(0)
            os_ref[...] = ss.astype(bf16)
            for j in range(3):
                ov_ref[j] = sv[j].astype(bf16)

    return pl.pallas_call(
        kernel,
        grid=(1,),
        in_specs=specs,
        out_specs=[full(shape) for shape, _ in outs],
        out_shape=[jax.ShapeDtypeStruct(shape, dtype) for shape, dtype in outs],
        scratch_shapes=scratch,
    )(*ins)


def per_device(
    scalars,
    vectors,
    w_qkw_s,
    w_qkw_v,
    w_out_s,
    w_out_v,
    w_up,
    w_down,
    w_mix,
    w_gate,
    gains,
    pe_w1,
    pe_w2,
    pe_w3,
    rates,
):
    chans = scalars.shape[0]
    tok_local = scalars.shape[1]
    shards = lax.axis_size("seq")
    rank = lax.axis_index("seq")
    length = tok_local * shards
    own = chans // shards
    depth = w_qkw_s.shape[0]
    tables = make_tables(shards, tok_local)
    positions = jnp.arange(length, dtype=jnp.int32)

    def filter_spec(first, second, third, decay):
        third = lax.dynamic_slice_in_dim(third, rank * own, own, axis=0)
        decay = lax.dynamic_slice_in_dim(decay, rank * own, own, axis=0)
        made = filter_values(positions, length, first, second, third, decay)
        made = made.reshape(own, shards, tok_local).transpose(1, 0, 2)
        return forward_dft(made[:, None].astype(jnp.float32), tables, FAST)[:, 0]

    spec_next = filter_spec(pe_w1[0], pe_w2[0], pe_w3[0], rates[0])
    weights = {
        "w_qkw_s": w_qkw_s,
        "w_qkw_v": w_qkw_v,
        "w_out_s": w_out_s,
        "w_out_v": w_out_v,
        "w_up": w_up,
        "w_down": w_down,
        "w_mix": w_mix,
        "w_gate": w_gate,
        "gains_t": gains,
    }
    arrays = {"state_s": scalars, "state_v": vectors}
    packed = own % 16 == 0
    planes, query = token_step(None, 0, arrays, weights, shards)
    for layer in range(depth):
        outgoing = planes
        if not packed:
            outgoing = planes.reshape(7, shards, own, tok_local).transpose(1, 0, 2, 3)
        regrouped = lax.all_to_all(outgoing, "seq", 0, 0, tiled=True)
        convolved = convolve(regrouped, spec_next, tables)
        if layer + 1 < depth:
            tied = lax.optimization_barrier(
                (pe_w1[layer + 1], pe_w2[layer + 1], pe_w3[layer + 1], rates[layer + 1], convolved)
            )
            spec_next = filter_spec(*tied[:4])
        returned = lax.all_to_all(convolved, "seq", 0, 0, tiled=True)
        arrays["conv"] = returned
        if not packed:
            arrays["conv"] = returned.transpose(1, 0, 2, 3).reshape(4, chans, tok_local)
        arrays["query"] = query
        if layer + 1 < depth:
            planes, query, new_s, new_v = token_step(layer, layer + 1, arrays, weights, shards)
            arrays["state_s"], arrays["state_v"] = new_s, new_v
        else:
            return tuple(token_step(layer, None, arrays, weights, shards))


def solution(mesh):
    in_specs = (
        P(None, ("grp", "seq")),
        P(None, None, ("grp", "seq")),
        P(),
        P(),
        P(),
        P(),
        P(),
        P(),
        P(),
        P(),
        P(),
        P(),
        P(),
        P(),
        P(),
    )
    out_specs = (P(None, ("grp", "seq")), P(None, None, ("grp", "seq")))
    return jax.shard_map(
        per_device, mesh=mesh, in_specs=in_specs, out_specs=out_specs, check_vma=False
    )
```

```python
import math

import jax
import jax.numpy as jnp
import numpy as np
from jax import lax
from jax.experimental import pallas as pl
from jax.sharding import PartitionSpec as P

HIGH = lax.Precision.HIGHEST
FAST = lax.Precision.DEFAULT


def filter_values(positions, length, first, second, third, decay):
    count = first.shape[1] // 2
    freqs = jnp.arange(1, count + 1, dtype=jnp.int32)
    turns = freqs[:, None] * positions[None, :] % length
    angle = turns.astype(jnp.float32) * (2.0 * math.pi / length)
    feats = jnp.concatenate([jnp.cos(angle), jnp.sin(angle)], axis=0)
    hid_one = jnp.sin(jnp.dot(first, feats, precision=HIGH))
    hid_two = jnp.sin(jnp.dot(second, hid_one, precision=HIGH))
    raw = jnp.dot(third, hid_two, precision=HIGH)
    envelope = jnp.exp(-decay[:, None] * positions[None, :].astype(jnp.float32) / length)
    return (raw * envelope / math.sqrt(length)).astype(jnp.bfloat16)


def scalar_norm(field, gain):
    return field * lax.rsqrt(jnp.mean(field * field, axis=0, keepdims=True) + 1e-05) * gain[:, None]


def vector_norm(field, gain):
    return (
        field
        * lax.rsqrt(jnp.mean(field * field, axis=(0, 1), keepdims=True) + 1e-05)
        * gain[None, :, None]
    )


def make_tables(shards, local):
    length = shards * local
    f32, bf16 = jnp.float32, jnp.bfloat16

    def turns(rows, cols, period):
        rows = jnp.arange(rows, dtype=jnp.int32)[:, None]
        cols = jnp.arange(cols, dtype=jnp.int32)[None, :]
        return ((rows * cols) % period).astype(f32) * (2.0 * math.pi / period)

    ang_s = turns(shards, shards, shards)
    cos_s, sin_s = jnp.cos(ang_s), jnp.sin(ang_s)
    lead_fwd = jnp.concatenate([cos_s, -sin_s], axis=0)
    lead_inv = jnp.concatenate([cos_s, -sin_s], axis=1)
    ang_t = turns(shards, local, length)
    tw_c = jnp.cos(ang_t)[:, None, None, :]
    tw_s = jnp.sin(ang_t)[:, None, None, :]
    ang_l = turns(local, local, local)
    cos_l, sin_l = jnp.cos(ang_l), jnp.sin(ang_l)
    lane_fwd = jnp.block([[cos_l, -sin_l], [sin_l, cos_l]])
    lane_inv = jnp.block([[cos_l, sin_l], [-sin_l, cos_l]])
    return (
        lead_fwd.astype(bf16),
        lead_inv.astype(bf16),
        tw_c,
        tw_s,
        lane_fwd.astype(bf16),
        lane_inv.astype(bf16),
    )


def forward_dft(field, tables, prec):
    lead_fwd, _, tw_c, tw_s, lane_fwd, _ = tables
    shards, planes, chans, local = field.shape
    flat = field.reshape(shards, -1).astype(jnp.bfloat16)
    stage = jnp.dot(lead_fwd, flat, preferred_element_type=jnp.float32)
    stage = stage.reshape(2 * shards, planes, chans, local)
    st_r, st_i = stage[:shards], stage[shards:]
    tw_r = st_r * tw_c + st_i * tw_s
    tw_i = st_i * tw_c - st_r * tw_s
    joined = jnp.concatenate([tw_r, tw_i], axis=-1).reshape(-1, 2 * local).astype(jnp.bfloat16)
    spec = jnp.dot(joined, lane_fwd, preferred_element_type=jnp.float32)
    return spec.reshape(shards, planes, chans, 2 * local)


def inverse_dft(spec, tables, prec):
    _, lead_inv, tw_c, tw_s, _, lane_inv = tables
    shards, planes, chans, width = spec.shape
    local = width // 2
    flat = spec.reshape(-1, width).astype(jnp.bfloat16)
    back = jnp.dot(flat, lane_inv, preferred_element_type=jnp.float32)
    back = back.reshape(shards, planes, chans, width)
    bk_r, bk_i = back[..., :local], back[..., local:]
    un_r = bk_r * tw_c - bk_i * tw_s
    un_i = bk_r * tw_s + bk_i * tw_c
    stacked = jnp.concatenate([un_r, un_i], axis=0).reshape(2 * shards, -1).astype(jnp.bfloat16)
    whole = jnp.dot(lead_inv, stacked, preferred_element_type=jnp.float32)
    return whole.reshape(shards, planes, chans, local)


def cmul(a_r, a_i, b_r, b_i):
    return a_r * b_r - a_i * b_i, a_r * b_i + a_i * b_r


def convolve(received, filt_spec, tables):
    shards, _, chans, local = received.shape
    length = shards * local
    spec = forward_dft(received.astype(jnp.float32), tables, FAST)
    re, im = spec[..., :local], spec[..., local:]
    h_r, h_i = filt_spec[..., :local], filt_spec[..., local:]
    p_r, p_i = cmul(re[:, 0], im[:, 0], h_r, h_i)
    outs_r, outs_i = [p_r], [p_i]
    for j in range(3):
        one, two = (j + 1) % 3, (j + 2) % 3
        a_r, a_i = cmul(re[:, 1 + one], im[:, 1 + one], re[:, 4 + two], im[:, 4 + two])
        b_r, b_i = cmul(re[:, 1 + two], im[:, 1 + two], re[:, 4 + one], im[:, 4 + one])
        outs_r.append(a_r - b_r)
        outs_i.append(a_i - b_i)
    prod = jnp.concatenate([jnp.stack(outs_r, axis=1), jnp.stack(outs_i, axis=1)], axis=-1)
    result = inverse_dft(prod, tables, FAST)
    inv_root = 1.0 / math.sqrt(length)
    scale = jnp.array([1.0, inv_root, inv_root, inv_root], dtype=jnp.float32) / length
    return (result * scale[None, :, None, None]).astype(jnp.bfloat16)


def gelu_tanh(x):
    return 0.5 * x * (1.0 + jnp.tanh(math.sqrt(2.0 / math.pi) * (x + 0.044715 * (x * x * x))))


def token_step(post, pre, arrays, weights, shards):
    f32, bf16 = jnp.float32, jnp.bfloat16
    state_s, state_v = arrays["state_s"], arrays["state_v"]
    chans, tok = state_s.shape
    own = chans // shards
    packed = own % 16 == 0
    full = lambda shape: pl.BlockSpec(shape, lambda i, n=len(shape): (0,) * n)

    def layer_spec(w, layer):
        return pl.BlockSpec((pl.Squeezed(),) + w.shape[1:], lambda i: (layer,) + (0,) * (w.ndim - 1))

    ins, specs = [state_s, state_v], [full(state_s.shape), full(state_v.shape)]
    post_names = ("w_out_s", "w_out_v", "w_up", "w_down", "w_mix", "w_gate")
    if post is not None:
        ins += [arrays["conv"], arrays["query"]]
        specs += [full(arrays["conv"].shape), full(arrays["query"].shape)]
        for name in post_names + ("gains_t",):
            ins.append(weights[name])
            specs.append(layer_spec(weights[name], post))
    if pre is not None:
        for name in ("w_qkw_s", "w_qkw_v", "gains_t"):
            ins.append(weights[name])
            specs.append(layer_spec(weights[name], pre))
    outs = []
    if pre is not None:
        plane_shape = (shards, 7, own, tok) if packed else (7, chans, tok)
        outs += [(plane_shape, bf16), ((4, chans, tok), bf16)]
        if post is not None:
            outs += [((chans, tok), f32), ((3, chans, tok), f32)]
    else:
        outs += [((chans, tok), bf16), ((3, chans, tok), bf16)]

    def snorm(x, g):
        return x * lax.rsqrt(jnp.mean(x * x, axis=0, keepdims=True) + 1e-05) * g

    def vnorm(xs, g):
        total = sum(jnp.sum(x * x, axis=0, keepdims=True) for x in xs)
        scale = lax.rsqrt(total / (3 * chans) + 1e-05)
        return [x * scale * g for x in xs]

    def mm(w, x):
        return jnp.dot(w, x, preferred_element_type=f32)

    def kernel(*refs):
        refs = list(refs)
        ss_ref, sv_ref = refs.pop(0), refs.pop(0)
        ss = ss_ref[...].astype(f32)
        sv = [sv_ref[j].astype(f32) for j in range(3)]
        if post is not None:
            conv_ref, q_ref = refs.pop(0), refs.pop(0)
            wos, wov, wup, wdn, wmx, wgt, gp = [refs.pop(0) for _ in range(7)]
            g = gp[...].T
            qs = q_ref[0].astype(f32)
            if packed:
                planes = [jnp.concatenate([conv_ref[d, p] for d in range(shards)], axis=0) for p in range(4)]
            else:
                planes = [conv_ref[p] for p in range(4)]
            ys = planes[0].astype(f32)
            yv = [planes[1 + j].astype(f32) for j in range(3)]
            mix = q_ref[1].astype(f32) * yv[0]
            mix = mix + q_ref[2].astype(f32) * yv[1]
            mix = mix + q_ref[3].astype(f32) * yv[2]
            out_s = (qs * ys + mix).astype(bf16)
            ss = ss + mm(wos[...], out_s)
            sv = [sv[j] + mm(wov[...], (qs * yv[j]).astype(bf16)) for j in range(3)]
            mlp_s = snorm(ss, g[:, 2:3]).astype(bf16)
            mlp_v = [v.astype(bf16) for v in vnorm(sv, g[:, 3:4])]
            hidden = gelu_tanh(mm(wup[...], mlp_s)).astype(bf16)
            gate = 1.0 / (1.0 + jnp.exp(-mm(wgt[...], mlp_s)))
            ss = ss + mm(wdn[...], hidden)
            sv = [sv[j] + mm(wmx[...], mlp_v[j]) * gate for j in range(3)]
        if pre is not None:
            wqs, wqv, gq = [refs.pop(0) for _ in range(3)]
            g = gq[...].T
            planes_ref, query_ref = refs.pop(0), refs.pop(0)

            def put(p, value):
                if packed:
                    for d in range(shards):
                        planes_ref[d, p] = value[d * own : (d + 1) * own]
                else:
                    planes_ref[p] = value

            normed_s = snorm(ss, g[:, 0:1]).astype(bf16)
            normed_v = [v.astype(bf16) for v in vnorm(sv, g[:, 1:2])]
            ps = mm(wqs[...], normed_s)
            query_ref[0] = ps[:chans].astype(bf16)
            put(0, (ps[chans : 2 * chans] * ps[2 * chans :]).astype(bf16))
            for j in range(3):
                pv = mm(wqv[...], normed_v[j]).astype(bf16)
                query_ref[1 + j] = pv[:chans]
                put(1 + j, pv[chans : 2 * chans])
                put(4 + j, pv[2 * chans :])
            if post is not None:
                ns_ref, nv_ref = refs.pop(0), refs.pop(0)
                ns_ref[...] = ss
                for j in range(3):
                    nv_ref[j] = sv[j]
        else:
            os_ref, ov_ref = refs.pop(0), refs.pop(0)
            os_ref[...] = ss.astype(bf16)
            for j in range(3):
                ov_ref[j] = sv[j].astype(bf16)

    return pl.pallas_call(
        kernel,
        grid=(1,),
        in_specs=specs,
        out_specs=[full(shape) for shape, _ in outs],
        out_shape=[jax.ShapeDtypeStruct(shape, dtype) for shape, dtype in outs],
    )(*ins)


def per_device(
    scalars,
    vectors,
    w_qkw_s,
    w_qkw_v,
    w_out_s,
    w_out_v,
    w_up,
    w_down,
    w_mix,
    w_gate,
    gains,
    pe_w1,
    pe_w2,
    pe_w3,
    rates,
):
    chans = scalars.shape[0]
    tok_local = scalars.shape[1]
    shards = lax.axis_size("seq")
    rank = lax.axis_index("seq")
    length = tok_local * shards
    own = chans // shards
    depth = w_qkw_s.shape[0]
    tables = make_tables(shards, tok_local)
    positions = jnp.arange(length, dtype=jnp.int32)

    def filter_spec(first, second, third, decay):
        third = lax.dynamic_slice_in_dim(third, rank * own, own, axis=0)
        decay = lax.dynamic_slice_in_dim(decay, rank * own, own, axis=0)
        made = filter_values(positions, length, first, second, third, decay)
        made = made.reshape(own, shards, tok_local).transpose(1, 0, 2)
        return forward_dft(made[:, None].astype(jnp.float32), tables, FAST)[:, 0]

    weights = {
        "w_qkw_s": w_qkw_s,
        "w_qkw_v": w_qkw_v,
        "w_out_s": w_out_s,
        "w_out_v": w_out_v,
        "w_up": w_up,
        "w_down": w_down,
        "w_mix": w_mix,
        "w_gate": w_gate,
        "gains_t": gains,
    }
    arrays = {"state_s": scalars, "state_v": vectors}
    packed = own % 16 == 0
    planes, query = token_step(None, 0, arrays, weights, shards)
    tied = lax.optimization_barrier((pe_w1[0], pe_w2[0], pe_w3[0], rates[0], planes))
    spec_next = filter_spec(*tied[:4])
    for layer in range(depth):
        outgoing = planes
        if not packed:
            outgoing = planes.reshape(7, shards, own, tok_local).transpose(1, 0, 2, 3)
        regrouped = lax.all_to_all(outgoing, "seq", 0, 0, tiled=True)
        convolved = convolve(regrouped, spec_next, tables)
        if layer + 1 < depth:
            tied = lax.optimization_barrier(
                (pe_w1[layer + 1], pe_w2[layer + 1], pe_w3[layer + 1], rates[layer + 1], convolved)
            )
            spec_next = filter_spec(*tied[:4])
        returned = lax.all_to_all(convolved, "seq", 0, 0, tiled=True)
        arrays["conv"] = returned
        if not packed:
            arrays["conv"] = returned.transpose(1, 0, 2, 3).reshape(4, chans, tok_local)
        arrays["query"] = query
        if layer + 1 < depth:
            planes, query, new_s, new_v = token_step(layer, layer + 1, arrays, weights, shards)
            arrays["state_s"], arrays["state_v"] = new_s, new_v
        else:
            return tuple(token_step(layer, None, arrays, weights, shards))


def solution(mesh):
    in_specs = (
        P(None, ("grp", "seq")),
        P(None, None, ("grp", "seq")),
        P(),
        P(),
        P(),
        P(),
        P(),
        P(),
        P(),
        P(),
        P(),
        P(),
        P(),
        P(),
        P(),
    )
    out_specs = (P(None, ("grp", "seq")), P(None, None, ("grp", "seq")))
    return jax.shard_map(
        per_device, mesh=mesh, in_specs=in_specs, out_specs=out_specs, check_vma=False
    )
```

```python
import math

import jax
import jax.numpy as jnp
import numpy as np
from jax import lax
from jax.experimental import pallas as pl
from jax.sharding import PartitionSpec as P

HIGH = lax.Precision.HIGHEST
FAST = lax.Precision.DEFAULT


def filter_values(positions, length, first, second, third, decay):
    count = first.shape[1] // 2
    freqs = jnp.arange(1, count + 1, dtype=jnp.int32)
    turns = freqs[:, None] * positions[None, :] % length
    angle = turns.astype(jnp.float32) * (2.0 * math.pi / length)
    feats = jnp.concatenate([jnp.cos(angle), jnp.sin(angle)], axis=0)
    hid_one = jnp.sin(jnp.dot(first, feats, precision=HIGH))
    hid_two = jnp.sin(jnp.dot(second, hid_one, precision=HIGH))
    raw = jnp.dot(third, hid_two, precision=HIGH)
    envelope = jnp.exp(-decay[:, None] * positions[None, :].astype(jnp.float32) / length)
    return (raw * envelope / math.sqrt(length)).astype(jnp.bfloat16)


def scalar_norm(field, gain):
    return field * lax.rsqrt(jnp.mean(field * field, axis=0, keepdims=True) + 1e-05) * gain[:, None]


def vector_norm(field, gain):
    return (
        field
        * lax.rsqrt(jnp.mean(field * field, axis=(0, 1), keepdims=True) + 1e-05)
        * gain[None, :, None]
    )


def make_tables(shards, local):
    length = shards * local
    f32, bf16 = jnp.float32, jnp.bfloat16

    def turns(rows, cols, period):
        rows = jnp.arange(rows, dtype=jnp.int32)[:, None]
        cols = jnp.arange(cols, dtype=jnp.int32)[None, :]
        return ((rows * cols) % period).astype(f32) * (2.0 * math.pi / period)

    half = shards // 2 + 1 if shards % 2 == 0 else shards
    ang_s = turns(half, shards, shards)
    cos_s, sin_s = jnp.cos(ang_s), jnp.sin(ang_s)
    lead_fwd = jnp.concatenate([cos_s, -sin_s], axis=0)
    if half == shards:
        weight = jnp.ones((half,), f32)
    else:
        weight = jnp.full((half,), 2.0, f32).at[0].set(1.0).at[half - 1].set(1.0)
    lead_inv = jnp.concatenate([cos_s.T * weight, -sin_s.T * weight], axis=1)
    ang_t = turns(half, local, length)
    tw_c = jnp.cos(ang_t)[:, None, None, :]
    tw_s = jnp.sin(ang_t)[:, None, None, :]
    ang_l = turns(local, local, local)
    cos_l, sin_l = jnp.cos(ang_l), jnp.sin(ang_l)
    lane_fwd = jnp.block([[cos_l, -sin_l], [sin_l, cos_l]])
    lane_inv = jnp.block([[cos_l, sin_l], [-sin_l, cos_l]])
    return (
        lead_fwd.astype(bf16),
        lead_inv.astype(bf16),
        tw_c,
        tw_s,
        lane_fwd.astype(bf16),
        lane_inv.astype(bf16),
    )


def forward_dft(field, tables, prec):
    lead_fwd, _, tw_c, tw_s, lane_fwd, _ = tables
    shards, planes, chans, local = field.shape
    flat = field.reshape(shards, -1).astype(jnp.bfloat16)
    stage = jnp.dot(lead_fwd, flat, preferred_element_type=jnp.float32)
    half = lead_fwd.shape[0] // 2
    stage = stage.reshape(2 * half, planes, chans, local)
    st_r, st_i = stage[:half], stage[half:]
    tw_r = st_r * tw_c + st_i * tw_s
    tw_i = st_i * tw_c - st_r * tw_s
    joined = jnp.concatenate([tw_r, tw_i], axis=-1).reshape(-1, 2 * local).astype(jnp.bfloat16)
    spec = jnp.dot(joined, lane_fwd, preferred_element_type=jnp.float32)
    return spec.reshape(half, planes, chans, 2 * local)


def inverse_dft(spec, tables, prec):
    _, lead_inv, tw_c, tw_s, _, lane_inv = tables
    half, planes, chans, width = spec.shape
    shards = lead_inv.shape[0]
    local = width // 2
    flat = spec.reshape(-1, width).astype(jnp.bfloat16)
    back = jnp.dot(flat, lane_inv, preferred_element_type=jnp.float32)
    back = back.reshape(half, planes, chans, width)
    bk_r, bk_i = back[..., :local], back[..., local:]
    un_r = bk_r * tw_c - bk_i * tw_s
    un_i = bk_r * tw_s + bk_i * tw_c
    stacked = jnp.concatenate([un_r, un_i], axis=0).reshape(2 * half, -1).astype(jnp.bfloat16)
    whole = jnp.dot(lead_inv, stacked, preferred_element_type=jnp.float32)
    return whole.reshape(shards, planes, chans, local)


def cmul(a_r, a_i, b_r, b_i):
    return a_r * b_r - a_i * b_i, a_r * b_i + a_i * b_r


def convolve(received, filt_spec, tables):
    shards, _, chans, local = received.shape
    length = shards * local
    spec = forward_dft(received.astype(jnp.float32), tables, FAST)
    re, im = spec[..., :local], spec[..., local:]
    h_r, h_i = filt_spec[..., :local], filt_spec[..., local:]
    p_r, p_i = cmul(re[:, 0], im[:, 0], h_r, h_i)
    outs_r, outs_i = [p_r], [p_i]
    for j in range(3):
        one, two = (j + 1) % 3, (j + 2) % 3
        a_r, a_i = cmul(re[:, 1 + one], im[:, 1 + one], re[:, 4 + two], im[:, 4 + two])
        b_r, b_i = cmul(re[:, 1 + two], im[:, 1 + two], re[:, 4 + one], im[:, 4 + one])
        outs_r.append(a_r - b_r)
        outs_i.append(a_i - b_i)
    prod = jnp.concatenate([jnp.stack(outs_r, axis=1), jnp.stack(outs_i, axis=1)], axis=-1)
    result = inverse_dft(prod, tables, FAST)
    inv_root = 1.0 / math.sqrt(length)
    scale = jnp.array([1.0, inv_root, inv_root, inv_root], dtype=jnp.float32) / length
    return (result * scale[None, :, None, None]).astype(jnp.bfloat16)


def gelu_tanh(x):
    return 0.5 * x * (1.0 + jnp.tanh(math.sqrt(2.0 / math.pi) * (x + 0.044715 * (x * x * x))))


def token_step(post, pre, arrays, weights, shards):
    f32, bf16 = jnp.float32, jnp.bfloat16
    state_s, state_v = arrays["state_s"], arrays["state_v"]
    chans, tok = state_s.shape
    own = chans // shards
    packed = own % 16 == 0
    full = lambda shape: pl.BlockSpec(shape, lambda i, n=len(shape): (0,) * n)

    def layer_spec(w, layer):
        return pl.BlockSpec((pl.Squeezed(),) + w.shape[1:], lambda i: (layer,) + (0,) * (w.ndim - 1))

    ins, specs = [state_s, state_v], [full(state_s.shape), full(state_v.shape)]
    post_names = ("w_out_s", "w_out_v", "w_up", "w_down", "w_mix", "w_gate")
    if post is not None:
        ins += [arrays["conv"], arrays["query"]]
        specs += [full(arrays["conv"].shape), full(arrays["query"].shape)]
        for name in post_names + ("gains_t",):
            ins.append(weights[name])
            specs.append(layer_spec(weights[name], post))
    if pre is not None:
        for name in ("w_qkw_s", "w_qkw_v", "gains_t"):
            ins.append(weights[name])
            specs.append(layer_spec(weights[name], pre))
    outs = []
    if pre is not None:
        plane_shape = (shards, 7, own, tok) if packed else (7, chans, tok)
        outs += [(plane_shape, bf16), ((4, chans, tok), bf16)]
        if post is not None:
            outs += [((chans, tok), f32), ((3, chans, tok), f32)]
    else:
        outs += [((chans, tok), bf16), ((3, chans, tok), bf16)]

    def snorm(x, g):
        return x * lax.rsqrt(jnp.mean(x * x, axis=0, keepdims=True) + 1e-05) * g

    def vnorm(xs, g):
        total = sum(jnp.sum(x * x, axis=0, keepdims=True) for x in xs)
        scale = lax.rsqrt(total / (3 * chans) + 1e-05)
        return [x * scale * g for x in xs]

    def mm(w, x):
        return jnp.dot(w, x, preferred_element_type=f32)

    def kernel(*refs):
        refs = list(refs)
        ss_ref, sv_ref = refs.pop(0), refs.pop(0)
        ss = ss_ref[...].astype(f32)
        sv = [sv_ref[j].astype(f32) for j in range(3)]
        if post is not None:
            conv_ref, q_ref = refs.pop(0), refs.pop(0)
            wos, wov, wup, wdn, wmx, wgt, gp = [refs.pop(0) for _ in range(7)]
            g = gp[...].T
            qs = q_ref[0].astype(f32)
            if packed:
                planes = [jnp.concatenate([conv_ref[d, p] for d in range(shards)], axis=0) for p in range(4)]
            else:
                planes = [conv_ref[p] for p in range(4)]
            ys = planes[0].astype(f32)
            yv = [planes[1 + j].astype(f32) for j in range(3)]
            mix = q_ref[1].astype(f32) * yv[0]
            mix = mix + q_ref[2].astype(f32) * yv[1]
            mix = mix + q_ref[3].astype(f32) * yv[2]
            out_s = (qs * ys + mix).astype(bf16)
            ss = ss + mm(wos[...], out_s)
            sv = [sv[j] + mm(wov[...], (qs * yv[j]).astype(bf16)) for j in range(3)]
            mlp_s = snorm(ss, g[:, 2:3]).astype(bf16)
            mlp_v = [v.astype(bf16) for v in vnorm(sv, g[:, 3:4])]
            hidden = gelu_tanh(mm(wup[...], mlp_s)).astype(bf16)
            gate = 1.0 / (1.0 + jnp.exp(-mm(wgt[...], mlp_s)))
            ss = ss + mm(wdn[...], hidden)
            sv = [sv[j] + mm(wmx[...], mlp_v[j]) * gate for j in range(3)]
        if pre is not None:
            wqs, wqv, gq = [refs.pop(0) for _ in range(3)]
            g = gq[...].T
            planes_ref, query_ref = refs.pop(0), refs.pop(0)

            def put(p, value):
                if packed:
                    for d in range(shards):
                        planes_ref[d, p] = value[d * own : (d + 1) * own]
                else:
                    planes_ref[p] = value

            normed_s = snorm(ss, g[:, 0:1]).astype(bf16)
            normed_v = [v.astype(bf16) for v in vnorm(sv, g[:, 1:2])]
            ps = mm(wqs[...], normed_s)
            query_ref[0] = ps[:chans].astype(bf16)
            put(0, (ps[chans : 2 * chans] * ps[2 * chans :]).astype(bf16))
            for j in range(3):
                pv = mm(wqv[...], normed_v[j]).astype(bf16)
                query_ref[1 + j] = pv[:chans]
                put(1 + j, pv[chans : 2 * chans])
                put(4 + j, pv[2 * chans :])
            if post is not None:
                ns_ref, nv_ref = refs.pop(0), refs.pop(0)
                ns_ref[...] = ss
                for j in range(3):
                    nv_ref[j] = sv[j]
        else:
            os_ref, ov_ref = refs.pop(0), refs.pop(0)
            os_ref[...] = ss.astype(bf16)
            for j in range(3):
                ov_ref[j] = sv[j].astype(bf16)

    return pl.pallas_call(
        kernel,
        grid=(1,),
        in_specs=specs,
        out_specs=[full(shape) for shape, _ in outs],
        out_shape=[jax.ShapeDtypeStruct(shape, dtype) for shape, dtype in outs],
    )(*ins)


def per_device(
    scalars,
    vectors,
    w_qkw_s,
    w_qkw_v,
    w_out_s,
    w_out_v,
    w_up,
    w_down,
    w_mix,
    w_gate,
    gains,
    pe_w1,
    pe_w2,
    pe_w3,
    rates,
):
    chans = scalars.shape[0]
    tok_local = scalars.shape[1]
    shards = lax.axis_size("seq")
    rank = lax.axis_index("seq")
    length = tok_local * shards
    own = chans // shards
    depth = w_qkw_s.shape[0]
    tables = make_tables(shards, tok_local)
    positions = jnp.arange(length, dtype=jnp.int32)

    def filter_spec(first, second, third, decay):
        third = lax.dynamic_slice_in_dim(third, rank * own, own, axis=0)
        decay = lax.dynamic_slice_in_dim(decay, rank * own, own, axis=0)
        made = filter_values(positions, length, first, second, third, decay)
        made = made.reshape(own, shards, tok_local).transpose(1, 0, 2)
        return forward_dft(made[:, None].astype(jnp.float32), tables, FAST)[:, 0]

    weights = {
        "w_qkw_s": w_qkw_s,
        "w_qkw_v": w_qkw_v,
        "w_out_s": w_out_s,
        "w_out_v": w_out_v,
        "w_up": w_up,
        "w_down": w_down,
        "w_mix": w_mix,
        "w_gate": w_gate,
        "gains_t": gains,
    }
    arrays = {"state_s": scalars, "state_v": vectors}
    packed = own % 16 == 0
    planes, query = token_step(None, 0, arrays, weights, shards)
    tied = lax.optimization_barrier((pe_w1[0], pe_w2[0], pe_w3[0], rates[0], planes))
    spec_next = filter_spec(*tied[:4])
    for layer in range(depth):
        outgoing = planes
        if not packed:
            outgoing = planes.reshape(7, shards, own, tok_local).transpose(1, 0, 2, 3)
        regrouped = lax.all_to_all(outgoing, "seq", 0, 0, tiled=True)
        convolved = convolve(regrouped, spec_next, tables)
        if layer + 1 < depth:
            tied = lax.optimization_barrier(
                (pe_w1[layer + 1], pe_w2[layer + 1], pe_w3[layer + 1], rates[layer + 1], convolved)
            )
            spec_next = filter_spec(*tied[:4])
        returned = lax.all_to_all(convolved, "seq", 0, 0, tiled=True)
        arrays["conv"] = returned
        if not packed:
            arrays["conv"] = returned.transpose(1, 0, 2, 3).reshape(4, chans, tok_local)
        arrays["query"] = query
        if layer + 1 < depth:
            planes, query, new_s, new_v = token_step(layer, layer + 1, arrays, weights, shards)
            arrays["state_s"], arrays["state_v"] = new_s, new_v
        else:
            return tuple(token_step(layer, None, arrays, weights, shards))


def solution(mesh):
    in_specs = (
        P(None, ("grp", "seq")),
        P(None, None, ("grp", "seq")),
        P(),
        P(),
        P(),
        P(),
        P(),
        P(),
        P(),
        P(),
        P(),
        P(),
        P(),
        P(),
        P(),
    )
    out_specs = (P(None, ("grp", "seq")), P(None, None, ("grp", "seq")))
    return jax.shard_map(
        per_device, mesh=mesh, in_specs=in_specs, out_specs=out_specs, check_vma=False
    )
```

```python
import math

import jax
import jax.numpy as jnp
import numpy as np
from jax import lax
from jax.experimental import pallas as pl
from jax.sharding import PartitionSpec as P

HIGH = lax.Precision.HIGHEST
FAST = lax.Precision.DEFAULT


def filter_values(positions, length, first, second, third, decay):
    count = first.shape[1] // 2
    freqs = jnp.arange(1, count + 1, dtype=jnp.int32)
    turns = freqs[:, None] * positions[None, :] % length
    angle = turns.astype(jnp.float32) * (2.0 * math.pi / length)
    feats = jnp.concatenate([jnp.cos(angle), jnp.sin(angle)], axis=0)
    hid_one = jnp.sin(jnp.dot(first, feats, precision=HIGH))
    hid_two = jnp.sin(jnp.dot(second, hid_one, precision=HIGH))
    raw = jnp.dot(third, hid_two, precision=HIGH)
    envelope = jnp.exp(-decay[:, None] * positions[None, :].astype(jnp.float32) / length)
    return (raw * envelope / math.sqrt(length)).astype(jnp.bfloat16)


def scalar_norm(field, gain):
    return field * lax.rsqrt(jnp.mean(field * field, axis=0, keepdims=True) + 1e-05) * gain[:, None]


def vector_norm(field, gain):
    return (
        field
        * lax.rsqrt(jnp.mean(field * field, axis=(0, 1), keepdims=True) + 1e-05)
        * gain[None, :, None]
    )


def make_tables(shards, local):
    length = shards * local
    f32, bf16 = jnp.float32, jnp.bfloat16

    def turns(rows, cols, period):
        rows = jnp.arange(rows, dtype=jnp.int32)[:, None]
        cols = jnp.arange(cols, dtype=jnp.int32)[None, :]
        return ((rows * cols) % period).astype(f32) * (2.0 * math.pi / period)

    half = shards // 2 + 1 if shards % 2 == 0 else shards
    ang_s = turns(half, shards, shards)
    cos_s, sin_s = jnp.cos(ang_s), jnp.sin(ang_s)
    lead_fwd = jnp.concatenate([cos_s, -sin_s], axis=0)
    if half == shards:
        weight = jnp.ones((half,), f32)
    else:
        weight = jnp.full((half,), 2.0, f32).at[0].set(1.0).at[half - 1].set(1.0)
    weight = weight / length
    lead_inv = jnp.concatenate([cos_s.T * weight, -sin_s.T * weight], axis=1)
    ang_t = turns(half, local, length)
    tw_c = jnp.cos(ang_t)[:, None, None, :]
    tw_s = jnp.sin(ang_t)[:, None, None, :]
    ang_l = turns(local, local, local)
    cos_l, sin_l = jnp.cos(ang_l), jnp.sin(ang_l)
    lane_fwd = jnp.block([[cos_l, -sin_l], [sin_l, cos_l]])
    lane_inv = jnp.block([[cos_l, sin_l], [-sin_l, cos_l]])
    return (
        lead_fwd.astype(bf16),
        lead_inv.astype(bf16),
        tw_c,
        tw_s,
        lane_fwd.astype(bf16),
        lane_inv.astype(bf16),
    )


def forward_dft(field, tables, prec):
    lead_fwd, _, tw_c, tw_s, lane_fwd, _ = tables
    shards, planes, chans, local = field.shape
    flat = field.reshape(shards, -1).astype(jnp.bfloat16)
    stage = jnp.dot(lead_fwd, flat, preferred_element_type=jnp.float32)
    half = lead_fwd.shape[0] // 2
    stage = stage.reshape(2 * half, planes, chans, local)
    st_r, st_i = stage[:half], stage[half:]
    tw_r = st_r * tw_c + st_i * tw_s
    tw_i = st_i * tw_c - st_r * tw_s
    joined = jnp.concatenate([tw_r, tw_i], axis=-1).reshape(-1, 2 * local).astype(jnp.bfloat16)
    spec = jnp.dot(joined, lane_fwd, preferred_element_type=jnp.float32)
    return spec.reshape(half, planes, chans, 2 * local)


def inverse_dft(spec, tables, prec):
    _, lead_inv, tw_c, tw_s, _, lane_inv = tables
    half, planes, chans, width = spec.shape
    shards = lead_inv.shape[0]
    local = width // 2
    flat = spec.reshape(-1, width).astype(jnp.bfloat16)
    back = jnp.dot(flat, lane_inv, preferred_element_type=jnp.float32)
    back = back.reshape(half, planes, chans, width)
    bk_r, bk_i = back[..., :local], back[..., local:]
    un_r = bk_r * tw_c - bk_i * tw_s
    un_i = bk_r * tw_s + bk_i * tw_c
    stacked = jnp.concatenate([un_r, un_i], axis=0).reshape(2 * half, -1).astype(jnp.bfloat16)
    whole = jnp.dot(lead_inv, stacked, preferred_element_type=jnp.float32)
    return whole.reshape(shards, planes, chans, local)


def cmul(a_r, a_i, b_r, b_i):
    return a_r * b_r - a_i * b_i, a_r * b_i + a_i * b_r


def convolve(received, filt_spec, tables):
    shards, _, chans, local = received.shape
    length = shards * local
    spec = forward_dft(received.astype(jnp.float32), tables, FAST)
    re, im = spec[..., :local], spec[..., local:]
    h_r, h_i = filt_spec[..., :local], filt_spec[..., local:]
    inv_root = 1.0 / math.sqrt(length)
    p_r, p_i = cmul(re[:, 0], im[:, 0], h_r, h_i)
    outs_r, outs_i = [p_r], [p_i]
    for j in range(3):
        one, two = (j + 1) % 3, (j + 2) % 3
        a_r, a_i = cmul(re[:, 1 + one], im[:, 1 + one], re[:, 4 + two], im[:, 4 + two])
        b_r, b_i = cmul(re[:, 1 + two], im[:, 1 + two], re[:, 4 + one], im[:, 4 + one])
        outs_r.append((a_r - b_r) * inv_root)
        outs_i.append((a_i - b_i) * inv_root)
    prod = jnp.concatenate([jnp.stack(outs_r, axis=1), jnp.stack(outs_i, axis=1)], axis=-1)
    return inverse_dft(prod, tables, FAST).astype(jnp.bfloat16)


def gelu_tanh(x):
    return 0.5 * x * (1.0 + jnp.tanh(math.sqrt(2.0 / math.pi) * (x + 0.044715 * (x * x * x))))


def token_step(post, pre, arrays, weights, shards):
    f32, bf16 = jnp.float32, jnp.bfloat16
    state_s, state_v = arrays["state_s"], arrays["state_v"]
    chans, tok = state_s.shape
    own = chans // shards
    packed = own % 16 == 0
    full = lambda shape: pl.BlockSpec(shape, lambda i, n=len(shape): (0,) * n)

    def layer_spec(w, layer):
        return pl.BlockSpec((pl.Squeezed(),) + w.shape[1:], lambda i: (layer,) + (0,) * (w.ndim - 1))

    ins, specs = [state_s, state_v], [full(state_s.shape), full(state_v.shape)]
    post_names = ("w_out_s", "w_out_v", "w_up", "w_down", "w_mix", "w_gate")
    if post is not None:
        ins += [arrays["conv"], arrays["query"]]
        specs += [full(arrays["conv"].shape), full(arrays["query"].shape)]
        for name in post_names + ("gains_t",):
            ins.append(weights[name])
            specs.append(layer_spec(weights[name], post))
    if pre is not None:
        for name in ("w_qkw_s", "w_qkw_v", "gains_t"):
            ins.append(weights[name])
            specs.append(layer_spec(weights[name], pre))
    outs = []
    if pre is not None:
        plane_shape = (shards, 7, own, tok) if packed else (7, chans, tok)
        outs += [(plane_shape, bf16), ((4, chans, tok), bf16)]
        if post is not None:
            outs += [((chans, tok), f32), ((3, chans, tok), f32)]
    else:
        outs += [((chans, tok), bf16), ((3, chans, tok), bf16)]

    def snorm(x, g):
        return x * lax.rsqrt(jnp.mean(x * x, axis=0, keepdims=True) + 1e-05) * g

    def vnorm(xs, g):
        total = sum(jnp.sum(x * x, axis=0, keepdims=True) for x in xs)
        scale = lax.rsqrt(total / (3 * chans) + 1e-05)
        return [x * scale * g for x in xs]

    def mm(w, x):
        return jnp.dot(w, x, preferred_element_type=f32)

    def kernel(*refs):
        refs = list(refs)
        ss_ref, sv_ref = refs.pop(0), refs.pop(0)
        ss = ss_ref[...].astype(f32)
        sv = [sv_ref[j].astype(f32) for j in range(3)]
        if post is not None:
            conv_ref, q_ref = refs.pop(0), refs.pop(0)
            wos, wov, wup, wdn, wmx, wgt, gp = [refs.pop(0) for _ in range(7)]
            g = gp[...].T
            qs = q_ref[0].astype(f32)
            if packed:
                planes = [jnp.concatenate([conv_ref[d, p] for d in range(shards)], axis=0) for p in range(4)]
            else:
                planes = [conv_ref[p] for p in range(4)]
            ys = planes[0].astype(f32)
            yv = [planes[1 + j].astype(f32) for j in range(3)]
            mix = q_ref[1].astype(f32) * yv[0]
            mix = mix + q_ref[2].astype(f32) * yv[1]
            mix = mix + q_ref[3].astype(f32) * yv[2]
            out_s = (qs * ys + mix).astype(bf16)
            ss = ss + mm(wos[...], out_s)
            sv = [sv[j] + mm(wov[...], (qs * yv[j]).astype(bf16)) for j in range(3)]
            mlp_s = snorm(ss, g[:, 2:3]).astype(bf16)
            mlp_v = [v.astype(bf16) for v in vnorm(sv, g[:, 3:4])]
            hidden = gelu_tanh(mm(wup[...], mlp_s)).astype(bf16)
            gate = 1.0 / (1.0 + jnp.exp(-mm(wgt[...], mlp_s)))
            ss = ss + mm(wdn[...], hidden)
            sv = [sv[j] + mm(wmx[...], mlp_v[j]) * gate for j in range(3)]
        if pre is not None:
            wqs, wqv, gq = [refs.pop(0) for _ in range(3)]
            g = gq[...].T
            planes_ref, query_ref = refs.pop(0), refs.pop(0)

            def put(p, value):
                if packed:
                    for d in range(shards):
                        planes_ref[d, p] = value[d * own : (d + 1) * own]
                else:
                    planes_ref[p] = value

            normed_s = snorm(ss, g[:, 0:1]).astype(bf16)
            normed_v = [v.astype(bf16) for v in vnorm(sv, g[:, 1:2])]
            ps = mm(wqs[...], normed_s)
            query_ref[0] = ps[:chans].astype(bf16)
            put(0, (ps[chans : 2 * chans] * ps[2 * chans :]).astype(bf16))
            for j in range(3):
                pv = mm(wqv[...], normed_v[j]).astype(bf16)
                query_ref[1 + j] = pv[:chans]
                put(1 + j, pv[chans : 2 * chans])
                put(4 + j, pv[2 * chans :])
            if post is not None:
                ns_ref, nv_ref = refs.pop(0), refs.pop(0)
                ns_ref[...] = ss
                for j in range(3):
                    nv_ref[j] = sv[j]
        else:
            os_ref, ov_ref = refs.pop(0), refs.pop(0)
            os_ref[...] = ss.astype(bf16)
            for j in range(3):
                ov_ref[j] = sv[j].astype(bf16)

    return pl.pallas_call(
        kernel,
        grid=(1,),
        in_specs=specs,
        out_specs=[full(shape) for shape, _ in outs],
        out_shape=[jax.ShapeDtypeStruct(shape, dtype) for shape, dtype in outs],
    )(*ins)


def per_device(
    scalars,
    vectors,
    w_qkw_s,
    w_qkw_v,
    w_out_s,
    w_out_v,
    w_up,
    w_down,
    w_mix,
    w_gate,
    gains,
    pe_w1,
    pe_w2,
    pe_w3,
    rates,
):
    chans = scalars.shape[0]
    tok_local = scalars.shape[1]
    shards = lax.axis_size("seq")
    rank = lax.axis_index("seq")
    length = tok_local * shards
    own = chans // shards
    depth = w_qkw_s.shape[0]
    tables = make_tables(shards, tok_local)
    positions = jnp.arange(length, dtype=jnp.int32)

    def filter_spec(first, second, third, decay):
        third = lax.dynamic_slice_in_dim(third, rank * own, own, axis=0)
        decay = lax.dynamic_slice_in_dim(decay, rank * own, own, axis=0)
        made = filter_values(positions, length, first, second, third, decay)
        made = made.reshape(own, shards, tok_local).transpose(1, 0, 2)
        return forward_dft(made[:, None].astype(jnp.float32), tables, FAST)[:, 0]

    weights = {
        "w_qkw_s": w_qkw_s,
        "w_qkw_v": w_qkw_v,
        "w_out_s": w_out_s,
        "w_out_v": w_out_v,
        "w_up": w_up,
        "w_down": w_down,
        "w_mix": w_mix,
        "w_gate": w_gate,
        "gains_t": gains,
    }
    arrays = {"state_s": scalars, "state_v": vectors}
    packed = own % 16 == 0
    planes, query = token_step(None, 0, arrays, weights, shards)
    tied = lax.optimization_barrier((pe_w1[0], pe_w2[0], pe_w3[0], rates[0], planes))
    spec_next = filter_spec(*tied[:4])
    for layer in range(depth):
        outgoing = planes
        if not packed:
            outgoing = planes.reshape(7, shards, own, tok_local).transpose(1, 0, 2, 3)
        regrouped = lax.all_to_all(outgoing, "seq", 0, 0, tiled=True)
        convolved = convolve(regrouped, spec_next, tables)
        if layer + 1 < depth:
            tied = lax.optimization_barrier(
                (pe_w1[layer + 1], pe_w2[layer + 1], pe_w3[layer + 1], rates[layer + 1], convolved)
            )
            spec_next = filter_spec(*tied[:4])
        returned = lax.all_to_all(convolved, "seq", 0, 0, tiled=True)
        arrays["conv"] = returned
        if not packed:
            arrays["conv"] = returned.transpose(1, 0, 2, 3).reshape(4, chans, tok_local)
        arrays["query"] = query
        if layer + 1 < depth:
            planes, query, new_s, new_v = token_step(layer, layer + 1, arrays, weights, shards)
            arrays["state_s"], arrays["state_v"] = new_s, new_v
        else:
            return tuple(token_step(layer, None, arrays, weights, shards))


def solution(mesh):
    in_specs = (
        P(None, ("grp", "seq")),
        P(None, None, ("grp", "seq")),
        P(),
        P(),
        P(),
        P(),
        P(),
        P(),
        P(),
        P(),
        P(),
        P(),
        P(),
        P(),
        P(),
    )
    out_specs = (P(None, ("grp", "seq")), P(None, None, ("grp", "seq")))
    return jax.shard_map(
        per_device, mesh=mesh, in_specs=in_specs, out_specs=out_specs, check_vma=False
    )
```

```python
import math

import jax
import jax.numpy as jnp
import numpy as np
from jax import lax
from jax.experimental import pallas as pl
from jax.sharding import PartitionSpec as P

HIGH = lax.Precision.HIGHEST
FAST = lax.Precision.DEFAULT


def filter_values(positions, length, first, second, third, decay):
    count = first.shape[1] // 2
    freqs = jnp.arange(1, count + 1, dtype=jnp.int32)
    turns = freqs[:, None] * positions[None, :] % length
    angle = turns.astype(jnp.float32) * (2.0 * math.pi / length)
    feats = jnp.concatenate([jnp.cos(angle), jnp.sin(angle)], axis=0)
    hid_one = jnp.sin(jnp.dot(first, feats, precision=HIGH))
    hid_two = jnp.sin(jnp.dot(second, hid_one, precision=HIGH))
    raw = jnp.dot(third, hid_two, precision=HIGH)
    envelope = jnp.exp(-decay[:, None] * positions[None, :].astype(jnp.float32) / length)
    return (raw * envelope / math.sqrt(length)).astype(jnp.bfloat16)


def scalar_norm(field, gain):
    return field * lax.rsqrt(jnp.mean(field * field, axis=0, keepdims=True) + 1e-05) * gain[:, None]


def vector_norm(field, gain):
    return (
        field
        * lax.rsqrt(jnp.mean(field * field, axis=(0, 1), keepdims=True) + 1e-05)
        * gain[None, :, None]
    )


def make_tables(shards, local):
    length = shards * local
    f32, bf16 = jnp.float32, jnp.bfloat16

    def turns(rows, cols, period):
        rows = jnp.arange(rows, dtype=jnp.int32)[:, None]
        cols = jnp.arange(cols, dtype=jnp.int32)[None, :]
        return ((rows * cols) % period).astype(f32) * (2.0 * math.pi / period)

    half = shards // 2 + 1 if shards % 2 == 0 else shards
    ang_s = turns(half, shards, shards)
    cos_s, sin_s = jnp.cos(ang_s), jnp.sin(ang_s)
    lead_fwd = jnp.concatenate([cos_s, -sin_s], axis=0)
    if half == shards:
        weight = jnp.ones((half,), f32)
    else:
        weight = jnp.full((half,), 2.0, f32).at[0].set(1.0).at[half - 1].set(1.0)
    weight = weight / length
    lead_inv = jnp.concatenate([cos_s.T * weight, -sin_s.T * weight], axis=1)
    ang_t = turns(half, local, length)
    tw_c = jnp.cos(ang_t)[:, None, None, :]
    tw_s = jnp.sin(ang_t)[:, None, None, :]
    ang_l = turns(local, local, local)
    cos_l, sin_l = jnp.cos(ang_l), jnp.sin(ang_l)
    lane_fwd = jnp.block([[cos_l, -sin_l], [sin_l, cos_l]])
    lane_inv = jnp.block([[cos_l, sin_l], [-sin_l, cos_l]])
    return (
        lead_fwd.astype(bf16),
        lead_inv.astype(bf16),
        tw_c,
        tw_s,
        lane_fwd.astype(bf16),
        lane_inv.astype(bf16),
    )


def forward_dft(field, tables, prec):
    lead_fwd, _, tw_c, tw_s, lane_fwd, _ = tables
    shards, planes, chans, local = field.shape
    flat = field.reshape(shards, -1).astype(jnp.bfloat16)
    stage = jnp.dot(lead_fwd, flat, preferred_element_type=jnp.float32)
    half = lead_fwd.shape[0] // 2
    stage = stage.reshape(2 * half, planes, chans, local)
    st_r, st_i = stage[:half], stage[half:]
    tw_r = st_r * tw_c + st_i * tw_s
    tw_i = st_i * tw_c - st_r * tw_s
    joined = jnp.concatenate([tw_r, tw_i], axis=-1).reshape(-1, 2 * local).astype(jnp.bfloat16)
    spec = jnp.dot(joined, lane_fwd, preferred_element_type=jnp.float32)
    return spec.reshape(half, planes, chans, 2 * local)


def inverse_dft(spec, tables, prec):
    _, lead_inv, tw_c, tw_s, _, lane_inv = tables
    half, planes, chans, width = spec.shape
    shards = lead_inv.shape[0]
    local = width // 2
    flat = spec.reshape(-1, width).astype(jnp.bfloat16)
    back = jnp.dot(flat, lane_inv, preferred_element_type=jnp.float32)
    back = back.reshape(half, planes, chans, width)
    bk_r, bk_i = back[..., :local], back[..., local:]
    un_r = bk_r * tw_c - bk_i * tw_s
    un_i = bk_r * tw_s + bk_i * tw_c
    stacked = jnp.concatenate([un_r, un_i], axis=0).reshape(2 * half, -1).astype(jnp.bfloat16)
    whole = jnp.dot(lead_inv, stacked, preferred_element_type=jnp.float32)
    return whole.reshape(shards, planes, chans, local)


def cmul(a_r, a_i, b_r, b_i):
    return a_r * b_r - a_i * b_i, a_r * b_i + a_i * b_r


def convolve(received, filt_spec, tables):
    shards, _, chans, local = received.shape
    length = shards * local
    spec = forward_dft(received.astype(jnp.float32), tables, FAST)
    re, im = spec[..., :local], spec[..., local:]
    h_r, h_i = filt_spec[..., :local], filt_spec[..., local:]
    inv_root = 1.0 / math.sqrt(length)
    p_r, p_i = cmul(re[:, 0], im[:, 0], h_r, h_i)
    outs_r, outs_i = [p_r], [p_i]
    for j in range(3):
        one, two = (j + 1) % 3, (j + 2) % 3
        a_r, a_i = cmul(re[:, 1 + one], im[:, 1 + one], re[:, 4 + two], im[:, 4 + two])
        b_r, b_i = cmul(re[:, 1 + two], im[:, 1 + two], re[:, 4 + one], im[:, 4 + one])
        outs_r.append((a_r - b_r) * inv_root)
        outs_i.append((a_i - b_i) * inv_root)
    prod = jnp.concatenate([jnp.stack(outs_r, axis=1), jnp.stack(outs_i, axis=1)], axis=-1)
    return inverse_dft(prod, tables, FAST).astype(jnp.bfloat16)


def gelu_tanh(x):
    return 0.5 * x * (1.0 + jnp.tanh(math.sqrt(2.0 / math.pi) * (x + 0.044715 * (x * x * x))))


def token_step(post, pre, arrays, weights, shards):
    f32, bf16 = jnp.float32, jnp.bfloat16
    state_s, state_v = arrays["state_s"], arrays["state_v"]
    chans, tok = state_s.shape
    own = chans // shards
    packed = own % 16 == 0
    full = lambda shape: pl.BlockSpec(shape, lambda i, n=len(shape): (0,) * n)

    def layer_spec(w, layer):
        return pl.BlockSpec((pl.Squeezed(),) + w.shape[1:], lambda i: (layer,) + (0,) * (w.ndim - 1))

    ins, specs = [state_s, state_v], [full(state_s.shape), full(state_v.shape)]
    post_names = ("w_out_s", "w_out_v", "w_up", "w_down", "w_mix", "w_gate")
    if post is not None:
        ins += [arrays["conv"], arrays["query"]]
        specs += [full(arrays["conv"].shape), full(arrays["query"].shape)]
        for name in post_names + ("gains_t",):
            ins.append(weights[name])
            specs.append(layer_spec(weights[name], post))
    if pre is not None:
        for name in ("w_qkw_s", "w_qkw_v", "gains_t"):
            ins.append(weights[name])
            specs.append(layer_spec(weights[name], pre))
    outs = []
    if pre is not None:
        plane_shape = (shards, 7, own, tok) if packed else (7, chans, tok)
        outs += [(plane_shape, bf16), ((4, chans, tok), bf16)]
        if post is not None:
            outs += [((chans, tok), f32), ((3, chans, tok), f32)]
    else:
        outs += [((chans, tok), bf16), ((3, chans, tok), bf16)]

    def snorm(x, g):
        return x * lax.rsqrt(jnp.mean(x * x, axis=0, keepdims=True) + 1e-05) * g

    def vnorm(xs, g):
        total = sum(jnp.sum(x * x, axis=0, keepdims=True) for x in xs)
        scale = lax.rsqrt(total / (3 * chans) + 1e-05)
        return [x * scale * g for x in xs]

    def mm(w, x):
        return jnp.dot(w, x, preferred_element_type=f32)

    def kernel(*refs):
        refs = list(refs)
        ss_ref, sv_ref = refs.pop(0), refs.pop(0)
        ss = ss_ref[...].astype(f32)
        sv = [sv_ref[j].astype(f32) for j in range(3)]
        if post is not None:
            conv_ref, q_ref = refs.pop(0), refs.pop(0)
            wos, wov, wup, wdn, wmx, wgt, gp = [refs.pop(0) for _ in range(7)]
            g = gp[...].T
            qs = q_ref[0].astype(f32)
            if packed:
                planes = [jnp.concatenate([conv_ref[d, p] for d in range(shards)], axis=0) for p in range(4)]
            else:
                planes = [conv_ref[p] for p in range(4)]
            ys = planes[0].astype(f32)
            yv = [planes[1 + j].astype(f32) for j in range(3)]
            mix = q_ref[1].astype(f32) * yv[0]
            mix = mix + q_ref[2].astype(f32) * yv[1]
            mix = mix + q_ref[3].astype(f32) * yv[2]
            out_s = (qs * ys + mix).astype(bf16)
            ss = ss + mm(wos[...], out_s)
            sv = [sv[j] + mm(wov[...], (qs * yv[j]).astype(bf16)) for j in range(3)]
            mlp_s = snorm(ss, g[:, 2:3]).astype(bf16)
            mlp_v = [v.astype(bf16) for v in vnorm(sv, g[:, 3:4])]
            hidden = gelu_tanh(mm(wup[...], mlp_s)).astype(bf16)
            gate = 1.0 / (1.0 + jnp.exp(-mm(wgt[...], mlp_s)))
            ss = ss + mm(wdn[...], hidden)
            sv = [sv[j] + mm(wmx[...], mlp_v[j]) * gate for j in range(3)]
        if pre is not None:
            wqs, wqv, gq = [refs.pop(0) for _ in range(3)]
            g = gq[...].T
            planes_ref, query_ref = refs.pop(0), refs.pop(0)

            def put(p, value):
                if packed:
                    for d in range(shards):
                        planes_ref[d, p] = value[d * own : (d + 1) * own]
                else:
                    planes_ref[p] = value

            normed_s = snorm(ss, g[:, 0:1]).astype(bf16)
            normed_v = [v.astype(bf16) for v in vnorm(sv, g[:, 1:2])]
            ps = mm(wqs[...], normed_s)
            query_ref[0] = ps[:chans].astype(bf16)
            put(0, (ps[chans : 2 * chans] * ps[2 * chans :]).astype(bf16))
            for j in range(3):
                pv = mm(wqv[...], normed_v[j]).astype(bf16)
                query_ref[1 + j] = pv[:chans]
                put(1 + j, pv[chans : 2 * chans])
                put(4 + j, pv[2 * chans :])
            if post is not None:
                ns_ref, nv_ref = refs.pop(0), refs.pop(0)
                ns_ref[...] = ss
                for j in range(3):
                    nv_ref[j] = sv[j]
        else:
            os_ref, ov_ref = refs.pop(0), refs.pop(0)
            os_ref[...] = ss.astype(bf16)
            for j in range(3):
                ov_ref[j] = sv[j].astype(bf16)

    return pl.pallas_call(
        kernel,
        grid=(1,),
        in_specs=specs,
        out_specs=[full(shape) for shape, _ in outs],
        out_shape=[jax.ShapeDtypeStruct(shape, dtype) for shape, dtype in outs],
    )(*ins)


def per_device(
    scalars,
    vectors,
    w_qkw_s,
    w_qkw_v,
    w_out_s,
    w_out_v,
    w_up,
    w_down,
    w_mix,
    w_gate,
    gains,
    pe_w1,
    pe_w2,
    pe_w3,
    rates,
):
    chans = scalars.shape[0]
    tok_local = scalars.shape[1]
    shards = lax.axis_size("seq")
    rank = lax.axis_index("seq")
    length = tok_local * shards
    own = chans // shards
    depth = w_qkw_s.shape[0]
    tables = make_tables(shards, tok_local)
    positions = jnp.arange(length, dtype=jnp.int32)

    def filter_spec(first, second, third, decay):
        third = lax.dynamic_slice_in_dim(third, rank * own, own, axis=0)
        decay = lax.dynamic_slice_in_dim(decay, rank * own, own, axis=0)
        made = filter_values(positions, length, first, second, third, decay)
        made = made.reshape(own, shards, tok_local).transpose(1, 0, 2)
        return forward_dft(made[:, None].astype(jnp.float32), tables, FAST)[:, 0]

    weights = {
        "w_qkw_s": w_qkw_s,
        "w_qkw_v": w_qkw_v,
        "w_out_s": w_out_s,
        "w_out_v": w_out_v,
        "w_up": w_up,
        "w_down": w_down,
        "w_mix": w_mix,
        "w_gate": w_gate,
        "gains_t": gains,
    }
    arrays = {"state_s": scalars, "state_v": vectors}
    packed = own % 16 == 0
    planes, query = token_step(None, 0, arrays, weights, shards)
    tied = lax.optimization_barrier((pe_w1[0], pe_w2[0], pe_w3[0], rates[0], planes))
    spec_next = filter_spec(*tied[:4])
    for layer in range(depth):
        outgoing = planes
        if not packed:
            outgoing = planes.reshape(7, shards, own, tok_local).transpose(1, 0, 2, 3)
        regrouped = lax.all_to_all(outgoing, "seq", 0, 0, tiled=True)
        convolved = convolve(regrouped, spec_next, tables)
        returned = lax.all_to_all(convolved, "seq", 0, 0, tiled=True)
        arrays["conv"] = returned
        if not packed:
            arrays["conv"] = returned.transpose(1, 0, 2, 3).reshape(4, chans, tok_local)
        arrays["query"] = query
        if layer + 1 < depth:
            planes, query, new_s, new_v = token_step(layer, layer + 1, arrays, weights, shards)
            tied = lax.optimization_barrier(
                (pe_w1[layer + 1], pe_w2[layer + 1], pe_w3[layer + 1], rates[layer + 1], planes)
            )
            spec_next = filter_spec(*tied[:4])
            arrays["state_s"], arrays["state_v"] = new_s, new_v
        else:
            return tuple(token_step(layer, None, arrays, weights, shards))


def solution(mesh):
    in_specs = (
        P(None, ("grp", "seq")),
        P(None, None, ("grp", "seq")),
        P(),
        P(),
        P(),
        P(),
        P(),
        P(),
        P(),
        P(),
        P(),
        P(),
        P(),
        P(),
        P(),
    )
    out_specs = (P(None, ("grp", "seq")), P(None, None, ("grp", "seq")))
    return jax.shard_map(
        per_device, mesh=mesh, in_specs=in_specs, out_specs=out_specs, check_vma=False
    )
```

```python
import math

import jax
import jax.numpy as jnp
import numpy as np
from jax import lax
from jax.experimental import pallas as pl
from jax.sharding import PartitionSpec as P

HIGH = lax.Precision.HIGHEST
FAST = lax.Precision.DEFAULT


def filter_values(positions, length, first, second, third, decay):
    count = first.shape[1] // 2
    freqs = jnp.arange(1, count + 1, dtype=jnp.int32)
    turns = freqs[:, None] * positions[None, :] % length
    angle = turns.astype(jnp.float32) * (2.0 * math.pi / length)
    feats = jnp.concatenate([jnp.cos(angle), jnp.sin(angle)], axis=0)
    hid_one = jnp.sin(jnp.dot(first, feats, precision=HIGH))
    hid_two = jnp.sin(jnp.dot(second, hid_one, precision=HIGH))
    raw = jnp.dot(third, hid_two, precision=HIGH)
    envelope = jnp.exp(-decay[:, None] * positions[None, :].astype(jnp.float32) / length)
    return (raw * envelope / math.sqrt(length)).astype(jnp.bfloat16)


def scalar_norm(field, gain):
    return field * lax.rsqrt(jnp.mean(field * field, axis=0, keepdims=True) + 1e-05) * gain[:, None]


def vector_norm(field, gain):
    return (
        field
        * lax.rsqrt(jnp.mean(field * field, axis=(0, 1), keepdims=True) + 1e-05)
        * gain[None, :, None]
    )


def make_tables(shards, local):
    length = shards * local
    f32, bf16 = jnp.float32, jnp.bfloat16

    def turns(rows, cols, period):
        rows = jnp.arange(rows, dtype=jnp.int32)[:, None]
        cols = jnp.arange(cols, dtype=jnp.int32)[None, :]
        return ((rows * cols) % period).astype(f32) * (2.0 * math.pi / period)

    half = shards // 2 + 1 if shards % 2 == 0 else shards
    ang_s = turns(half, shards, shards)
    cos_s, sin_s = jnp.cos(ang_s), jnp.sin(ang_s)
    lead_fwd = jnp.concatenate([cos_s, -sin_s], axis=0)
    if half == shards:
        weight = jnp.ones((half,), f32)
    else:
        weight = jnp.full((half,), 2.0, f32).at[0].set(1.0).at[half - 1].set(1.0)
    weight = weight / length
    lead_inv = jnp.concatenate([cos_s.T * weight, -sin_s.T * weight], axis=1)
    ang_t = turns(half, local, length)
    tw_c = jnp.cos(ang_t)[:, None, None, :]
    tw_s = jnp.sin(ang_t)[:, None, None, :]
    ang_l = turns(local, local, local)
    cos_l, sin_l = jnp.cos(ang_l), jnp.sin(ang_l)
    lane_fwd = jnp.block([[cos_l, -sin_l], [sin_l, cos_l]])
    lane_inv = jnp.block([[cos_l, sin_l], [-sin_l, cos_l]])
    return (
        lead_fwd.astype(bf16),
        lead_inv.astype(bf16),
        tw_c,
        tw_s,
        lane_fwd.astype(bf16),
        lane_inv.astype(bf16),
    )


def forward_dft(field, tables, prec):
    lead_fwd, _, tw_c, tw_s, lane_fwd, _ = tables
    shards, planes, chans, local = field.shape
    flat = field.reshape(shards, -1).astype(jnp.bfloat16)
    stage = jnp.dot(lead_fwd, flat, preferred_element_type=jnp.float32)
    half = lead_fwd.shape[0] // 2
    stage = stage.reshape(2 * half, planes, chans, local)
    st_r, st_i = stage[:half], stage[half:]
    tw_r = st_r * tw_c + st_i * tw_s
    tw_i = st_i * tw_c - st_r * tw_s
    joined = jnp.concatenate([tw_r, tw_i], axis=-1).reshape(-1, 2 * local).astype(jnp.bfloat16)
    spec = jnp.dot(joined, lane_fwd, preferred_element_type=jnp.float32)
    return spec.reshape(half, planes, chans, 2 * local)


def inverse_dft(spec, tables, prec):
    _, lead_inv, tw_c, tw_s, _, lane_inv = tables
    half, planes, chans, width = spec.shape
    shards = lead_inv.shape[0]
    local = width // 2
    flat = spec.reshape(-1, width).astype(jnp.bfloat16)
    back = jnp.dot(flat, lane_inv, preferred_element_type=jnp.float32)
    back = back.reshape(half, planes, chans, width)
    bk_r, bk_i = back[..., :local], back[..., local:]
    un_r = bk_r * tw_c - bk_i * tw_s
    un_i = bk_r * tw_s + bk_i * tw_c
    stacked = jnp.concatenate([un_r, un_i], axis=0).reshape(2 * half, -1).astype(jnp.bfloat16)
    whole = jnp.dot(lead_inv, stacked, preferred_element_type=jnp.float32)
    return whole.reshape(shards, planes, chans, local)


def cmul(a_r, a_i, b_r, b_i):
    return a_r * b_r - a_i * b_i, a_r * b_i + a_i * b_r


def convolve(received, filt_spec, tables):
    shards, _, chans, local = received.shape
    length = shards * local
    spec = forward_dft(received.astype(jnp.float32), tables, FAST)
    re, im = spec[..., :local], spec[..., local:]
    h_r, h_i = filt_spec[..., :local], filt_spec[..., local:]
    inv_root = 1.0 / math.sqrt(length)
    p_r, p_i = cmul(re[:, 0], im[:, 0], h_r, h_i)
    outs_r, outs_i = [p_r], [p_i]
    for j in range(3):
        one, two = (j + 1) % 3, (j + 2) % 3
        a_r, a_i = cmul(re[:, 1 + one], im[:, 1 + one], re[:, 4 + two], im[:, 4 + two])
        b_r, b_i = cmul(re[:, 1 + two], im[:, 1 + two], re[:, 4 + one], im[:, 4 + one])
        outs_r.append((a_r - b_r) * inv_root)
        outs_i.append((a_i - b_i) * inv_root)
    prod = jnp.concatenate([jnp.stack(outs_r, axis=1), jnp.stack(outs_i, axis=1)], axis=-1)
    return inverse_dft(prod, tables, FAST).astype(jnp.bfloat16)


def gelu_tanh(x):
    return 0.5 * x * (1.0 + jnp.tanh(math.sqrt(2.0 / math.pi) * (x + 0.044715 * (x * x * x))))


def token_step(post, pre, arrays, weights, shards):
    f32, bf16 = jnp.float32, jnp.bfloat16
    state_s, state_v = arrays["state_s"], arrays["state_v"]
    chans, tok = state_s.shape
    own = chans // shards
    packed = own % 16 == 0
    full = lambda shape: pl.BlockSpec(shape, lambda i, n=len(shape): (0,) * n)

    def layer_spec(w, layer):
        return pl.BlockSpec((pl.Squeezed(),) + w.shape[1:], lambda i: (layer,) + (0,) * (w.ndim - 1))

    def row_spec(w, layer, rows, block):
        return pl.BlockSpec((pl.Squeezed(), rows, w.shape[2]), lambda i: (layer, block, 0))

    ins, specs = [state_s, state_v], [full(state_s.shape), full(state_v.shape)]
    post_names = ("w_out_s", "w_out_v", "w_up", "w_down", "w_mix", "w_gate")
    if post is not None:
        ins += [arrays["conv"], arrays["query"]]
        specs += [full(arrays["conv"].shape), full(arrays["query"].shape)]
        for name in post_names + ("gains_t",):
            ins.append(weights[name])
            specs.append(layer_spec(weights[name], post))
    if pre is not None:
        for name in ("w_qkw_s", "w_qkw_v"):
            for block in (1, 2):
                ins.append(weights[name])
                specs.append(row_spec(weights[name], pre, chans, block))
        ins.append(weights["gains_t"])
        specs.append(layer_spec(weights["gains_t"], pre))
    outs = []
    if pre is not None:
        plane_shape = (shards, 7, own, tok) if packed else (7, chans, tok)
        outs += [(plane_shape, bf16)]
        if post is not None:
            outs += [((chans, tok), f32), ((3, chans, tok), f32)]
    else:
        outs += [((chans, tok), bf16), ((3, chans, tok), bf16)]

    def snorm(x, g):
        return x * lax.rsqrt(jnp.mean(x * x, axis=0, keepdims=True) + 1e-05) * g

    def vnorm(xs, g):
        total = sum(jnp.sum(x * x, axis=0, keepdims=True) for x in xs)
        scale = lax.rsqrt(total / (3 * chans) + 1e-05)
        return [x * scale * g for x in xs]

    def mm(w, x):
        return jnp.dot(w, x, preferred_element_type=f32)

    def kernel(*refs):
        refs = list(refs)
        ss_ref, sv_ref = refs.pop(0), refs.pop(0)
        ss = ss_ref[...].astype(f32)
        sv = [sv_ref[j].astype(f32) for j in range(3)]
        if post is not None:
            conv_ref, q_ref = refs.pop(0), refs.pop(0)
            wos, wov, wup, wdn, wmx, wgt, gp = [refs.pop(0) for _ in range(7)]
            g = gp[...].T
            qs = q_ref[0].astype(f32)
            if packed:
                planes = [jnp.concatenate([conv_ref[d, p] for d in range(shards)], axis=0) for p in range(4)]
            else:
                planes = [conv_ref[p] for p in range(4)]
            ys = planes[0].astype(f32)
            yv = [planes[1 + j].astype(f32) for j in range(3)]
            mix = q_ref[1].astype(f32) * yv[0]
            mix = mix + q_ref[2].astype(f32) * yv[1]
            mix = mix + q_ref[3].astype(f32) * yv[2]
            out_s = (qs * ys + mix).astype(bf16)
            ss = ss + mm(wos[...], out_s)
            sv = [sv[j] + mm(wov[...], (qs * yv[j]).astype(bf16)) for j in range(3)]
            mlp_s = snorm(ss, g[:, 2:3]).astype(bf16)
            mlp_v = [v.astype(bf16) for v in vnorm(sv, g[:, 3:4])]
            hidden = gelu_tanh(mm(wup[...], mlp_s)).astype(bf16)
            gate = 1.0 / (1.0 + jnp.exp(-mm(wgt[...], mlp_s)))
            ss = ss + mm(wdn[...], hidden)
            sv = [sv[j] + mm(wmx[...], mlp_v[j]) * gate for j in range(3)]
        if pre is not None:
            wqs_k, wqs_w, wqv_k, wqv_w, gq = [refs.pop(0) for _ in range(5)]
            g = gq[...].T
            planes_ref = refs.pop(0)

            def put(p, value):
                if packed:
                    for d in range(shards):
                        planes_ref[d, p] = value[d * own : (d + 1) * own]
                else:
                    planes_ref[p] = value

            normed_s = snorm(ss, g[:, 0:1]).astype(bf16)
            normed_v = [v.astype(bf16) for v in vnorm(sv, g[:, 1:2])]
            put(0, (mm(wqs_k[...], normed_s) * mm(wqs_w[...], normed_s)).astype(bf16))
            for j in range(3):
                put(1 + j, mm(wqv_k[...], normed_v[j]).astype(bf16))
                put(4 + j, mm(wqv_w[...], normed_v[j]).astype(bf16))
            if post is not None:
                ns_ref, nv_ref = refs.pop(0), refs.pop(0)
                ns_ref[...] = ss
                for j in range(3):
                    nv_ref[j] = sv[j]
        else:
            os_ref, ov_ref = refs.pop(0), refs.pop(0)
            os_ref[...] = ss.astype(bf16)
            for j in range(3):
                ov_ref[j] = sv[j].astype(bf16)

    return pl.pallas_call(
        kernel,
        grid=(1,),
        in_specs=specs,
        out_specs=[full(shape) for shape, _ in outs],
        out_shape=[jax.ShapeDtypeStruct(shape, dtype) for shape, dtype in outs],
    )(*ins)


def query_step(layer, state_s, state_v, weights):
    f32, bf16 = jnp.float32, jnp.bfloat16
    chans, tok = state_s.shape
    w_s, w_v, gains = weights["w_qkw_s"], weights["w_qkw_v"], weights["gains_t"]
    full = lambda shape: pl.BlockSpec(shape, lambda i, n=len(shape): (0,) * n)
    rows = lambda w: pl.BlockSpec((pl.Squeezed(), chans, w.shape[2]), lambda i: (layer, 0, 0))
    g_spec = pl.BlockSpec((pl.Squeezed(),) + gains.shape[1:], lambda i: (layer, 0, 0))

    def kernel(ss_ref, sv_ref, ws_ref, wv_ref, g_ref, q_ref):
        g = g_ref[...].T
        ss = ss_ref[...].astype(f32)
        sv = [sv_ref[j].astype(f32) for j in range(3)]
        normed_s = (ss * lax.rsqrt(jnp.mean(ss * ss, axis=0, keepdims=True) + 1e-05) * g[:, 0:1]).astype(bf16)
        total = sum(jnp.sum(x * x, axis=0, keepdims=True) for x in sv)
        scale = lax.rsqrt(total / (3 * chans) + 1e-05)
        q_ref[0] = jnp.dot(ws_ref[...], normed_s, preferred_element_type=f32).astype(bf16)
        for j in range(3):
            normed = (sv[j] * scale * g[:, 1:2]).astype(bf16)
            q_ref[1 + j] = jnp.dot(wv_ref[...], normed, preferred_element_type=f32).astype(bf16)

    return pl.pallas_call(
        kernel,
        grid=(1,),
        in_specs=[full(state_s.shape), full(state_v.shape), rows(w_s), rows(w_v), g_spec],
        out_specs=full((4, chans, tok)),
        out_shape=jax.ShapeDtypeStruct((4, chans, tok), bf16),
    )(state_s, state_v, w_s, w_v, gains)


def per_device(
    scalars,
    vectors,
    w_qkw_s,
    w_qkw_v,
    w_out_s,
    w_out_v,
    w_up,
    w_down,
    w_mix,
    w_gate,
    gains,
    pe_w1,
    pe_w2,
    pe_w3,
    rates,
):
    chans = scalars.shape[0]
    tok_local = scalars.shape[1]
    shards = lax.axis_size("seq")
    rank = lax.axis_index("seq")
    length = tok_local * shards
    own = chans // shards
    depth = w_qkw_s.shape[0]
    tables = make_tables(shards, tok_local)
    positions = jnp.arange(length, dtype=jnp.int32)

    def filter_spec(first, second, third, decay):
        third = lax.dynamic_slice_in_dim(third, rank * own, own, axis=0)
        decay = lax.dynamic_slice_in_dim(decay, rank * own, own, axis=0)
        made = filter_values(positions, length, first, second, third, decay)
        made = made.reshape(own, shards, tok_local).transpose(1, 0, 2)
        return forward_dft(made[:, None].astype(jnp.float32), tables, FAST)[:, 0]

    weights = {
        "w_qkw_s": w_qkw_s,
        "w_qkw_v": w_qkw_v,
        "w_out_s": w_out_s,
        "w_out_v": w_out_v,
        "w_up": w_up,
        "w_down": w_down,
        "w_mix": w_mix,
        "w_gate": w_gate,
        "gains_t": gains,
    }
    arrays = {"state_s": scalars, "state_v": vectors}
    packed = own % 16 == 0
    (planes,) = token_step(None, 0, arrays, weights, shards)
    tied = lax.optimization_barrier((scalars, vectors, planes))
    query = query_step(0, tied[0], tied[1], weights)
    tied = lax.optimization_barrier((pe_w1[0], pe_w2[0], pe_w3[0], rates[0], planes))
    spec_next = filter_spec(*tied[:4])
    for layer in range(depth):
        outgoing = planes
        if not packed:
            outgoing = planes.reshape(7, shards, own, tok_local).transpose(1, 0, 2, 3)
        regrouped = lax.all_to_all(outgoing, "seq", 0, 0, tiled=True)
        regrouped, query = lax.optimization_barrier((regrouped, query))
        convolved = convolve(regrouped, spec_next, tables)
        returned = lax.all_to_all(convolved, "seq", 0, 0, tiled=True)
        arrays["conv"] = returned
        if not packed:
            arrays["conv"] = returned.transpose(1, 0, 2, 3).reshape(4, chans, tok_local)
        arrays["query"] = query
        if layer + 1 < depth:
            planes, new_s, new_v = token_step(layer, layer + 1, arrays, weights, shards)
            query = query_step(layer + 1, new_s, new_v, weights)
            tied = lax.optimization_barrier(
                (pe_w1[layer + 1], pe_w2[layer + 1], pe_w3[layer + 1], rates[layer + 1], planes)
            )
            spec_next = filter_spec(*tied[:4])
            arrays["state_s"], arrays["state_v"] = new_s, new_v
        else:
            return tuple(token_step(layer, None, arrays, weights, shards))


def solution(mesh):
    in_specs = (
        P(None, ("grp", "seq")),
        P(None, None, ("grp", "seq")),
        P(),
        P(),
        P(),
        P(),
        P(),
        P(),
        P(),
        P(),
        P(),
        P(),
        P(),
        P(),
        P(),
    )
    out_specs = (P(None, ("grp", "seq")), P(None, None, ("grp", "seq")))
    return jax.shard_map(
        per_device, mesh=mesh, in_specs=in_specs, out_specs=out_specs, check_vma=False
    )
```

```python
import math

import jax
import jax.numpy as jnp
import numpy as np
from jax import lax
from jax.experimental import pallas as pl
from jax.sharding import PartitionSpec as P

HIGH = lax.Precision.HIGHEST
FAST = lax.Precision.DEFAULT


def filter_values(positions, length, first, second, third, decay):
    count = first.shape[1] // 2
    freqs = jnp.arange(1, count + 1, dtype=jnp.int32)
    turns = freqs[:, None] * positions[None, :] % length
    angle = turns.astype(jnp.float32) * (2.0 * math.pi / length)
    feats = jnp.concatenate([jnp.cos(angle), jnp.sin(angle)], axis=0)
    hid_one = jnp.sin(jnp.dot(first, feats, precision=HIGH))
    hid_two = jnp.sin(jnp.dot(second, hid_one, precision=HIGH))
    raw = jnp.dot(third, hid_two, precision=HIGH)
    envelope = jnp.exp(-decay[:, None] * positions[None, :].astype(jnp.float32) / length)
    return (raw * envelope / math.sqrt(length)).astype(jnp.bfloat16)


def scalar_norm(field, gain):
    return field * lax.rsqrt(jnp.mean(field * field, axis=0, keepdims=True) + 1e-05) * gain[:, None]


def vector_norm(field, gain):
    return (
        field
        * lax.rsqrt(jnp.mean(field * field, axis=(0, 1), keepdims=True) + 1e-05)
        * gain[None, :, None]
    )


def make_tables(shards, local):
    length = shards * local
    f32, bf16 = jnp.float32, jnp.bfloat16

    def turns(rows, cols, period):
        rows = jnp.arange(rows, dtype=jnp.int32)[:, None]
        cols = jnp.arange(cols, dtype=jnp.int32)[None, :]
        return ((rows * cols) % period).astype(f32) * (2.0 * math.pi / period)

    half = shards // 2 + 1 if shards % 2 == 0 else shards
    ang_s = turns(half, shards, shards)
    cos_s, sin_s = jnp.cos(ang_s), jnp.sin(ang_s)
    lead_fwd = jnp.concatenate([cos_s, -sin_s], axis=0)
    if half == shards:
        weight = jnp.ones((half,), f32)
    else:
        weight = jnp.full((half,), 2.0, f32).at[0].set(1.0).at[half - 1].set(1.0)
    weight = weight / length
    lead_inv = jnp.concatenate([cos_s.T * weight, -sin_s.T * weight], axis=1)
    ang_t = turns(half, local, length)
    tw_c = jnp.cos(ang_t)[:, None, None, :]
    tw_s = jnp.sin(ang_t)[:, None, None, :]
    ang_l = turns(local, local, local)
    cos_l, sin_l = jnp.cos(ang_l), jnp.sin(ang_l)
    lane_fwd = jnp.block([[cos_l, -sin_l], [sin_l, cos_l]])
    lane_inv = jnp.block([[cos_l, sin_l], [-sin_l, cos_l]])
    return (
        lead_fwd.astype(bf16),
        lead_inv.astype(bf16),
        tw_c,
        tw_s,
        lane_fwd.astype(bf16),
        lane_inv.astype(bf16),
    )


def forward_dft(field, tables, prec):
    lead_fwd, _, tw_c, tw_s, lane_fwd, _ = tables
    shards, planes, chans, local = field.shape
    flat = field.reshape(shards, -1).astype(jnp.bfloat16)
    half = lead_fwd.shape[0] // 2
    st_r = jnp.dot(lead_fwd[:half], flat, preferred_element_type=jnp.float32)
    st_i = jnp.dot(lead_fwd[half:], flat, preferred_element_type=jnp.float32)
    st_r = st_r.reshape(half, planes, chans, local)
    st_i = st_i.reshape(half, planes, chans, local)
    tw_r = st_r * tw_c + st_i * tw_s
    tw_i = st_i * tw_c - st_r * tw_s
    joined = jnp.concatenate([tw_r, tw_i], axis=-1).reshape(-1, 2 * local).astype(jnp.bfloat16)
    spec = jnp.dot(joined, lane_fwd, preferred_element_type=jnp.float32)
    return spec.reshape(half, planes, chans, 2 * local)


def inverse_dft(spec, tables, prec):
    _, lead_inv, tw_c, tw_s, _, lane_inv = tables
    half, planes, chans, width = spec.shape
    shards = lead_inv.shape[0]
    local = width // 2
    flat = spec.reshape(-1, width).astype(jnp.bfloat16)
    back = jnp.dot(flat, lane_inv, preferred_element_type=jnp.float32)
    back = back.reshape(half, planes, chans, width)
    bk_r, bk_i = back[..., :local], back[..., local:]
    un_r = bk_r * tw_c - bk_i * tw_s
    un_i = bk_r * tw_s + bk_i * tw_c
    un_r = un_r.reshape(half, -1).astype(jnp.bfloat16)
    un_i = un_i.reshape(half, -1).astype(jnp.bfloat16)
    whole = jnp.dot(lead_inv[:, :half], un_r, preferred_element_type=jnp.float32)
    whole = whole + jnp.dot(lead_inv[:, half:], un_i, preferred_element_type=jnp.float32)
    return whole.reshape(shards, planes, chans, local)


def cmul(a_r, a_i, b_r, b_i):
    return a_r * b_r - a_i * b_i, a_r * b_i + a_i * b_r


def convolve(received, filt_spec, tables):
    shards, _, chans, local = received.shape
    length = shards * local
    spec = forward_dft(received.astype(jnp.float32), tables, FAST)
    re, im = spec[..., :local], spec[..., local:]
    h_r, h_i = filt_spec[..., :local], filt_spec[..., local:]
    inv_root = 1.0 / math.sqrt(length)
    p_r, p_i = cmul(re[:, 0], im[:, 0], h_r, h_i)
    outs_r, outs_i = [p_r], [p_i]
    for j in range(3):
        one, two = (j + 1) % 3, (j + 2) % 3
        a_r, a_i = cmul(re[:, 1 + one], im[:, 1 + one], re[:, 4 + two], im[:, 4 + two])
        b_r, b_i = cmul(re[:, 1 + two], im[:, 1 + two], re[:, 4 + one], im[:, 4 + one])
        outs_r.append((a_r - b_r) * inv_root)
        outs_i.append((a_i - b_i) * inv_root)
    prod = jnp.concatenate([jnp.stack(outs_r, axis=1), jnp.stack(outs_i, axis=1)], axis=-1)
    return inverse_dft(prod, tables, FAST).astype(jnp.bfloat16)


def gelu_tanh(x):
    return 0.5 * x * (1.0 + jnp.tanh(math.sqrt(2.0 / math.pi) * (x + 0.044715 * (x * x * x))))


def token_step(post, pre, arrays, weights, shards):
    f32, bf16 = jnp.float32, jnp.bfloat16
    state_s, state_v = arrays["state_s"], arrays["state_v"]
    chans, tok = state_s.shape
    own = chans // shards
    packed = own % 16 == 0
    full = lambda shape: pl.BlockSpec(shape, lambda i, n=len(shape): (0,) * n)

    def layer_spec(w, layer):
        return pl.BlockSpec((pl.Squeezed(),) + w.shape[1:], lambda i: (layer,) + (0,) * (w.ndim - 1))

    def row_spec(w, layer, rows, block):
        return pl.BlockSpec((pl.Squeezed(), rows, w.shape[2]), lambda i: (layer, block, 0))

    ins, specs = [state_s, state_v], [full(state_s.shape), full(state_v.shape)]
    post_names = ("w_out_s", "w_out_v", "w_up", "w_down", "w_mix", "w_gate")
    if post is not None:
        ins += [arrays["conv"], arrays["query"]]
        specs += [full(arrays["conv"].shape), full(arrays["query"].shape)]
        for name in post_names + ("gains_t",):
            ins.append(weights[name])
            specs.append(layer_spec(weights[name], post))
    if pre is not None:
        for name in ("w_qkw_s", "w_qkw_v"):
            for block in (1, 2):
                ins.append(weights[name])
                specs.append(row_spec(weights[name], pre, chans, block))
        ins.append(weights["gains_t"])
        specs.append(layer_spec(weights["gains_t"], pre))
    outs = []
    if pre is not None:
        plane_shape = (shards, 7, own, tok) if packed else (7, chans, tok)
        outs += [(plane_shape, bf16)]
        if post is not None:
            outs += [((chans, tok), f32), ((3, chans, tok), f32)]
    else:
        outs += [((chans, tok), bf16), ((3, chans, tok), bf16)]

    def snorm(x, g):
        return x * lax.rsqrt(jnp.mean(x * x, axis=0, keepdims=True) + 1e-05) * g

    def vnorm(xs, g):
        total = sum(jnp.sum(x * x, axis=0, keepdims=True) for x in xs)
        scale = lax.rsqrt(total / (3 * chans) + 1e-05)
        return [x * scale * g for x in xs]

    def mm(w, x):
        return jnp.dot(w, x, preferred_element_type=f32)

    def kernel(*refs):
        refs = list(refs)
        ss_ref, sv_ref = refs.pop(0), refs.pop(0)
        ss = ss_ref[...].astype(f32)
        sv = [sv_ref[j].astype(f32) for j in range(3)]
        if post is not None:
            conv_ref, q_ref = refs.pop(0), refs.pop(0)
            wos, wov, wup, wdn, wmx, wgt, gp = [refs.pop(0) for _ in range(7)]
            g = gp[...].T
            qs = q_ref[0].astype(f32)
            if packed:
                planes = [jnp.concatenate([conv_ref[d, p] for d in range(shards)], axis=0) for p in range(4)]
            else:
                planes = [conv_ref[p] for p in range(4)]
            ys = planes[0].astype(f32)
            yv = [planes[1 + j].astype(f32) for j in range(3)]
            mix = q_ref[1].astype(f32) * yv[0]
            mix = mix + q_ref[2].astype(f32) * yv[1]
            mix = mix + q_ref[3].astype(f32) * yv[2]
            out_s = (qs * ys + mix).astype(bf16)
            ss = ss + mm(wos[...], out_s)
            sv = [sv[j] + mm(wov[...], (qs * yv[j]).astype(bf16)) for j in range(3)]
            mlp_s = snorm(ss, g[:, 2:3]).astype(bf16)
            mlp_v = [v.astype(bf16) for v in vnorm(sv, g[:, 3:4])]
            hidden = gelu_tanh(mm(wup[...], mlp_s)).astype(bf16)
            gate = 1.0 / (1.0 + jnp.exp(-mm(wgt[...], mlp_s)))
            ss = ss + mm(wdn[...], hidden)
            sv = [sv[j] + mm(wmx[...], mlp_v[j]) * gate for j in range(3)]
        if pre is not None:
            wqs_k, wqs_w, wqv_k, wqv_w, gq = [refs.pop(0) for _ in range(5)]
            g = gq[...].T
            planes_ref = refs.pop(0)

            def put(p, value):
                if packed:
                    for d in range(shards):
                        planes_ref[d, p] = value[d * own : (d + 1) * own]
                else:
                    planes_ref[p] = value

            normed_s = snorm(ss, g[:, 0:1]).astype(bf16)
            normed_v = [v.astype(bf16) for v in vnorm(sv, g[:, 1:2])]
            put(0, (mm(wqs_k[...], normed_s) * mm(wqs_w[...], normed_s)).astype(bf16))
            for j in range(3):
                put(1 + j, mm(wqv_k[...], normed_v[j]).astype(bf16))
                put(4 + j, mm(wqv_w[...], normed_v[j]).astype(bf16))
            if post is not None:
                ns_ref, nv_ref = refs.pop(0), refs.pop(0)
                ns_ref[...] = ss
                for j in range(3):
                    nv_ref[j] = sv[j]
        else:
            os_ref, ov_ref = refs.pop(0), refs.pop(0)
            os_ref[...] = ss.astype(bf16)
            for j in range(3):
                ov_ref[j] = sv[j].astype(bf16)

    return pl.pallas_call(
        kernel,
        grid=(1,),
        in_specs=specs,
        out_specs=[full(shape) for shape, _ in outs],
        out_shape=[jax.ShapeDtypeStruct(shape, dtype) for shape, dtype in outs],
    )(*ins)


def query_step(layer, state_s, state_v, weights):
    f32, bf16 = jnp.float32, jnp.bfloat16
    chans, tok = state_s.shape
    w_s, w_v, gains = weights["w_qkw_s"], weights["w_qkw_v"], weights["gains_t"]
    full = lambda shape: pl.BlockSpec(shape, lambda i, n=len(shape): (0,) * n)
    rows = lambda w: pl.BlockSpec((pl.Squeezed(), chans, w.shape[2]), lambda i: (layer, 0, 0))
    g_spec = pl.BlockSpec((pl.Squeezed(),) + gains.shape[1:], lambda i: (layer, 0, 0))

    def kernel(ss_ref, sv_ref, ws_ref, wv_ref, g_ref, q_ref):
        g = g_ref[...].T
        ss = ss_ref[...].astype(f32)
        sv = [sv_ref[j].astype(f32) for j in range(3)]
        normed_s = (ss * lax.rsqrt(jnp.mean(ss * ss, axis=0, keepdims=True) + 1e-05) * g[:, 0:1]).astype(bf16)
        total = sum(jnp.sum(x * x, axis=0, keepdims=True) for x in sv)
        scale = lax.rsqrt(total / (3 * chans) + 1e-05)
        q_ref[0] = jnp.dot(ws_ref[...], normed_s, preferred_element_type=f32).astype(bf16)
        for j in range(3):
            normed = (sv[j] * scale * g[:, 1:2]).astype(bf16)
            q_ref[1 + j] = jnp.dot(wv_ref[...], normed, preferred_element_type=f32).astype(bf16)

    return pl.pallas_call(
        kernel,
        grid=(1,),
        in_specs=[full(state_s.shape), full(state_v.shape), rows(w_s), rows(w_v), g_spec],
        out_specs=full((4, chans, tok)),
        out_shape=jax.ShapeDtypeStruct((4, chans, tok), bf16),
    )(state_s, state_v, w_s, w_v, gains)


def per_device(
    scalars,
    vectors,
    w_qkw_s,
    w_qkw_v,
    w_out_s,
    w_out_v,
    w_up,
    w_down,
    w_mix,
    w_gate,
    gains,
    pe_w1,
    pe_w2,
    pe_w3,
    rates,
):
    chans = scalars.shape[0]
    tok_local = scalars.shape[1]
    shards = lax.axis_size("seq")
    rank = lax.axis_index("seq")
    length = tok_local * shards
    own = chans // shards
    depth = w_qkw_s.shape[0]
    tables = make_tables(shards, tok_local)
    positions = jnp.arange(length, dtype=jnp.int32)

    def filter_spec(first, second, third, decay):
        third = lax.dynamic_slice_in_dim(third, rank * own, own, axis=0)
        decay = lax.dynamic_slice_in_dim(decay, rank * own, own, axis=0)
        made = filter_values(positions, length, first, second, third, decay)
        made = made.reshape(own, shards, tok_local).transpose(1, 0, 2)
        return forward_dft(made[:, None].astype(jnp.float32), tables, FAST)[:, 0]

    weights = {
        "w_qkw_s": w_qkw_s,
        "w_qkw_v": w_qkw_v,
        "w_out_s": w_out_s,
        "w_out_v": w_out_v,
        "w_up": w_up,
        "w_down": w_down,
        "w_mix": w_mix,
        "w_gate": w_gate,
        "gains_t": gains,
    }
    arrays = {"state_s": scalars, "state_v": vectors}
    packed = own % 16 == 0
    (planes,) = token_step(None, 0, arrays, weights, shards)
    tied = lax.optimization_barrier((scalars, vectors, planes))
    query = query_step(0, tied[0], tied[1], weights)
    tied = lax.optimization_barrier((pe_w1[0], pe_w2[0], pe_w3[0], rates[0], planes))
    spec_next = filter_spec(*tied[:4])
    for layer in range(depth):
        outgoing = planes
        if not packed:
            outgoing = planes.reshape(7, shards, own, tok_local).transpose(1, 0, 2, 3)
        regrouped = lax.all_to_all(outgoing, "seq", 0, 0, tiled=True)
        regrouped, query = lax.optimization_barrier((regrouped, query))
        convolved = convolve(regrouped, spec_next, tables)
        returned = lax.all_to_all(convolved, "seq", 0, 0, tiled=True)
        arrays["conv"] = returned
        if not packed:
            arrays["conv"] = returned.transpose(1, 0, 2, 3).reshape(4, chans, tok_local)
        arrays["query"] = query
        if layer + 1 < depth:
            planes, new_s, new_v = token_step(layer, layer + 1, arrays, weights, shards)
            query = query_step(layer + 1, new_s, new_v, weights)
            tied = lax.optimization_barrier(
                (pe_w1[layer + 1], pe_w2[layer + 1], pe_w3[layer + 1], rates[layer + 1], planes)
            )
            spec_next = filter_spec(*tied[:4])
            arrays["state_s"], arrays["state_v"] = new_s, new_v
        else:
            return tuple(token_step(layer, None, arrays, weights, shards))


def solution(mesh):
    in_specs = (
        P(None, ("grp", "seq")),
        P(None, None, ("grp", "seq")),
        P(),
        P(),
        P(),
        P(),
        P(),
        P(),
        P(),
        P(),
        P(),
        P(),
        P(),
        P(),
        P(),
    )
    out_specs = (P(None, ("grp", "seq")), P(None, None, ("grp", "seq")))
    return jax.shard_map(
        per_device, mesh=mesh, in_specs=in_specs, out_specs=out_specs, check_vma=False
    )
```

```python
import math

import jax
import jax.numpy as jnp
import numpy as np
from jax import lax
from jax.experimental import pallas as pl
from jax.sharding import PartitionSpec as P

HIGH = lax.Precision.HIGHEST
FAST = lax.Precision.DEFAULT


def filter_values(positions, length, first, second, third, decay):
    count = first.shape[1] // 2
    freqs = jnp.arange(1, count + 1, dtype=jnp.int32)
    turns = freqs[:, None] * positions[None, :] % length
    angle = turns.astype(jnp.float32) * (2.0 * math.pi / length)
    feats = jnp.concatenate([jnp.cos(angle), jnp.sin(angle)], axis=0)
    hid_one = jnp.sin(jnp.dot(first, feats, precision=HIGH))
    hid_two = jnp.sin(jnp.dot(second, hid_one, precision=HIGH))
    raw = jnp.dot(third, hid_two, precision=HIGH)
    envelope = jnp.exp(-decay[:, None] * positions[None, :].astype(jnp.float32) / length)
    return (raw * envelope / math.sqrt(length)).astype(jnp.bfloat16)


def scalar_norm(field, gain):
    return field * lax.rsqrt(jnp.mean(field * field, axis=0, keepdims=True) + 1e-05) * gain[:, None]


def vector_norm(field, gain):
    return (
        field
        * lax.rsqrt(jnp.mean(field * field, axis=(0, 1), keepdims=True) + 1e-05)
        * gain[None, :, None]
    )


def make_tables(shards, local):
    length = shards * local
    f32, bf16 = jnp.float32, jnp.bfloat16

    def turns(rows, cols, period):
        rows = jnp.arange(rows, dtype=jnp.int32)[:, None]
        cols = jnp.arange(cols, dtype=jnp.int32)[None, :]
        return ((rows * cols) % period).astype(f32) * (2.0 * math.pi / period)

    half = shards // 2 + 1 if shards % 2 == 0 else shards
    ang_s = turns(half, shards, shards)
    cos_s, sin_s = jnp.cos(ang_s), jnp.sin(ang_s)
    lead_fwd = jnp.concatenate([cos_s, -sin_s], axis=0)
    if half == shards:
        weight = jnp.ones((half,), f32)
    else:
        weight = jnp.full((half,), 2.0, f32).at[0].set(1.0).at[half - 1].set(1.0)
    weight = weight / length
    lead_inv = jnp.concatenate([cos_s.T * weight, -sin_s.T * weight], axis=1)
    ang_t = turns(half, local, length)
    tw_c = jnp.cos(ang_t)[:, None, None, :]
    tw_s = jnp.sin(ang_t)[:, None, None, :]
    ang_l = turns(local, local, local)
    cos_l, sin_l = jnp.cos(ang_l), jnp.sin(ang_l)
    lane_fwd = jnp.block([[cos_l, -sin_l], [sin_l, cos_l]])
    lane_inv = jnp.block([[cos_l, sin_l], [-sin_l, cos_l]])
    return (
        lead_fwd.astype(bf16),
        lead_inv.astype(bf16),
        tw_c,
        tw_s,
        lane_fwd.astype(bf16),
        lane_inv.astype(bf16),
    )


def forward_dft(field, tables, prec):
    lead_fwd, _, tw_c, tw_s, lane_fwd, _ = tables
    shards, planes, chans, local = field.shape
    flat = field.reshape(shards, -1).astype(jnp.bfloat16)
    stage = jnp.dot(lead_fwd, flat, preferred_element_type=jnp.float32)
    half = lead_fwd.shape[0] // 2
    stage = stage.reshape(2 * half, planes, chans, local)
    st_r, st_i = stage[:half], stage[half:]
    tw_r = st_r * tw_c + st_i * tw_s
    tw_i = st_i * tw_c - st_r * tw_s
    joined = jnp.concatenate([tw_r, tw_i], axis=-1).reshape(-1, 2 * local).astype(jnp.bfloat16)
    spec = jnp.dot(joined, lane_fwd, preferred_element_type=jnp.float32)
    return spec.reshape(half, planes, chans, 2 * local)


def inverse_dft(spec, tables, prec):
    _, lead_inv, tw_c, tw_s, _, lane_inv = tables
    half, planes, chans, width = spec.shape
    shards = lead_inv.shape[0]
    local = width // 2
    flat = spec.reshape(-1, width).astype(jnp.bfloat16)
    back = jnp.dot(flat, lane_inv, preferred_element_type=jnp.float32)
    back = back.reshape(half, planes, chans, width)
    bk_r, bk_i = back[..., :local], back[..., local:]
    un_r = bk_r * tw_c - bk_i * tw_s
    un_i = bk_r * tw_s + bk_i * tw_c
    stacked = jnp.concatenate([un_r, un_i], axis=0).reshape(2 * half, -1).astype(jnp.bfloat16)
    whole = jnp.dot(lead_inv, stacked, preferred_element_type=jnp.float32)
    return whole.reshape(shards, planes, chans, local)


def cmul(a_r, a_i, b_r, b_i):
    return a_r * b_r - a_i * b_i, a_r * b_i + a_i * b_r


def convolve(received, filt_spec, tables):
    shards, _, chans, local = received.shape
    length = shards * local
    spec = forward_dft(received.astype(jnp.float32), tables, FAST)
    re, im = spec[..., :local], spec[..., local:]
    h_r, h_i = filt_spec[..., :local], filt_spec[..., local:]
    inv_root = 1.0 / math.sqrt(length)
    p_r, p_i = cmul(re[:, 0], im[:, 0], h_r, h_i)
    outs_r, outs_i = [p_r], [p_i]
    for j in range(3):
        one, two = (j + 1) % 3, (j + 2) % 3
        a_r, a_i = cmul(re[:, 1 + one], im[:, 1 + one], re[:, 4 + two], im[:, 4 + two])
        b_r, b_i = cmul(re[:, 1 + two], im[:, 1 + two], re[:, 4 + one], im[:, 4 + one])
        outs_r.append((a_r - b_r) * inv_root)
        outs_i.append((a_i - b_i) * inv_root)
    prod = jnp.concatenate([jnp.stack(outs_r, axis=1), jnp.stack(outs_i, axis=1)], axis=-1)
    return inverse_dft(prod, tables, FAST).astype(jnp.bfloat16)


def gelu_tanh(x):
    return 0.5 * x * (1.0 + jnp.tanh(math.sqrt(2.0 / math.pi) * (x + 0.044715 * (x * x * x))))


def token_step(post, pre, arrays, weights, shards):
    f32, bf16 = jnp.float32, jnp.bfloat16
    state_s, state_v = arrays["state_s"], arrays["state_v"]
    chans, tok = state_s.shape
    own = chans // shards
    packed = own % 16 == 0
    full = lambda shape: pl.BlockSpec(shape, lambda i, n=len(shape): (0,) * n)

    def layer_spec(w, layer):
        return pl.BlockSpec((pl.Squeezed(),) + w.shape[1:], lambda i: (layer,) + (0,) * (w.ndim - 1))

    def row_spec(w, layer, rows, block):
        return pl.BlockSpec((pl.Squeezed(), rows, w.shape[2]), lambda i: (layer, block, 0))

    ins, specs = [state_s, state_v], [full(state_s.shape), full(state_v.shape)]
    post_names = ("w_out_s", "w_out_v", "w_up", "w_down", "w_mix", "w_gate")
    if post is not None:
        ins += [arrays["conv"], arrays["query"]]
        specs += [full(arrays["conv"].shape), full(arrays["query"].shape)]
        for name in post_names + ("gains_t",):
            ins.append(weights[name])
            specs.append(layer_spec(weights[name], post))
    if pre is not None:
        for name in ("w_qkw_s", "w_qkw_v"):
            for block in (1, 2):
                ins.append(weights[name])
                specs.append(row_spec(weights[name], pre, chans, block))
        ins.append(weights["gains_t"])
        specs.append(layer_spec(weights["gains_t"], pre))
    outs = []
    if pre is not None:
        plane_shape = (shards, 7, own, tok) if packed else (7, chans, tok)
        outs += [(plane_shape, bf16)]
        if post is not None:
            outs += [((chans, tok), f32), ((3, chans, tok), f32)]
    else:
        outs += [((chans, tok), bf16), ((3, chans, tok), bf16)]

    def snorm(x, g):
        return x * lax.rsqrt(jnp.mean(x * x, axis=0, keepdims=True) + 1e-05) * g

    def vnorm(xs, g):
        total = sum(jnp.sum(x * x, axis=0, keepdims=True) for x in xs)
        scale = lax.rsqrt(total / (3 * chans) + 1e-05)
        return [x * scale * g for x in xs]

    def mm(w, x):
        return jnp.dot(w, x, preferred_element_type=f32)

    def kernel(*refs):
        refs = list(refs)
        ss_ref, sv_ref = refs.pop(0), refs.pop(0)
        ss = ss_ref[...].astype(f32)
        sv = [sv_ref[j].astype(f32) for j in range(3)]
        if post is not None:
            conv_ref, q_ref = refs.pop(0), refs.pop(0)
            wos, wov, wup, wdn, wmx, wgt, gp = [refs.pop(0) for _ in range(7)]
            g = gp[...].T
            qs = q_ref[0].astype(f32)
            if packed:
                planes = [jnp.concatenate([conv_ref[d, p] for d in range(shards)], axis=0) for p in range(4)]
            else:
                planes = [conv_ref[p] for p in range(4)]
            ys = planes[0].astype(f32)
            yv = [planes[1 + j].astype(f32) for j in range(3)]
            mix = q_ref[1].astype(f32) * yv[0]
            mix = mix + q_ref[2].astype(f32) * yv[1]
            mix = mix + q_ref[3].astype(f32) * yv[2]
            out_s = (qs * ys + mix).astype(bf16)
            ss = ss + mm(wos[...], out_s)
            sv = [sv[j] + mm(wov[...], (qs * yv[j]).astype(bf16)) for j in range(3)]
            mlp_f = snorm(ss, g[:, 2:3])
            mlp_s = mlp_f.astype(bf16)
            mlp_v = [v.astype(bf16) for v in vnorm(sv, g[:, 3:4])]
            nt = (((1,), (1,)), ((), ()))
            mlp_t = mlp_f.T.astype(bf16)
            hidden_t = lax.dot_general(mlp_t, wup[...], nt, preferred_element_type=f32)
            hidden_t = gelu_tanh(hidden_t).astype(bf16)
            gate = 1.0 / (1.0 + jnp.exp(-mm(wgt[...], mlp_s)))
            down_t = lax.dot_general(hidden_t, wdn[...], nt, preferred_element_type=f32)
            ss = ss + down_t.T
            sv = [sv[j] + mm(wmx[...], mlp_v[j]) * gate for j in range(3)]
        if pre is not None:
            wqs_k, wqs_w, wqv_k, wqv_w, gq = [refs.pop(0) for _ in range(5)]
            g = gq[...].T
            planes_ref = refs.pop(0)

            def put(p, value):
                if packed:
                    for d in range(shards):
                        planes_ref[d, p] = value[d * own : (d + 1) * own]
                else:
                    planes_ref[p] = value

            normed_s = snorm(ss, g[:, 0:1]).astype(bf16)
            normed_v = [v.astype(bf16) for v in vnorm(sv, g[:, 1:2])]
            put(0, (mm(wqs_k[...], normed_s) * mm(wqs_w[...], normed_s)).astype(bf16))
            for j in range(3):
                put(1 + j, mm(wqv_k[...], normed_v[j]).astype(bf16))
                put(4 + j, mm(wqv_w[...], normed_v[j]).astype(bf16))
            if post is not None:
                ns_ref, nv_ref = refs.pop(0), refs.pop(0)
                ns_ref[...] = ss
                for j in range(3):
                    nv_ref[j] = sv[j]
        else:
            os_ref, ov_ref = refs.pop(0), refs.pop(0)
            os_ref[...] = ss.astype(bf16)
            for j in range(3):
                ov_ref[j] = sv[j].astype(bf16)

    return pl.pallas_call(
        kernel,
        grid=(1,),
        in_specs=specs,
        out_specs=[full(shape) for shape, _ in outs],
        out_shape=[jax.ShapeDtypeStruct(shape, dtype) for shape, dtype in outs],
    )(*ins)


def query_step(layer, state_s, state_v, weights):
    f32, bf16 = jnp.float32, jnp.bfloat16
    chans, tok = state_s.shape
    w_s, w_v, gains = weights["w_qkw_s"], weights["w_qkw_v"], weights["gains_t"]
    full = lambda shape: pl.BlockSpec(shape, lambda i, n=len(shape): (0,) * n)
    rows = lambda w: pl.BlockSpec((pl.Squeezed(), chans, w.shape[2]), lambda i: (layer, 0, 0))
    g_spec = pl.BlockSpec((pl.Squeezed(),) + gains.shape[1:], lambda i: (layer, 0, 0))

    def kernel(ss_ref, sv_ref, ws_ref, wv_ref, g_ref, q_ref):
        g = g_ref[...].T
        ss = ss_ref[...].astype(f32)
        sv = [sv_ref[j].astype(f32) for j in range(3)]
        normed_s = (ss * lax.rsqrt(jnp.mean(ss * ss, axis=0, keepdims=True) + 1e-05) * g[:, 0:1]).astype(bf16)
        total = sum(jnp.sum(x * x, axis=0, keepdims=True) for x in sv)
        scale = lax.rsqrt(total / (3 * chans) + 1e-05)
        q_ref[0] = jnp.dot(ws_ref[...], normed_s, preferred_element_type=f32).astype(bf16)
        for j in range(3):
            normed = (sv[j] * scale * g[:, 1:2]).astype(bf16)
            q_ref[1 + j] = jnp.dot(wv_ref[...], normed, preferred_element_type=f32).astype(bf16)

    return pl.pallas_call(
        kernel,
        grid=(1,),
        in_specs=[full(state_s.shape), full(state_v.shape), rows(w_s), rows(w_v), g_spec],
        out_specs=full((4, chans, tok)),
        out_shape=jax.ShapeDtypeStruct((4, chans, tok), bf16),
    )(state_s, state_v, w_s, w_v, gains)


def per_device(
    scalars,
    vectors,
    w_qkw_s,
    w_qkw_v,
    w_out_s,
    w_out_v,
    w_up,
    w_down,
    w_mix,
    w_gate,
    gains,
    pe_w1,
    pe_w2,
    pe_w3,
    rates,
):
    chans = scalars.shape[0]
    tok_local = scalars.shape[1]
    shards = lax.axis_size("seq")
    rank = lax.axis_index("seq")
    length = tok_local * shards
    own = chans // shards
    depth = w_qkw_s.shape[0]
    tables = make_tables(shards, tok_local)
    positions = jnp.arange(length, dtype=jnp.int32)

    def filter_spec(first, second, third, decay):
        third = lax.dynamic_slice_in_dim(third, rank * own, own, axis=0)
        decay = lax.dynamic_slice_in_dim(decay, rank * own, own, axis=0)
        made = filter_values(positions, length, first, second, third, decay)
        made = made.reshape(own, shards, tok_local).transpose(1, 0, 2)
        return forward_dft(made[:, None].astype(jnp.float32), tables, FAST)[:, 0]

    weights = {
        "w_qkw_s": w_qkw_s,
        "w_qkw_v": w_qkw_v,
        "w_out_s": w_out_s,
        "w_out_v": w_out_v,
        "w_up": w_up,
        "w_down": w_down,
        "w_mix": w_mix,
        "w_gate": w_gate,
        "gains_t": gains,
    }
    arrays = {"state_s": scalars, "state_v": vectors}
    packed = own % 16 == 0
    (planes,) = token_step(None, 0, arrays, weights, shards)
    tied = lax.optimization_barrier((scalars, vectors, planes))
    query = query_step(0, tied[0], tied[1], weights)
    tied = lax.optimization_barrier((pe_w1[0], pe_w2[0], pe_w3[0], rates[0], planes))
    spec_next = filter_spec(*tied[:4])
    for layer in range(depth):
        outgoing = planes
        if not packed:
            outgoing = planes.reshape(7, shards, own, tok_local).transpose(1, 0, 2, 3)
        regrouped = lax.all_to_all(outgoing, "seq", 0, 0, tiled=True)
        regrouped, query = lax.optimization_barrier((regrouped, query))
        convolved = convolve(regrouped, spec_next, tables)
        returned = lax.all_to_all(convolved, "seq", 0, 0, tiled=True)
        arrays["conv"] = returned
        if not packed:
            arrays["conv"] = returned.transpose(1, 0, 2, 3).reshape(4, chans, tok_local)
        arrays["query"] = query
        if layer + 1 < depth:
            planes, new_s, new_v = token_step(layer, layer + 1, arrays, weights, shards)
            query = query_step(layer + 1, new_s, new_v, weights)
            tied = lax.optimization_barrier(
                (pe_w1[layer + 1], pe_w2[layer + 1], pe_w3[layer + 1], rates[layer + 1], planes)
            )
            spec_next = filter_spec(*tied[:4])
            arrays["state_s"], arrays["state_v"] = new_s, new_v
        else:
            return tuple(token_step(layer, None, arrays, weights, shards))


def solution(mesh):
    in_specs = (
        P(None, ("grp", "seq")),
        P(None, None, ("grp", "seq")),
        P(),
        P(),
        P(),
        P(),
        P(),
        P(),
        P(),
        P(),
        P(),
        P(),
        P(),
        P(),
        P(),
    )
    out_specs = (P(None, ("grp", "seq")), P(None, None, ("grp", "seq")))
    return jax.shard_map(
        per_device, mesh=mesh, in_specs=in_specs, out_specs=out_specs, check_vma=False
    )
```

```python
import math

import jax
import jax.numpy as jnp
import numpy as np
from jax import lax
from jax.experimental import pallas as pl
from jax.experimental.pallas import tpu as pltpu
from jax.sharding import PartitionSpec as P

HIGH = lax.Precision.HIGHEST
FAST = lax.Precision.DEFAULT


def filter_values(positions, length, first, second, third, decay):
    count = first.shape[1] // 2
    freqs = jnp.arange(1, count + 1, dtype=jnp.int32)
    turns = freqs[:, None] * positions[None, :] % length
    angle = turns.astype(jnp.float32) * (2.0 * math.pi / length)
    feats = jnp.concatenate([jnp.cos(angle), jnp.sin(angle)], axis=0)
    hid_one = jnp.sin(jnp.dot(first, feats, precision=HIGH))
    hid_two = jnp.sin(jnp.dot(second, hid_one, precision=HIGH))
    raw = jnp.dot(third, hid_two, precision=HIGH)
    envelope = jnp.exp(-decay[:, None] * positions[None, :].astype(jnp.float32) / length)
    return (raw * envelope / math.sqrt(length)).astype(jnp.bfloat16)


def scalar_norm(field, gain):
    return field * lax.rsqrt(jnp.mean(field * field, axis=0, keepdims=True) + 1e-05) * gain[:, None]


def vector_norm(field, gain):
    return (
        field
        * lax.rsqrt(jnp.mean(field * field, axis=(0, 1), keepdims=True) + 1e-05)
        * gain[None, :, None]
    )


def make_tables(shards, local):
    length = shards * local
    f32, bf16 = jnp.float32, jnp.bfloat16

    def turns(rows, cols, period):
        rows = jnp.arange(rows, dtype=jnp.int32)[:, None]
        cols = jnp.arange(cols, dtype=jnp.int32)[None, :]
        return ((rows * cols) % period).astype(f32) * (2.0 * math.pi / period)

    half = shards // 2 + 1 if shards % 2 == 0 else shards
    ang_s = turns(half, shards, shards)
    cos_s, sin_s = jnp.cos(ang_s), jnp.sin(ang_s)
    lead_fwd = jnp.concatenate([cos_s, -sin_s], axis=0)
    if half == shards:
        weight = jnp.ones((half,), f32)
    else:
        weight = jnp.full((half,), 2.0, f32).at[0].set(1.0).at[half - 1].set(1.0)
    weight = weight / length
    lead_inv = jnp.concatenate([cos_s.T * weight, -sin_s.T * weight], axis=1)
    ang_t = turns(half, local, length)
    tw_c = jnp.cos(ang_t)[:, None, None, :]
    tw_s = jnp.sin(ang_t)[:, None, None, :]
    ang_l = turns(local, local, local)
    cos_l, sin_l = jnp.cos(ang_l), jnp.sin(ang_l)
    lane_fwd = jnp.block([[cos_l, -sin_l], [sin_l, cos_l]])
    lane_inv = jnp.block([[cos_l, sin_l], [-sin_l, cos_l]])
    return (
        lead_fwd.astype(bf16),
        lead_inv.astype(bf16),
        tw_c,
        tw_s,
        lane_fwd.astype(bf16),
        lane_inv.astype(bf16),
    )


def forward_dft(field, tables, prec):
    lead_fwd, _, tw_c, tw_s, lane_fwd, _ = tables
    shards, planes, chans, local = field.shape
    flat = field.reshape(shards, -1).astype(jnp.bfloat16)
    stage = jnp.dot(lead_fwd, flat, preferred_element_type=jnp.float32)
    half = lead_fwd.shape[0] // 2
    stage = stage.reshape(2 * half, planes, chans, local)
    st_r, st_i = stage[:half], stage[half:]
    tw_r = st_r * tw_c + st_i * tw_s
    tw_i = st_i * tw_c - st_r * tw_s
    joined = jnp.concatenate([tw_r, tw_i], axis=-1).reshape(-1, 2 * local).astype(jnp.bfloat16)
    spec = jnp.dot(joined, lane_fwd, preferred_element_type=jnp.float32)
    return spec.reshape(half, planes, chans, 2 * local)


def inverse_dft(spec, tables, prec):
    _, lead_inv, tw_c, tw_s, _, lane_inv = tables
    half, planes, chans, width = spec.shape
    shards = lead_inv.shape[0]
    local = width // 2
    flat = spec.reshape(-1, width).astype(jnp.bfloat16)
    back = jnp.dot(flat, lane_inv, preferred_element_type=jnp.float32)
    back = back.reshape(half, planes, chans, width)
    bk_r, bk_i = back[..., :local], back[..., local:]
    un_r = bk_r * tw_c - bk_i * tw_s
    un_i = bk_r * tw_s + bk_i * tw_c
    stacked = jnp.concatenate([un_r, un_i], axis=0).reshape(2 * half, -1).astype(jnp.bfloat16)
    whole = jnp.dot(lead_inv, stacked, preferred_element_type=jnp.float32)
    return whole.reshape(shards, planes, chans, local)


def cmul(a_r, a_i, b_r, b_i):
    return a_r * b_r - a_i * b_i, a_r * b_i + a_i * b_r


def convolve(received, filt_spec, tables):
    shards, _, chans, local = received.shape
    length = shards * local
    spec = forward_dft(received.astype(jnp.float32), tables, FAST)
    re, im = spec[..., :local], spec[..., local:]
    h_r, h_i = filt_spec[..., :local], filt_spec[..., local:]
    inv_root = 1.0 / math.sqrt(length)
    p_r, p_i = cmul(re[:, 0], im[:, 0], h_r, h_i)
    outs_r, outs_i = [p_r], [p_i]
    for j in range(3):
        one, two = (j + 1) % 3, (j + 2) % 3
        a_r, a_i = cmul(re[:, 1 + one], im[:, 1 + one], re[:, 4 + two], im[:, 4 + two])
        b_r, b_i = cmul(re[:, 1 + two], im[:, 1 + two], re[:, 4 + one], im[:, 4 + one])
        outs_r.append((a_r - b_r) * inv_root)
        outs_i.append((a_i - b_i) * inv_root)
    prod = jnp.concatenate([jnp.stack(outs_r, axis=1), jnp.stack(outs_i, axis=1)], axis=-1)
    return inverse_dft(prod, tables, FAST).astype(jnp.bfloat16)


def gelu_tanh(x):
    return 0.5 * x * (1.0 + jnp.tanh(math.sqrt(2.0 / math.pi) * (x + 0.044715 * (x * x * x))))


def token_step(post, pre, arrays, weights, shards):
    f32, bf16 = jnp.float32, jnp.bfloat16
    state_s, state_v = arrays["state_s"], arrays["state_v"]
    chans, tok = state_s.shape
    own = chans // shards
    packed = own % 16 == 0
    full = lambda shape: pl.BlockSpec(shape, lambda i, n=len(shape): (0,) * n)

    def layer_spec(w, layer):
        return pl.BlockSpec((pl.Squeezed(),) + w.shape[1:], lambda i: (layer,) + (0,) * (w.ndim - 1))

    def row_spec(w, layer, rows, block):
        return pl.BlockSpec((pl.Squeezed(), rows, w.shape[2]), lambda i: (layer, block, 0))

    resident = pl.BlockSpec(memory_space=pltpu.MemorySpace.VMEM)
    ins, specs = [state_s, state_v], [full(state_s.shape), full(state_v.shape)]
    post_names = ("w_out_s", "w_out_v", "w_up", "w_down", "w_mix", "w_gate")
    if post is not None:
        ins += [arrays["conv"], arrays["query"]]
        specs += [full(arrays["conv"].shape), full(arrays["query"].shape)]
        for name in post_names + ("gains_t",):
            ins.append(weights[name][post])
            specs.append(resident)
    if pre is not None:
        for name in ("w_qkw_s", "w_qkw_v"):
            for block in (1, 2):
                ins.append(weights[name][pre, block * chans : (block + 1) * chans])
                specs.append(resident)
        ins.append(weights["gains_t"][pre])
        specs.append(resident)
    outs = []
    if pre is not None:
        plane_shape = (shards, 7, own, tok) if packed else (7, chans, tok)
        outs += [(plane_shape, bf16)]
        if post is not None:
            outs += [((chans, tok), f32), ((3, chans, tok), f32)]
    else:
        outs += [((chans, tok), bf16), ((3, chans, tok), bf16)]

    def snorm(x, g):
        return x * lax.rsqrt(jnp.mean(x * x, axis=0, keepdims=True) + 1e-05) * g

    def vnorm(xs, g):
        total = sum(jnp.sum(x * x, axis=0, keepdims=True) for x in xs)
        scale = lax.rsqrt(total / (3 * chans) + 1e-05)
        return [x * scale * g for x in xs]

    def mm(w, x):
        return jnp.dot(w, x, preferred_element_type=f32)

    def kernel(*refs):
        refs = list(refs)
        ss_ref, sv_ref = refs.pop(0), refs.pop(0)
        ss = ss_ref[...].astype(f32)
        sv = [sv_ref[j].astype(f32) for j in range(3)]
        if post is not None:
            conv_ref, q_ref = refs.pop(0), refs.pop(0)
            wos, wov, wup, wdn, wmx, wgt, gp = [refs.pop(0) for _ in range(7)]
            g = gp[...].T
            qs = q_ref[0].astype(f32)
            if packed:
                planes = [jnp.concatenate([conv_ref[d, p] for d in range(shards)], axis=0) for p in range(4)]
            else:
                planes = [conv_ref[p] for p in range(4)]
            ys = planes[0].astype(f32)
            yv = [planes[1 + j].astype(f32) for j in range(3)]
            mix = q_ref[1].astype(f32) * yv[0]
            mix = mix + q_ref[2].astype(f32) * yv[1]
            mix = mix + q_ref[3].astype(f32) * yv[2]
            out_s = (qs * ys + mix).astype(bf16)
            ss = ss + mm(wos[...], out_s)
            sv = [sv[j] + mm(wov[...], (qs * yv[j]).astype(bf16)) for j in range(3)]
            mlp_s = snorm(ss, g[:, 2:3]).astype(bf16)
            mlp_v = [v.astype(bf16) for v in vnorm(sv, g[:, 3:4])]
            hidden = gelu_tanh(mm(wup[...], mlp_s)).astype(bf16)
            gate = 1.0 / (1.0 + jnp.exp(-mm(wgt[...], mlp_s)))
            ss = ss + mm(wdn[...], hidden)
            sv = [sv[j] + mm(wmx[...], mlp_v[j]) * gate for j in range(3)]
        if pre is not None:
            wqs_k, wqs_w, wqv_k, wqv_w, gq = [refs.pop(0) for _ in range(5)]
            g = gq[...].T
            planes_ref = refs.pop(0)

            def put(p, value):
                if packed:
                    for d in range(shards):
                        planes_ref[d, p] = value[d * own : (d + 1) * own]
                else:
                    planes_ref[p] = value

            normed_s = snorm(ss, g[:, 0:1]).astype(bf16)
            normed_v = [v.astype(bf16) for v in vnorm(sv, g[:, 1:2])]
            put(0, (mm(wqs_k[...], normed_s) * mm(wqs_w[...], normed_s)).astype(bf16))
            for j in range(3):
                put(1 + j, mm(wqv_k[...], normed_v[j]).astype(bf16))
                put(4 + j, mm(wqv_w[...], normed_v[j]).astype(bf16))
            if post is not None:
                ns_ref, nv_ref = refs.pop(0), refs.pop(0)
                ns_ref[...] = ss
                for j in range(3):
                    nv_ref[j] = sv[j]
        else:
            os_ref, ov_ref = refs.pop(0), refs.pop(0)
            os_ref[...] = ss.astype(bf16)
            for j in range(3):
                ov_ref[j] = sv[j].astype(bf16)

    return pl.pallas_call(
        kernel,
        grid=(1,),
        in_specs=specs,
        out_specs=[full(shape) for shape, _ in outs],
        out_shape=[jax.ShapeDtypeStruct(shape, dtype) for shape, dtype in outs],
    )(*ins)


def query_step(layer, state_s, state_v, weights):
    f32, bf16 = jnp.float32, jnp.bfloat16
    chans, tok = state_s.shape
    w_s, w_v, gains = weights["w_qkw_s"], weights["w_qkw_v"], weights["gains_t"]
    full = lambda shape: pl.BlockSpec(shape, lambda i, n=len(shape): (0,) * n)
    rows = lambda w: pl.BlockSpec((pl.Squeezed(), chans, w.shape[2]), lambda i: (layer, 0, 0))
    g_spec = pl.BlockSpec((pl.Squeezed(),) + gains.shape[1:], lambda i: (layer, 0, 0))

    def kernel(ss_ref, sv_ref, ws_ref, wv_ref, g_ref, q_ref):
        g = g_ref[...].T
        ss = ss_ref[...].astype(f32)
        sv = [sv_ref[j].astype(f32) for j in range(3)]
        normed_s = (ss * lax.rsqrt(jnp.mean(ss * ss, axis=0, keepdims=True) + 1e-05) * g[:, 0:1]).astype(bf16)
        total = sum(jnp.sum(x * x, axis=0, keepdims=True) for x in sv)
        scale = lax.rsqrt(total / (3 * chans) + 1e-05)
        q_ref[0] = jnp.dot(ws_ref[...], normed_s, preferred_element_type=f32).astype(bf16)
        for j in range(3):
            normed = (sv[j] * scale * g[:, 1:2]).astype(bf16)
            q_ref[1 + j] = jnp.dot(wv_ref[...], normed, preferred_element_type=f32).astype(bf16)

    return pl.pallas_call(
        kernel,
        grid=(1,),
        in_specs=[full(state_s.shape), full(state_v.shape), rows(w_s), rows(w_v), g_spec],
        out_specs=full((4, chans, tok)),
        out_shape=jax.ShapeDtypeStruct((4, chans, tok), bf16),
    )(state_s, state_v, w_s, w_v, gains)


def per_device(
    scalars,
    vectors,
    w_qkw_s,
    w_qkw_v,
    w_out_s,
    w_out_v,
    w_up,
    w_down,
    w_mix,
    w_gate,
    gains,
    pe_w1,
    pe_w2,
    pe_w3,
    rates,
):
    chans = scalars.shape[0]
    tok_local = scalars.shape[1]
    shards = lax.axis_size("seq")
    rank = lax.axis_index("seq")
    length = tok_local * shards
    own = chans // shards
    depth = w_qkw_s.shape[0]
    tables = make_tables(shards, tok_local)
    positions = jnp.arange(length, dtype=jnp.int32)

    def filter_spec(first, second, third, decay):
        third = lax.dynamic_slice_in_dim(third, rank * own, own, axis=0)
        decay = lax.dynamic_slice_in_dim(decay, rank * own, own, axis=0)
        made = filter_values(positions, length, first, second, third, decay)
        made = made.reshape(own, shards, tok_local).transpose(1, 0, 2)
        return forward_dft(made[:, None].astype(jnp.float32), tables, FAST)[:, 0]

    weights = {
        "w_qkw_s": w_qkw_s,
        "w_qkw_v": w_qkw_v,
        "w_out_s": w_out_s,
        "w_out_v": w_out_v,
        "w_up": w_up,
        "w_down": w_down,
        "w_mix": w_mix,
        "w_gate": w_gate,
        "gains_t": gains,
    }
    arrays = {"state_s": scalars, "state_v": vectors}
    packed = own % 16 == 0
    (planes,) = token_step(None, 0, arrays, weights, shards)
    tied = lax.optimization_barrier((scalars, vectors, planes))
    query = query_step(0, tied[0], tied[1], weights)
    tied = lax.optimization_barrier((pe_w1[0], pe_w2[0], pe_w3[0], rates[0], planes))
    spec_next = filter_spec(*tied[:4])
    for layer in range(depth):
        outgoing = planes
        if not packed:
            outgoing = planes.reshape(7, shards, own, tok_local).transpose(1, 0, 2, 3)
        regrouped = lax.all_to_all(outgoing, "seq", 0, 0, tiled=True)
        regrouped, query = lax.optimization_barrier((regrouped, query))
        convolved = convolve(regrouped, spec_next, tables)
        returned = lax.all_to_all(convolved, "seq", 0, 0, tiled=True)
        arrays["conv"] = returned
        if not packed:
            arrays["conv"] = returned.transpose(1, 0, 2, 3).reshape(4, chans, tok_local)
        arrays["query"] = query
        if layer + 1 < depth:
            planes, new_s, new_v = token_step(layer, layer + 1, arrays, weights, shards)
            query = query_step(layer + 1, new_s, new_v, weights)
            tied = lax.optimization_barrier(
                (pe_w1[layer + 1], pe_w2[layer + 1], pe_w3[layer + 1], rates[layer + 1], planes)
            )
            spec_next = filter_spec(*tied[:4])
            arrays["state_s"], arrays["state_v"] = new_s, new_v
        else:
            return tuple(token_step(layer, None, arrays, weights, shards))


def solution(mesh):
    in_specs = (
        P(None, ("grp", "seq")),
        P(None, None, ("grp", "seq")),
        P(),
        P(),
        P(),
        P(),
        P(),
        P(),
        P(),
        P(),
        P(),
        P(),
        P(),
        P(),
        P(),
    )
    out_specs = (P(None, ("grp", "seq")), P(None, None, ("grp", "seq")))
    return jax.shard_map(
        per_device, mesh=mesh, in_specs=in_specs, out_specs=out_specs, check_vma=False
    )
```
